32 devices in a mesh: dx: 8 (over y, x, core), dy: 4 (over z).
Axes of the slice: x: 2, y: 2, z: 4, core: 2. Of those that a mesh axis runs over, the one named last changes fastest.
Arguments:
- particles: float32 [8, 4, 14, 4096], P('dx', 'dy'), as said below
- leave_lists: int32 [8, 4, 4, 512], P('dx', 'dy'), may hold values from 0 to 4095, as said below
- leave_counts: int32 [8, 4, 4], P('dx', 'dy'), may hold values from 0 to 512, as said below
- slot_cells: int32 [8, 4, 6144], P('dx', 'dy'), may hold values from 0 to 32767
- velocity: float32 [3, 32, 256, 128], P(None, ('dx', 'dy')), may hold values from -4 to 4
- pressure: float32 [32, 256, 128], P(('dx', 'dy')), may hold values from -6 to 6
Outputs:
- particles_out: float32 [8, 4, 14, 6144], P('dx', 'dy')
- velocity_out: float32 [3, 32, 256, 128], P(None, ('dx', 'dy'))
- pressure_out: float32 [32, 256, 128], P(('dx', 'dy'))
The draws below stay inside these ranges and needn't reach their ends.
Inputs may be any that keep to these rules, and one draw needn't show every extreme that they name: `leave_lists`: each block's lists name 2048 distinct slots of that block. `leave_counts`: only the first count entries of a list are valid; some count equals 512 in every draw. `particles`: volumes lie in 0.2 to 1, drag coefficients in 0.2 to 2, mobilities in 0.5 to 2.
All inputs are finite; a program needn't handle non-finite values.
Results may differ from the reference program's by a relative error of at most 0.0003.
Values sent between devices are 32-bit elements; how exact they have to be, the bound alone decides.
No kernel may reach another device: no remote copies, remote signals or barrier semaphores. Data moves between devices by JAX's collectives and lax.ppermute only.
A program may use at most 320 MiB of HBM per device.

```python
import jax
import jax.numpy as jnp

CX = 32
CY = 32
P_SIZE = 4096
COUPLINGS = 2
CAP = 512
NX = 256
NY = 128
NZ = 32
N_DX = 8
N_DY = 4


def draw_particles(key, part):
    keys = jax.random.split(key, 7)
    speeds = jax.random.normal(keys[0], (N_DX, N_DY, 3, P_SIZE), jnp.float32)
    spins = jax.random.normal(keys[1], (N_DX, N_DY, 3, P_SIZE), jnp.float32)
    volumes = jax.random.uniform(keys[2], (N_DX, N_DY, 1, P_SIZE), jnp.float32, 0.2, 1.0)
    friction = jnp.exp(jax.random.uniform(keys[3], (N_DX, N_DY, 1, P_SIZE), jnp.float32, jnp.log(0.2), jnp.log(2.0)))
    mobility = jnp.exp(jax.random.uniform(keys[4], (N_DX, N_DY, 1, P_SIZE), jnp.float32, jnp.log(0.5), jnp.log(2.0)))
    places = jax.random.uniform(keys[5], (N_DX, N_DY, 3, P_SIZE), jnp.float32, 0.0, 1.0)
    extras = jax.random.normal(keys[6], (N_DX, N_DY, 2, P_SIZE), jnp.float32)
    return jnp.concatenate([speeds, spins, volumes, friction, mobility, places, extras], axis=2).astype(jnp.float32)


def draw_leave_lists(key, part):
    keys = jax.random.split(key, N_DX * N_DY)
    chosen = jax.vmap(lambda single: jax.random.permutation(single, P_SIZE)[:4 * CAP])(keys)
    return chosen.reshape(N_DX, N_DY, 4, CAP).astype(jnp.int32)


def draw_leave_counts(key, part):
    counts = jax.random.randint(key, (N_DX * N_DY * 4,), 0, CAP + 1, dtype=jnp.int32)
    picked = jax.random.randint(jax.random.fold_in(key, 7), (), 0, N_DX * N_DY * 4, dtype=jnp.int32)
    counts = counts.at[picked].set(CAP)
    return counts.reshape(N_DX, N_DY, 4).astype(jnp.int32)


def with_ends(drawn, own_key, least, high):
    spot = [jax.random.randint(jax.random.fold_in(own_key, axis), (), 0, length) for axis, length in enumerate(drawn.shape)]
    longest = drawn.shape.index(max(drawn.shape))
    neighbour = spot[:longest] + [(spot[longest] + 1) % drawn.shape[longest]] + spot[longest + 1:]
    return drawn.at[tuple(spot)].set(least).at[tuple(neighbour)].set(high)


def levels(rng, extent, cuts, low, top_value):
    def one(axis_at, shards_of):
        steps = jax.random.uniform(jax.random.fold_in(jax.random.fold_in(rng, 6), axis_at), (shards_of,), jnp.float32, low / len(cuts), top_value / len(cuts))
        return jnp.repeat(jnp.exp(steps), extent[axis_at] // shards_of).reshape((-1,) + (1,) * (len(extent) - axis_at - 1))

    loudness = one(*cuts[0])
    for cut in cuts[1:]:
        loudness = loudness * one(*cut)
    return loudness


def scatter_about(rng, extent, width, limit, cuts=(), kind=jnp.bfloat16):
    level = levels(rng, extent, cuts, -0.22, 0.18) if cuts else 1.0
    array = jax.random.normal(rng, extent, jnp.float32) * width * level
    return jnp.minimum(jnp.maximum(array, -limit), limit).astype(kind)


def setup_inputs(seed: int = 0) -> dict:
    streams_of = jax.random.split(jax.random.key(seed), 7)
    particles = draw_particles(jax.random.fold_in(streams_of[6], 71), 0)
    leave_lists = draw_leave_lists(jax.random.fold_in(streams_of[6], 71), 0)
    leave_counts = draw_leave_counts(jax.random.fold_in(streams_of[6], 71), 0)
    slot_cells = with_ends(jax.random.randint(streams_of[3], (N_DX, N_DY, P_SIZE + 4 * CAP), 0, NZ * CX * CY), jax.random.fold_in(streams_of[3], 1), 0, (NZ * CX * CY) - 1).astype(jnp.int32)
    velocity = scatter_about(streams_of[4], (3, NZ, NX, NY), 0.5, 4.0, ((1, 32),), jnp.float32)
    pressure = scatter_about(streams_of[5], (NZ, NX, NY), 1.0, 6.0, ((0, 32),), jnp.float32)
    return {"particles": particles, "leave_lists": leave_lists, "leave_counts": leave_counts, "slot_cells": slot_cells, "velocity": velocity, "pressure": pressure}


time_step = 0.1
viscosity = 0.5
gravity = -1.0


def split_block(records, leaver_lists, validity):
    holders = records.shape[1]
    flat_list = leaver_lists.reshape(-1)
    departed = jnp.zeros((holders,), jnp.float32).at[flat_list].add(validity.reshape(-1))
    remaining = records * (1.0 - departed)[None, :]
    outgoing = records[:, flat_list].reshape(records.shape[0], 4, CAP) * validity[None]
    return remaining, outgoing


def deposit_block(buffer, cell_index):
    sources = jnp.concatenate([buffer[6:8], buffer[7][None] * buffer[0:3]], axis=0)
    return jnp.zeros((5, NZ * CX * CY), jnp.float32).at[:, cell_index].add(sources)


def advance_block(buffer, cell_index, flow_block, voidage_block):
    speeds = buffer[0:3]
    friction = buffer[7]
    mobility = buffer[8]
    cell_flow = flow_block[:, cell_index]
    cell_void = voidage_block[cell_index]
    relaxation = time_step * friction * mobility / (cell_void * cell_void)
    live_mask = (buffer[6] > 0).astype(jnp.float32)
    gravity_push = jnp.zeros_like(speeds).at[2].set(time_step * gravity * live_mask)
    new_speeds = (speeds + relaxation * cell_flow + gravity_push) / (1.0 + relaxation)
    spins = buffer[3:6] / (1.0 + relaxation)
    places = buffer[9:12] + time_step * new_speeds
    return jnp.concatenate([new_speeds, spins, buffer[6:9], places, buffer[12:14]], axis=0)


def neighbour_sum(stacked):
    padded = jnp.pad(stacked, ((0, 0), (1, 1), (0, 0), (0, 0)))
    total = padded[:, 2:] + padded[:, :-2]
    total = total + jnp.roll(stacked, 1, axis=2) + jnp.roll(stacked, -1, axis=2)
    return total + jnp.roll(stacked, 1, axis=3) + jnp.roll(stacked, -1, axis=3)


def central(field):
    padded = jnp.pad(field, ((1, 1), (0, 0), (0, 0)))
    grad_x = 0.5 * (jnp.roll(field, -1, axis=1) - jnp.roll(field, 1, axis=1))
    grad_y = 0.5 * (jnp.roll(field, -1, axis=2) - jnp.roll(field, 1, axis=2))
    grad_z = 0.5 * (padded[2:] - padded[:-2])
    return grad_x, grad_y, grad_z


def fluid_step(velocity, pressure, deposits):
    solids = deposits[0]
    voidage = 1.0 / (1.0 + solids)
    growth = (1.0 + solids) * (1.0 + solids)
    drag_rate = deposits[1] * growth
    drag_pull = deposits[2:5] * growth
    stacked = jnp.concatenate([velocity, pressure[None]], axis=0)
    beside_all = neighbour_sum(stacked)
    predicted = (velocity + time_step * (viscosity * (beside_all[:3] - 6.0 * velocity) + drag_pull)) / (1.0 + time_step * drag_rate)
    flux = voidage[None] * predicted
    divergence = central(flux[0])[0] + central(flux[1])[1] + central(flux[2])[2]
    pressure_new = (beside_all[3] - divergence / time_step) / 6.0
    gradient = jnp.stack(central(pressure_new), axis=0)
    return predicted - time_step * gradient, pressure_new


def reference(particles, leave_lists, leave_counts, slot_cells, velocity, pressure):
    blocks_x, blocks_y = N_DX, N_DY
    positions = jnp.arange(CAP, dtype=jnp.int32)
    validity = (positions[None, None, None, :] < leave_counts[..., None]).astype(jnp.float32)
    remaining, outgoing = jax.vmap(jax.vmap(split_block))(particles, leave_lists, validity)
    from_left = jnp.roll(outgoing[:, :, :, 0], 1, axis=0)
    from_right = jnp.roll(outgoing[:, :, :, 1], -1, axis=0)
    from_below = jnp.roll(outgoing[:, :, :, 2], 1, axis=1)
    from_above = jnp.roll(outgoing[:, :, :, 3], -1, axis=1)
    buffer = jnp.concatenate([remaining, from_left, from_right, from_below, from_above], axis=3)
    for coupling in range(COUPLINGS):
        deposits = jax.vmap(jax.vmap(deposit_block))(buffer, slot_cells)
        voidage_blocks = 1.0 / (1.0 + deposits[:, :, 0])
        global_sources = deposits.reshape(blocks_x, blocks_y, 5, NZ, CX, CY).transpose(2, 3, 0, 4, 1, 5).reshape(5, NZ, NX, NY)
        velocity, pressure = fluid_step(velocity, pressure, global_sources)
        flow_blocks = velocity.reshape(3, NZ, blocks_x, CX, blocks_y, CY).transpose(2, 4, 0, 1, 3, 5).reshape(blocks_x, blocks_y, 3, NZ * CX * CY)
        buffer = jax.vmap(jax.vmap(advance_block))(buffer, slot_cells, flow_blocks, voidage_blocks)
    return buffer, velocity, pressure
```

```python
import jax
import jax.numpy as jnp
from jax import lax
from jax.sharding import PartitionSpec as P

COUPLINGS = 2


time_step = 0.1
viscosity = 0.5
gravity = -1.0


def from_behind(value, axis, steps):
    count = lax.axis_size(axis)
    pairs = [(source, (source + steps) % count) for source in range(count)]
    return lax.ppermute(value, axis, pairs)


def migrate(outgoing):
    arrivals = []
    for offset in (1, -1):
        arrivals.append(from_behind(outgoing[:, (1 - offset) // 2], "dx", offset))
    for offset in (1, -1):
        arrivals.append(from_behind(outgoing[:, 2 + (1 - offset) // 2], "dy", offset))
    return arrivals


def split_bf16(values):
    high = lax.reduce_precision(values, exponent_bits=8, mantissa_bits=7)
    low = values - high
    return high.astype(jnp.bfloat16), low.astype(jnp.bfloat16)


def deposit_block(buffer, on_layer, on_lane):
    sources = jnp.concatenate([buffer[6:8], buffer[7][None] * buffer[0:3]], axis=0)
    layered = sources[:, None, :] * on_layer[None]
    high, low = split_bf16(layered)
    channels, layers, slots = layered.shape
    stacked = jnp.concatenate([high, low], axis=0).reshape(2 * channels * layers, slots)
    summed = jnp.dot(stacked, on_lane, preferred_element_type=jnp.float32)
    summed = summed.reshape(2, channels, layers, on_lane.shape[1])
    return summed[0] + summed[1]


def gather_block(fields, on_layer, on_lane):
    channels, layers, lanes = fields.shape
    high, low = split_bf16(fields)
    stacked = jnp.concatenate([high, low], axis=0).reshape(2 * channels * layers, lanes)
    picked = lax.dot_general(
        stacked, on_lane, (((1,), (1,)), ((), ())), preferred_element_type=jnp.float32
    )
    picked = picked.reshape(2, channels, layers, on_lane.shape[0])
    return jnp.sum((picked[0] + picked[1]) * on_layer[None], axis=1)


def advance_block(buffer, cell_flow, cell_solids):
    speeds = buffer[0:3]
    friction = buffer[7]
    mobility = buffer[8]
    cell_void = 1.0 / (1.0 + cell_solids)
    relaxation = time_step * friction * mobility / (cell_void * cell_void)
    live_mask = (buffer[6] > 0).astype(jnp.float32)
    gravity_push = jnp.zeros_like(speeds).at[2].set(time_step * gravity * live_mask)
    new_speeds = (speeds + relaxation * cell_flow + gravity_push) / (1.0 + relaxation)
    spins = buffer[3:6] / (1.0 + relaxation)
    places = buffer[9:12] + time_step * new_speeds
    return jnp.concatenate([new_speeds, spins, buffer[6:9], places, buffer[12:14]], axis=0)


def slabs_to_blocks(field, blocks_x, blocks_y):
    channels, layers_z, cells_nx, cells_ny = field.shape
    cells_x, cells_y = cells_nx // blocks_x, cells_ny // blocks_y
    arranged = field.reshape(channels, layers_z, blocks_x, cells_x, blocks_y, cells_y).transpose(
        0, 2, 4, 1, 3, 5
    )
    arranged = arranged.reshape(channels, blocks_x * blocks_y * layers_z, cells_x * cells_y)
    return lax.all_to_all(arranged, ("dx", "dy"), split_axis=1, concat_axis=1, tiled=True)


def blocks_to_slabs(field, blocks_x, blocks_y, cells_x, cells_y):
    channels, depth, lanes = field.shape
    layers_z = depth // (blocks_x * blocks_y)
    moved = lax.all_to_all(field, ("dx", "dy"), split_axis=1, concat_axis=1, tiled=True)
    arranged = moved.reshape(channels, blocks_x, blocks_y, layers_z, cells_x, cells_y).transpose(
        0, 3, 1, 4, 2, 5
    )
    return arranged.reshape(channels, layers_z, blocks_x * cells_x, blocks_y * cells_y)


def along_z(field):
    zero = jnp.zeros_like(field[..., :1, :])
    above = jnp.concatenate([field[..., 1:, :], zero], axis=-2)
    below = jnp.concatenate([zero, field[..., :-1, :]], axis=-2)
    return above, below


def along_x(field, cells_y):
    ahead = from_behind(field[..., :cells_y], "dx", -1)
    behind = from_behind(field[..., field.shape[-1] - cells_y :], "dx", 1)
    plus = jnp.concatenate([field[..., cells_y:], ahead], axis=-1)
    minus = jnp.concatenate([behind, field[..., :-cells_y]], axis=-1)
    return plus, minus


def along_y(field, cells_x, cells_y):
    shape = field.shape
    grid = field.reshape(shape[:-1] + (cells_x, cells_y))
    ahead = from_behind(grid[..., 0], "dy", -1)
    behind = from_behind(grid[..., cells_y - 1], "dy", 1)
    lane_y = lax.broadcasted_iota(jnp.int32, shape, len(shape) - 1) % cells_y
    spread_ahead = jnp.broadcast_to(ahead[..., None], grid.shape).reshape(shape)
    spread_behind = jnp.broadcast_to(behind[..., None], grid.shape).reshape(shape)
    plus = jnp.where(lane_y == cells_y - 1, spread_ahead, jnp.roll(field, -1, axis=-1))
    minus = jnp.where(lane_y == 0, spread_behind, jnp.roll(field, 1, axis=-1))
    return plus, minus


def fluid_step(velocity, pressure, deposits, cells_x, cells_y):
    solids = deposits[0]
    voidage = 1.0 / (1.0 + solids)
    growth = (1.0 + solids) * (1.0 + solids)
    drag_rate = deposits[1] * growth
    drag_pull = deposits[2:5] * growth
    stacked = jnp.concatenate([velocity, pressure[None]], axis=0)
    z_plus, z_minus = along_z(stacked)
    x_plus, x_minus = along_x(stacked, cells_y)
    y_plus, y_minus = along_y(stacked, cells_x, cells_y)
    beside_all = (z_plus + z_minus) + x_plus + x_minus + y_plus + y_minus
    predicted = (
        velocity + time_step * (viscosity * (beside_all[:3] - 6.0 * velocity) + drag_pull)
    ) / (1.0 + time_step * drag_rate)
    flux = voidage[None] * predicted
    fx_plus, fx_minus = along_x(flux[0], cells_y)
    fy_plus, fy_minus = along_y(flux[1], cells_x, cells_y)
    fz_plus, fz_minus = along_z(flux[2])
    divergence = 0.5 * (fx_plus - fx_minus) + 0.5 * (fy_plus - fy_minus) + 0.5 * (fz_plus - fz_minus)
    pressure_new = (beside_all[3] - divergence / time_step) / 6.0
    px_plus, px_minus = along_x(pressure_new, cells_y)
    py_plus, py_minus = along_y(pressure_new, cells_x, cells_y)
    pz_plus, pz_minus = along_z(pressure_new)
    gradient = jnp.stack(
        [0.5 * (px_plus - px_minus), 0.5 * (py_plus - py_minus), 0.5 * (pz_plus - pz_minus)], axis=0
    )
    return (predicted - time_step * gradient, pressure_new)


def shards(particles, leave_lists, leave_counts, slot_cells, velocity, pressure):
    blocks_x = lax.axis_size("dx")
    blocks_y = lax.axis_size("dy")
    records = particles[0, 0]
    leaver_lists = leave_lists[0, 0]
    leaver_counts = leave_counts[0, 0]
    cell_index = slot_cells[0, 0]
    capacity = leaver_lists.shape[1]
    holders = records.shape[1]
    cells_x = velocity.shape[2] // blocks_x
    cells_y = velocity.shape[3] // blocks_y
    lanes = cells_x * cells_y
    depth = velocity.shape[1] * blocks_x * blocks_y

    fields = slabs_to_blocks(
        jnp.concatenate([velocity, pressure[None]], axis=0), blocks_x, blocks_y
    )
    flow = fields[:3]
    pressure_block = fields[3]

    positions = jnp.arange(capacity, dtype=jnp.int32)
    validity = (positions[None, :] < leaver_counts[:, None]).astype(jnp.float32)
    flat_list = leaver_lists.reshape(-1)
    departed = jnp.zeros((holders,), jnp.float32).at[flat_list].add(validity.reshape(-1))
    remaining = records * (1.0 - departed)[None, :]
    outgoing = records[:, flat_list].reshape(records.shape[0], 4, capacity) * validity[None]
    arrivals = migrate(outgoing)
    buffer = jnp.concatenate([remaining] + arrivals, axis=1)

    layer_of = cell_index // lanes
    lane_of = cell_index % lanes
    on_layer = (
        lax.broadcasted_iota(jnp.int32, (depth, cell_index.shape[0]), 0) == layer_of[None, :]
    ).astype(jnp.float32)
    on_lane = (
        lax.broadcasted_iota(jnp.int32, (cell_index.shape[0], lanes), 1) == lane_of[:, None]
    ).astype(jnp.bfloat16)

    for coupling in range(COUPLINGS):
        deposits = deposit_block(buffer, on_layer, on_lane)
        flow, pressure_block = fluid_step(flow, pressure_block, deposits, cells_x, cells_y)
        picked = gather_block(
            jnp.concatenate([flow, deposits[:1]], axis=0), on_layer, on_lane
        )
        buffer = advance_block(buffer, picked[:3], picked[3])

    fields = blocks_to_slabs(
        jnp.concatenate([flow, pressure_block[None]], axis=0), blocks_x, blocks_y, cells_x, cells_y
    )
    return (buffer[None, None], fields[:3], fields[3])


def solution(mesh):
    placed = (
        P("dx", "dy", None, None),
        P("dx", "dy", None, None),
        P("dx", "dy", None),
        P("dx", "dy", None),
        P(None, ("dx", "dy"), None, None),
        P(("dx", "dy"), None, None),
    )
    return jax.shard_map(
        shards,
        mesh=mesh,
        in_specs=placed,
        out_specs=(
            P("dx", "dy", None, None),
            P(None, ("dx", "dy"), None, None),
            P(("dx", "dy"), None, None),
        ),
        check_vma=False,
    )
```

```python
import jax
import jax.numpy as jnp
from jax import lax
from jax.sharding import PartitionSpec as P

COUPLINGS = 2


time_step = 0.1
viscosity = 0.5
gravity = -1.0


def from_behind(value, axis, steps):
    count = lax.axis_size(axis)
    pairs = [(source, (source + steps) % count) for source in range(count)]
    return lax.ppermute(value, axis, pairs)


def migrate(outgoing):
    arrivals = []
    for offset in (1, -1):
        arrivals.append(from_behind(outgoing[:, (1 - offset) // 2], "dx", offset))
    for offset in (1, -1):
        arrivals.append(from_behind(outgoing[:, 2 + (1 - offset) // 2], "dy", offset))
    return arrivals


def split_bf16(values):
    high = lax.reduce_precision(values, exponent_bits=8, mantissa_bits=7)
    low = values - high
    return high.astype(jnp.bfloat16), low.astype(jnp.bfloat16)


def deposit_block(buffer, on_layer, on_lane):
    sources = jnp.concatenate([buffer[6:8], buffer[7][None] * buffer[0:3]], axis=0)
    layered = sources[:, None, :] * on_layer[None]
    high, low = split_bf16(layered)
    channels, layers, slots = layered.shape
    stacked = jnp.concatenate([high, low], axis=0).reshape(2 * channels * layers, slots)
    summed = jnp.dot(stacked, on_lane, preferred_element_type=jnp.float32)
    summed = summed.reshape(2, channels, layers, on_lane.shape[1])
    return summed[0] + summed[1]


def gather_block(fields, on_layer, on_lane):
    channels, layers, lanes = fields.shape
    high, low = split_bf16(fields)
    stacked = jnp.concatenate([high, low], axis=0).reshape(2 * channels * layers, lanes)
    picked = lax.dot_general(
        stacked, on_lane, (((1,), (1,)), ((), ())), preferred_element_type=jnp.float32
    )
    picked = picked.reshape(2, channels, layers, on_lane.shape[0])
    return jnp.sum((picked[0] + picked[1]) * on_layer[None], axis=1)


def advance_block(buffer, cell_flow, cell_solids):
    speeds = buffer[0:3]
    friction = buffer[7]
    mobility = buffer[8]
    cell_void = 1.0 / (1.0 + cell_solids)
    relaxation = time_step * friction * mobility / (cell_void * cell_void)
    live_mask = (buffer[6] > 0).astype(jnp.float32)
    gravity_push = jnp.zeros_like(speeds).at[2].set(time_step * gravity * live_mask)
    new_speeds = (speeds + relaxation * cell_flow + gravity_push) / (1.0 + relaxation)
    spins = buffer[3:6] / (1.0 + relaxation)
    places = buffer[9:12] + time_step * new_speeds
    return jnp.concatenate([new_speeds, spins, buffer[6:9], places, buffer[12:14]], axis=0)


def slabs_to_blocks(field, blocks_x, blocks_y):
    channels, layers_z, cells_nx, cells_ny = field.shape
    cells_x, cells_y = cells_nx // blocks_x, cells_ny // blocks_y
    arranged = field.reshape(channels, layers_z, blocks_x, cells_x, blocks_y, cells_y).transpose(
        0, 2, 4, 1, 3, 5
    )
    arranged = arranged.reshape(channels, blocks_x * blocks_y * layers_z, cells_x * cells_y)
    return lax.all_to_all(arranged, ("dx", "dy"), split_axis=1, concat_axis=1, tiled=True)


def blocks_to_slabs(field, blocks_x, blocks_y, cells_x, cells_y):
    channels, depth, lanes = field.shape
    layers_z = depth // (blocks_x * blocks_y)
    moved = lax.all_to_all(field, ("dx", "dy"), split_axis=1, concat_axis=1, tiled=True)
    arranged = moved.reshape(channels, blocks_x, blocks_y, layers_z, cells_x, cells_y).transpose(
        0, 3, 1, 4, 2, 5
    )
    return arranged.reshape(channels, layers_z, blocks_x * cells_x, blocks_y * cells_y)


def shift_blocks(value, step_x, step_y):
    count_x = lax.axis_size("dx")
    count_y = lax.axis_size("dy")
    pairs = [
        (i * count_y + j, ((i + step_x) % count_x) * count_y + (j + step_y) % count_y)
        for i in range(count_x)
        for j in range(count_y)
    ]
    return lax.ppermute(value, ("dx", "dy"), pairs)


def extend(fields, cells_x, cells_y, width):
    channels, layers, _ = fields.shape
    grid = fields.reshape(channels, layers, cells_x, cells_y)
    low_x, high_x = grid[:, :, :width], grid[:, :, cells_x - width :]
    from_xp = shift_blocks(low_x, -1, 0)
    from_xm = shift_blocks(high_x, 1, 0)
    from_yp = shift_blocks(grid[..., :width], 0, -1)
    from_ym = shift_blocks(grid[..., cells_y - width :], 0, 1)
    from_xp_yp = shift_blocks(low_x[..., :width], -1, -1)
    from_xp_ym = shift_blocks(low_x[..., cells_y - width :], -1, 1)
    from_xm_yp = shift_blocks(high_x[..., :width], 1, -1)
    from_xm_ym = shift_blocks(high_x[..., cells_y - width :], 1, 1)
    top = jnp.concatenate([from_xm_ym, from_xm, from_xm_yp], axis=-1)
    middle = jnp.concatenate([from_ym, grid, from_yp], axis=-1)
    bottom = jnp.concatenate([from_xp_ym, from_xp, from_xp_yp], axis=-1)
    wide = jnp.concatenate([top, middle, bottom], axis=-2)
    return wide.reshape(channels, layers, (cells_x + 2 * width) * (cells_y + 2 * width))


def interior(wide, cells_x, cells_y, width):
    leading = wide.shape[:-1]
    grid = wide.reshape(leading + (cells_x + 2 * width, cells_y + 2 * width))
    inner = grid[..., width : width + cells_x, width : width + cells_y]
    return inner.reshape(leading + (cells_x * cells_y,))


def along_z(field):
    zero = jnp.zeros_like(field[..., :1, :])
    above = jnp.concatenate([field[..., 1:, :], zero], axis=-2)
    below = jnp.concatenate([zero, field[..., :-1, :]], axis=-2)
    return above, below


def along_lanes(field, stride):
    return jnp.roll(field, -stride, axis=-1), jnp.roll(field, stride, axis=-1)


def fluid_step(wide_flow, wide_pressure, wide_deposits, row):
    solids = wide_deposits[0]
    voidage = 1.0 / (1.0 + solids)
    growth = (1.0 + solids) * (1.0 + solids)
    drag_rate = wide_deposits[1] * growth
    drag_pull = wide_deposits[2:5] * growth
    stacked = jnp.concatenate([wide_flow, wide_pressure[None]], axis=0)
    z_plus, z_minus = along_z(stacked)
    x_plus, x_minus = along_lanes(stacked, row)
    y_plus, y_minus = along_lanes(stacked, 1)
    beside_all = (z_plus + z_minus) + x_minus + x_plus + y_minus + y_plus
    predicted = (
        wide_flow + time_step * (viscosity * (beside_all[:3] - 6.0 * wide_flow) + drag_pull)
    ) / (1.0 + time_step * drag_rate)
    flux = voidage[None] * predicted
    fx_plus, fx_minus = along_lanes(flux[0], row)
    fy_plus, fy_minus = along_lanes(flux[1], 1)
    fz_plus, fz_minus = along_z(flux[2])
    divergence = 0.5 * (fx_plus - fx_minus) + 0.5 * (fy_plus - fy_minus) + 0.5 * (fz_plus - fz_minus)
    pressure_new = (beside_all[3] - divergence / time_step) / 6.0
    px_plus, px_minus = along_lanes(pressure_new, row)
    py_plus, py_minus = along_lanes(pressure_new, 1)
    pz_plus, pz_minus = along_z(pressure_new)
    gradient = jnp.stack(
        [0.5 * (px_plus - px_minus), 0.5 * (py_plus - py_minus), 0.5 * (pz_plus - pz_minus)], axis=0
    )
    return (predicted - time_step * gradient, pressure_new)


def shards(particles, leave_lists, leave_counts, slot_cells, velocity, pressure):
    blocks_x = lax.axis_size("dx")
    blocks_y = lax.axis_size("dy")
    records = particles[0, 0]
    leaver_lists = leave_lists[0, 0]
    leaver_counts = leave_counts[0, 0]
    cell_index = slot_cells[0, 0]
    capacity = leaver_lists.shape[1]
    holders = records.shape[1]
    cells_x = velocity.shape[2] // blocks_x
    cells_y = velocity.shape[3] // blocks_y
    lanes = cells_x * cells_y
    depth = velocity.shape[1] * blocks_x * blocks_y

    fields = slabs_to_blocks(
        jnp.concatenate([velocity, pressure[None]], axis=0), blocks_x, blocks_y
    )
    flow = fields[:3]
    pressure_block = fields[3]

    positions = jnp.arange(capacity, dtype=jnp.int32)
    validity = (positions[None, :] < leaver_counts[:, None]).astype(jnp.float32)
    flat_list = leaver_lists.reshape(-1)
    named = (flat_list[None, :] == lax.broadcasted_iota(jnp.int32, (holders, flat_list.shape[0]), 0)) & (
        validity.reshape(1, -1) > 0
    )
    departed = jnp.any(named, axis=1).astype(jnp.float32)
    remaining = records * (1.0 - departed)[None, :]
    outgoing = records[:, flat_list].reshape(records.shape[0], 4, capacity) * validity[None]
    arrivals = migrate(outgoing)
    buffer = jnp.concatenate([remaining] + arrivals, axis=1)

    layer_of = cell_index // lanes
    lane_of = cell_index % lanes
    on_layer = (
        lax.broadcasted_iota(jnp.int32, (depth, cell_index.shape[0]), 0) == layer_of[None, :]
    ).astype(jnp.float32)
    on_lane = (
        lax.broadcasted_iota(jnp.int32, (cell_index.shape[0], lanes), 1) == lane_of[:, None]
    ).astype(jnp.bfloat16)

    width = 3
    for coupling in range(COUPLINGS):
        deposits = deposit_block(buffer, on_layer, on_lane)
        wide = extend(
            jnp.concatenate([flow, pressure_block[None], deposits], axis=0), cells_x, cells_y, width
        )
        wide_flow, wide_pressure = fluid_step(wide[:3], wide[3], wide[4:], cells_y + 2 * width)
        flow = interior(wide_flow, cells_x, cells_y, width)
        pressure_block = interior(wide_pressure, cells_x, cells_y, width)
        picked = gather_block(
            jnp.concatenate([flow, deposits[:1]], axis=0), on_layer, on_lane
        )
        buffer = advance_block(buffer, picked[:3], picked[3])

    fields = blocks_to_slabs(
        jnp.concatenate([flow, pressure_block[None]], axis=0), blocks_x, blocks_y, cells_x, cells_y
    )
    return (buffer[None, None], fields[:3], fields[3])


def solution(mesh):
    placed = (
        P("dx", "dy", None, None),
        P("dx", "dy", None, None),
        P("dx", "dy", None),
        P("dx", "dy", None),
        P(None, ("dx", "dy"), None, None),
        P(("dx", "dy"), None, None),
    )
    return jax.shard_map(
        shards,
        mesh=mesh,
        in_specs=placed,
        out_specs=(
            P("dx", "dy", None, None),
            P(None, ("dx", "dy"), None, None),
            P(("dx", "dy"), None, None),
        ),
        check_vma=False,
    )
```

```python
import jax
import jax.numpy as jnp
from jax import lax
from jax.sharding import PartitionSpec as P

COUPLINGS = 2


time_step = 0.1
viscosity = 0.5
gravity = -1.0


def from_behind(value, axis, steps):
    count = lax.axis_size(axis)
    pairs = [(source, (source + steps) % count) for source in range(count)]
    return lax.ppermute(value, axis, pairs)


def migrate(outgoing):
    arrivals = []
    for offset in (1, -1):
        arrivals.append(from_behind(outgoing[:, (1 - offset) // 2], "dx", offset))
    for offset in (1, -1):
        arrivals.append(from_behind(outgoing[:, 2 + (1 - offset) // 2], "dy", offset))
    return arrivals


def split_bf16(values):
    high = lax.reduce_precision(values, exponent_bits=8, mantissa_bits=7)
    low = values - high
    return high.astype(jnp.bfloat16), low.astype(jnp.bfloat16)


def deposit_block(buffer, on_layer, on_lane):
    sources = jnp.concatenate([buffer[6:8], buffer[7][None] * buffer[0:3]], axis=0)
    layered = sources[:, None, :] * on_layer[None]
    high, low = split_bf16(layered)
    channels, layers, slots = layered.shape
    stacked = jnp.concatenate([high, low], axis=0).reshape(2 * channels * layers, slots)
    summed = jnp.dot(stacked, on_lane, preferred_element_type=jnp.float32)
    summed = summed.reshape(2, channels, layers, on_lane.shape[1])
    return summed[0] + summed[1]


def gather_block(fields, on_layer, on_lane):
    channels, layers, lanes = fields.shape
    high, low = split_bf16(fields)
    stacked = jnp.concatenate([high, low], axis=0).reshape(2 * channels * layers, lanes)
    picked = lax.dot_general(
        stacked, on_lane, (((1,), (1,)), ((), ())), preferred_element_type=jnp.float32
    )
    picked = picked.reshape(2, channels, layers, on_lane.shape[0])
    return jnp.sum((picked[0] + picked[1]) * on_layer[None], axis=1)


def advance_block(buffer, cell_flow, cell_solids):
    speeds = buffer[0:3]
    friction = buffer[7]
    mobility = buffer[8]
    cell_void = 1.0 / (1.0 + cell_solids)
    relaxation = time_step * friction * mobility / (cell_void * cell_void)
    live_mask = (buffer[6] > 0).astype(jnp.float32)
    gravity_push = jnp.zeros_like(speeds).at[2].set(time_step * gravity * live_mask)
    new_speeds = (speeds + relaxation * cell_flow + gravity_push) / (1.0 + relaxation)
    spins = buffer[3:6] / (1.0 + relaxation)
    places = buffer[9:12] + time_step * new_speeds
    return jnp.concatenate([new_speeds, spins, buffer[6:9], places, buffer[12:14]], axis=0)


def slabs_to_blocks(field, blocks_x, blocks_y):
    channels, layers_z, cells_nx, cells_ny = field.shape
    cells_x, cells_y = cells_nx // blocks_x, cells_ny // blocks_y
    arranged = field.reshape(channels, layers_z, blocks_x, cells_x, blocks_y, cells_y).transpose(
        0, 2, 4, 1, 3, 5
    )
    arranged = arranged.reshape(channels, blocks_x * blocks_y * layers_z, cells_x * cells_y)
    return lax.all_to_all(arranged, ("dx", "dy"), split_axis=1, concat_axis=1, tiled=True)


def blocks_to_slabs(field, blocks_x, blocks_y, cells_x, cells_y):
    channels, depth, lanes = field.shape
    layers_z = depth // (blocks_x * blocks_y)
    moved = lax.all_to_all(field, ("dx", "dy"), split_axis=1, concat_axis=1, tiled=True)
    arranged = moved.reshape(channels, blocks_x, blocks_y, layers_z, cells_x, cells_y).transpose(
        0, 3, 1, 4, 2, 5
    )
    return arranged.reshape(channels, layers_z, blocks_x * cells_x, blocks_y * cells_y)


def along_z(field):
    zero = jnp.zeros_like(field[..., :1, :])
    above = jnp.concatenate([field[..., 1:, :], zero], axis=-2)
    below = jnp.concatenate([zero, field[..., :-1, :]], axis=-2)
    return above, below


def along_x(field, cells_y):
    ahead = from_behind(field[..., :cells_y], "dx", -1)
    behind = from_behind(field[..., field.shape[-1] - cells_y :], "dx", 1)
    plus = jnp.concatenate([field[..., cells_y:], ahead], axis=-1)
    minus = jnp.concatenate([behind, field[..., :-cells_y]], axis=-1)
    return plus, minus


def along_y(field, cells_x, cells_y):
    shape = field.shape
    grid = field.reshape(shape[:-1] + (cells_x, cells_y))
    ahead = from_behind(grid[..., 0], "dy", -1)
    behind = from_behind(grid[..., cells_y - 1], "dy", 1)
    lane_y = lax.broadcasted_iota(jnp.int32, shape, len(shape) - 1) % cells_y
    spreader = (
        lax.broadcasted_iota(jnp.int32, (cells_x, cells_x * cells_y), 1) // cells_y
        == lax.broadcasted_iota(jnp.int32, (cells_x, cells_x * cells_y), 0)
    ).astype(jnp.float32)
    spread_ahead = jnp.dot(ahead, spreader, precision=lax.Precision.HIGHEST)
    spread_behind = jnp.dot(behind, spreader, precision=lax.Precision.HIGHEST)
    plus = jnp.where(lane_y == cells_y - 1, spread_ahead, jnp.roll(field, -1, axis=-1))
    minus = jnp.where(lane_y == 0, spread_behind, jnp.roll(field, 1, axis=-1))
    return plus, minus


def fluid_step(velocity, pressure, deposits, cells_x, cells_y):
    solids = deposits[0]
    voidage = 1.0 / (1.0 + solids)
    growth = (1.0 + solids) * (1.0 + solids)
    drag_rate = deposits[1] * growth
    drag_pull = deposits[2:5] * growth
    stacked = jnp.concatenate([velocity, pressure[None]], axis=0)
    z_plus, z_minus = along_z(stacked)
    x_plus, x_minus = along_x(stacked, cells_y)
    y_plus, y_minus = along_y(stacked, cells_x, cells_y)
    beside_all = (z_plus + z_minus) + x_plus + x_minus + y_plus + y_minus
    predicted = (
        velocity + time_step * (viscosity * (beside_all[:3] - 6.0 * velocity) + drag_pull)
    ) / (1.0 + time_step * drag_rate)
    flux = voidage[None] * predicted
    fx_plus, fx_minus = along_x(flux[0], cells_y)
    fy_plus, fy_minus = along_y(flux[1], cells_x, cells_y)
    fz_plus, fz_minus = along_z(flux[2])
    divergence = 0.5 * (fx_plus - fx_minus) + 0.5 * (fy_plus - fy_minus) + 0.5 * (fz_plus - fz_minus)
    pressure_new = (beside_all[3] - divergence / time_step) / 6.0
    px_plus, px_minus = along_x(pressure_new, cells_y)
    py_plus, py_minus = along_y(pressure_new, cells_x, cells_y)
    pz_plus, pz_minus = along_z(pressure_new)
    gradient = jnp.stack(
        [0.5 * (px_plus - px_minus), 0.5 * (py_plus - py_minus), 0.5 * (pz_plus - pz_minus)], axis=0
    )
    return (predicted - time_step * gradient, pressure_new)


def shards(particles, leave_lists, leave_counts, slot_cells, velocity, pressure):
    blocks_x = lax.axis_size("dx")
    blocks_y = lax.axis_size("dy")
    records = particles[0, 0]
    leaver_lists = leave_lists[0, 0]
    leaver_counts = leave_counts[0, 0]
    cell_index = slot_cells[0, 0]
    capacity = leaver_lists.shape[1]
    holders = records.shape[1]
    cells_x = velocity.shape[2] // blocks_x
    cells_y = velocity.shape[3] // blocks_y
    lanes = cells_x * cells_y
    depth = velocity.shape[1] * blocks_x * blocks_y

    fields = slabs_to_blocks(
        jnp.concatenate([velocity, pressure[None]], axis=0), blocks_x, blocks_y
    )
    flow = fields[:3]
    pressure_block = fields[3]

    positions = jnp.arange(capacity, dtype=jnp.int32)
    validity = (positions[None, :] < leaver_counts[:, None]).astype(jnp.float32)
    flat_list = leaver_lists.reshape(-1)
    named = (flat_list[None, :] == lax.broadcasted_iota(jnp.int32, (holders, flat_list.shape[0]), 0)) & (
        validity.reshape(1, -1) > 0
    )
    departed = jnp.any(named, axis=1).astype(jnp.float32)
    remaining = records * (1.0 - departed)[None, :]
    outgoing = records[:, flat_list].reshape(records.shape[0], 4, capacity) * validity[None]
    arrivals = migrate(outgoing)
    buffer = jnp.concatenate([remaining] + arrivals, axis=1)

    layer_of = cell_index // lanes
    lane_of = cell_index % lanes
    on_layer = (
        lax.broadcasted_iota(jnp.int32, (depth, cell_index.shape[0]), 0) == layer_of[None, :]
    ).astype(jnp.float32)
    on_lane = (
        lax.broadcasted_iota(jnp.int32, (cell_index.shape[0], lanes), 1) == lane_of[:, None]
    ).astype(jnp.bfloat16)

    for coupling in range(COUPLINGS):
        deposits = deposit_block(buffer, on_layer, on_lane)
        flow, pressure_block = fluid_step(flow, pressure_block, deposits, cells_x, cells_y)
        picked = gather_block(
            jnp.concatenate([flow, deposits[:1]], axis=0), on_layer, on_lane
        )
        buffer = advance_block(buffer, picked[:3], picked[3])

    fields = blocks_to_slabs(
        jnp.concatenate([flow, pressure_block[None]], axis=0), blocks_x, blocks_y, cells_x, cells_y
    )
    return (buffer[None, None], fields[:3], fields[3])


def solution(mesh):
    placed = (
        P("dx", "dy", None, None),
        P("dx", "dy", None, None),
        P("dx", "dy", None),
        P("dx", "dy", None),
        P(None, ("dx", "dy"), None, None),
        P(("dx", "dy"), None, None),
    )
    return jax.shard_map(
        shards,
        mesh=mesh,
        in_specs=placed,
        out_specs=(
            P("dx", "dy", None, None),
            P(None, ("dx", "dy"), None, None),
            P(("dx", "dy"), None, None),
        ),
        check_vma=False,
    )
```

```python
import jax
import jax.numpy as jnp
from jax import lax
from jax.sharding import PartitionSpec as P

COUPLINGS = 2


time_step = 0.1
viscosity = 0.5
gravity = -1.0


def from_behind(value, axis, steps):
    count = lax.axis_size(axis)
    pairs = [(source, (source + steps) % count) for source in range(count)]
    return lax.ppermute(value, axis, pairs)


def migrate(outgoing):
    arrivals = []
    for offset in (1, -1):
        arrivals.append(from_behind(outgoing[:, (1 - offset) // 2], "dx", offset))
    for offset in (1, -1):
        arrivals.append(from_behind(outgoing[:, 2 + (1 - offset) // 2], "dy", offset))
    return arrivals


def split_bf16(values):
    high = lax.reduce_precision(values, exponent_bits=8, mantissa_bits=7)
    low = values - high
    return high.astype(jnp.bfloat16), low.astype(jnp.bfloat16)


def deposit_block(buffer, on_layer, on_lane):
    sources = jnp.concatenate([buffer[6:8], buffer[7][None] * buffer[0:3]], axis=0)
    layered = sources[:, None, :] * on_layer[None]
    high, low = split_bf16(layered)
    channels, layers, slots = layered.shape
    stacked = jnp.concatenate([high, low], axis=0).reshape(2 * channels * layers, slots)
    summed = jnp.dot(stacked, on_lane, preferred_element_type=jnp.float32)
    summed = summed.reshape(2, channels, layers, on_lane.shape[1])
    return summed[0] + summed[1]


def gather_block(fields, on_layer, on_lane):
    channels, layers, lanes = fields.shape
    high, low = split_bf16(fields)
    stacked = jnp.concatenate([high, low], axis=0).reshape(2 * channels * layers, lanes)
    picked = lax.dot_general(
        stacked, on_lane, (((1,), (1,)), ((), ())), preferred_element_type=jnp.float32
    )
    picked = picked.reshape(2, channels, layers, on_lane.shape[0])
    return jnp.sum((picked[0] + picked[1]) * on_layer[None], axis=1)


def advance_block(buffer, cell_flow, cell_solids):
    speeds = buffer[0:3]
    friction = buffer[7]
    mobility = buffer[8]
    cell_void = 1.0 / (1.0 + cell_solids)
    relaxation = time_step * friction * mobility / (cell_void * cell_void)
    live_mask = (buffer[6] > 0).astype(jnp.float32)
    gravity_push = jnp.zeros_like(speeds).at[2].set(time_step * gravity * live_mask)
    new_speeds = (speeds + relaxation * cell_flow + gravity_push) / (1.0 + relaxation)
    spins = buffer[3:6] / (1.0 + relaxation)
    places = buffer[9:12] + time_step * new_speeds
    return jnp.concatenate([new_speeds, spins, buffer[6:9], places, buffer[12:14]], axis=0)


def slabs_to_blocks(field, blocks_x, blocks_y):
    channels, layers_z, cells_nx, cells_ny = field.shape
    cells_x, cells_y = cells_nx // blocks_x, cells_ny // blocks_y
    arranged = field.reshape(channels, layers_z, blocks_x, cells_x, blocks_y, cells_y).transpose(
        0, 2, 4, 1, 3, 5
    )
    arranged = arranged.reshape(channels, blocks_x * blocks_y * layers_z, cells_x * cells_y)
    return lax.all_to_all(arranged, ("dx", "dy"), split_axis=1, concat_axis=1, tiled=True)


def blocks_to_slabs(field, blocks_x, blocks_y, cells_x, cells_y):
    channels, depth, lanes = field.shape
    layers_z = depth // (blocks_x * blocks_y)
    moved = lax.all_to_all(field, ("dx", "dy"), split_axis=1, concat_axis=1, tiled=True)
    arranged = moved.reshape(channels, blocks_x, blocks_y, layers_z, cells_x, cells_y).transpose(
        0, 3, 1, 4, 2, 5
    )
    return arranged.reshape(channels, layers_z, blocks_x * cells_x, blocks_y * cells_y)


def along_z(field):
    zero = jnp.zeros_like(field[..., :1, :])
    above = jnp.concatenate([field[..., 1:, :], zero], axis=-2)
    below = jnp.concatenate([zero, field[..., :-1, :]], axis=-2)
    return above, below


def along_x(field, cells_y):
    ahead = from_behind(field[..., :cells_y], "dx", -1)
    behind = from_behind(field[..., field.shape[-1] - cells_y :], "dx", 1)
    plus = jnp.concatenate([field[..., cells_y:], ahead], axis=-1)
    minus = jnp.concatenate([behind, field[..., :-cells_y]], axis=-1)
    return plus, minus


def lane_selectors(cells_x, cells_y):
    lane = lax.broadcasted_iota(jnp.int32, (cells_x * cells_y, cells_x), 0)
    row = lax.broadcasted_iota(jnp.int32, (cells_x * cells_y, cells_x), 1)
    first = (lane == row * cells_y).astype(jnp.float32)
    last = (lane == row * cells_y + cells_y - 1).astype(jnp.float32)
    spreader = (lane // cells_y == row).astype(jnp.float32).T
    return first, last, spreader


def along_y(field, selectors, cells_y):
    first, last, spreader = selectors
    shape = field.shape
    flat = field.reshape(-1, shape[-1])
    exact = lax.Precision.HIGHEST
    ahead = from_behind(jnp.dot(flat, first, precision=exact), "dy", -1)
    behind = from_behind(jnp.dot(flat, last, precision=exact), "dy", 1)
    spread_ahead = jnp.dot(ahead, spreader, precision=exact).reshape(shape)
    spread_behind = jnp.dot(behind, spreader, precision=exact).reshape(shape)
    lane_y = lax.broadcasted_iota(jnp.int32, shape, len(shape) - 1) % cells_y
    plus = jnp.where(lane_y == cells_y - 1, spread_ahead, jnp.roll(field, -1, axis=-1))
    minus = jnp.where(lane_y == 0, spread_behind, jnp.roll(field, 1, axis=-1))
    return plus, minus


def fluid_step(velocity, pressure, deposits, selectors, cells_y):
    solids = deposits[0]
    voidage = 1.0 / (1.0 + solids)
    growth = (1.0 + solids) * (1.0 + solids)
    drag_rate = deposits[1] * growth
    drag_pull = deposits[2:5] * growth
    stacked = jnp.concatenate([velocity, pressure[None]], axis=0)
    z_plus, z_minus = along_z(stacked)
    x_plus, x_minus = along_x(stacked, cells_y)
    y_plus, y_minus = along_y(stacked, selectors, cells_y)
    beside_all = (z_plus + z_minus) + x_plus + x_minus + y_plus + y_minus
    predicted = (
        velocity + time_step * (viscosity * (beside_all[:3] - 6.0 * velocity) + drag_pull)
    ) / (1.0 + time_step * drag_rate)
    flux = voidage[None] * predicted
    fx_plus, fx_minus = along_x(flux[0], cells_y)
    fy_plus, fy_minus = along_y(flux[1], selectors, cells_y)
    fz_plus, fz_minus = along_z(flux[2])
    divergence = 0.5 * (fx_plus - fx_minus) + 0.5 * (fy_plus - fy_minus) + 0.5 * (fz_plus - fz_minus)
    pressure_new = (beside_all[3] - divergence / time_step) / 6.0
    px_plus, px_minus = along_x(pressure_new, cells_y)
    py_plus, py_minus = along_y(pressure_new, selectors, cells_y)
    pz_plus, pz_minus = along_z(pressure_new)
    gradient = jnp.stack(
        [0.5 * (px_plus - px_minus), 0.5 * (py_plus - py_minus), 0.5 * (pz_plus - pz_minus)], axis=0
    )
    return (predicted - time_step * gradient, pressure_new)


def shards(particles, leave_lists, leave_counts, slot_cells, velocity, pressure):
    blocks_x = lax.axis_size("dx")
    blocks_y = lax.axis_size("dy")
    records = particles[0, 0]
    leaver_lists = leave_lists[0, 0]
    leaver_counts = leave_counts[0, 0]
    cell_index = slot_cells[0, 0]
    capacity = leaver_lists.shape[1]
    holders = records.shape[1]
    cells_x = velocity.shape[2] // blocks_x
    cells_y = velocity.shape[3] // blocks_y
    lanes = cells_x * cells_y
    depth = velocity.shape[1] * blocks_x * blocks_y

    fields = slabs_to_blocks(
        jnp.concatenate([velocity, pressure[None]], axis=0), blocks_x, blocks_y
    )
    flow = fields[:3]
    pressure_block = fields[3]

    positions = jnp.arange(capacity, dtype=jnp.int32)
    validity = (positions[None, :] < leaver_counts[:, None]).astype(jnp.float32)
    flat_list = leaver_lists.reshape(-1)
    named = (flat_list[None, :] == lax.broadcasted_iota(jnp.int32, (holders, flat_list.shape[0]), 0)) & (
        validity.reshape(1, -1) > 0
    )
    departed = jnp.any(named, axis=1).astype(jnp.float32)
    remaining = records * (1.0 - departed)[None, :]
    outgoing = records[:, flat_list].reshape(records.shape[0], 4, capacity) * validity[None]
    arrivals = migrate(outgoing)
    buffer = jnp.concatenate([remaining] + arrivals, axis=1)

    layer_of = cell_index // lanes
    lane_of = cell_index % lanes
    on_layer = (
        lax.broadcasted_iota(jnp.int32, (depth, cell_index.shape[0]), 0) == layer_of[None, :]
    ).astype(jnp.float32)
    on_lane = (
        lax.broadcasted_iota(jnp.int32, (cell_index.shape[0], lanes), 1) == lane_of[:, None]
    ).astype(jnp.bfloat16)

    selectors = lane_selectors(cells_x, cells_y)
    for coupling in range(COUPLINGS):
        deposits = deposit_block(buffer, on_layer, on_lane)
        flow, pressure_block = fluid_step(flow, pressure_block, deposits, selectors, cells_y)
        picked = gather_block(
            jnp.concatenate([flow, deposits[:1]], axis=0), on_layer, on_lane
        )
        if coupling == COUPLINGS - 1:
            fields = blocks_to_slabs(
                jnp.concatenate([flow, pressure_block[None]], axis=0), blocks_x, blocks_y, cells_x, cells_y
            )
            fields, picked = lax.optimization_barrier((fields, picked))
        buffer = advance_block(buffer, picked[:3], picked[3])

    return (buffer[None, None], fields[:3], fields[3])


def solution(mesh):
    placed = (
        P("dx", "dy", None, None),
        P("dx", "dy", None, None),
        P("dx", "dy", None),
        P("dx", "dy", None),
        P(None, ("dx", "dy"), None, None),
        P(("dx", "dy"), None, None),
    )
    return jax.shard_map(
        shards,
        mesh=mesh,
        in_specs=placed,
        out_specs=(
            P("dx", "dy", None, None),
            P(None, ("dx", "dy"), None, None),
            P(("dx", "dy"), None, None),
        ),
        check_vma=False,
    )
```

```python
import jax
import jax.numpy as jnp
from jax import lax
from jax.sharding import PartitionSpec as P

COUPLINGS = 2


time_step = 0.1
viscosity = 0.5
gravity = -1.0


def from_behind(value, axis, steps):
    count = lax.axis_size(axis)
    pairs = [(source, (source + steps) % count) for source in range(count)]
    return lax.ppermute(value, axis, pairs)


def migrate(outgoing):
    arrivals = []
    for offset in (1, -1):
        arrivals.append(from_behind(outgoing[:, (1 - offset) // 2], "dx", offset))
    for offset in (1, -1):
        arrivals.append(from_behind(outgoing[:, 2 + (1 - offset) // 2], "dy", offset))
    return arrivals


def split_bf16(values):
    high = lax.reduce_precision(values, exponent_bits=8, mantissa_bits=7)
    low = values - high
    return high.astype(jnp.bfloat16), low.astype(jnp.bfloat16)


def deposit_block(buffer, on_layer, on_lane):
    sources = jnp.concatenate([buffer[6:8], buffer[7][None] * buffer[0:3]], axis=0)
    layered = sources[:, None, :] * on_layer[None]
    high, low = split_bf16(layered)
    channels, layers, slots = layered.shape
    stacked = jnp.concatenate([high, low], axis=0).reshape(2 * channels * layers, slots)
    summed = jnp.dot(stacked, on_lane, preferred_element_type=jnp.float32)
    summed = summed.reshape(2, channels, layers, on_lane.shape[1])
    return summed[0] + summed[1]


def gather_block(fields, on_layer, on_lane):
    channels, layers, lanes = fields.shape
    high, low = split_bf16(fields)
    stacked = jnp.concatenate([high, low], axis=0).reshape(2 * channels * layers, lanes)
    picked = lax.dot_general(
        stacked, on_lane, (((1,), (1,)), ((), ())), preferred_element_type=jnp.float32
    )
    picked = picked.reshape(2, channels, layers, on_lane.shape[0])
    return jnp.sum((picked[0] + picked[1]) * on_layer[None], axis=1)


def advance_block(buffer, cell_flow, cell_solids):
    speeds = buffer[0:3]
    friction = buffer[7]
    mobility = buffer[8]
    cell_void = 1.0 / (1.0 + cell_solids)
    relaxation = time_step * friction * mobility / (cell_void * cell_void)
    live_mask = (buffer[6] > 0).astype(jnp.float32)
    gravity_push = jnp.zeros_like(speeds).at[2].set(time_step * gravity * live_mask)
    new_speeds = (speeds + relaxation * cell_flow + gravity_push) / (1.0 + relaxation)
    spins = buffer[3:6] / (1.0 + relaxation)
    places = buffer[9:12] + time_step * new_speeds
    return jnp.concatenate([new_speeds, spins, buffer[6:9], places, buffer[12:14]], axis=0)


def slabs_to_blocks(field, blocks_x, blocks_y):
    channels, layers_z, cells_nx, cells_ny = field.shape
    cells_x, cells_y = cells_nx // blocks_x, cells_ny // blocks_y
    arranged = field.reshape(channels, layers_z, blocks_x, cells_x, blocks_y, cells_y).transpose(
        0, 2, 4, 1, 3, 5
    )
    arranged = arranged.reshape(channels, blocks_x * blocks_y * layers_z, cells_x * cells_y)
    return lax.all_to_all(arranged, ("dx", "dy"), split_axis=1, concat_axis=1, tiled=True)


def blocks_to_slabs(field, blocks_x, blocks_y, cells_x, cells_y):
    channels, depth, lanes = field.shape
    layers_z = depth // (blocks_x * blocks_y)
    moved = lax.all_to_all(field, ("dx", "dy"), split_axis=1, concat_axis=1, tiled=True)
    arranged = moved.reshape(channels, blocks_x, blocks_y, layers_z, cells_x, cells_y).transpose(
        0, 3, 1, 4, 2, 5
    )
    return arranged.reshape(channels, layers_z, blocks_x * cells_x, blocks_y * cells_y)


def along_z(field):
    zero = jnp.zeros_like(field[..., :1, :])
    above = jnp.concatenate([field[..., 1:, :], zero], axis=-2)
    below = jnp.concatenate([zero, field[..., :-1, :]], axis=-2)
    return above, below


def faces_x(field, cells_y):
    ahead = from_behind(field[..., :cells_y], "dx", -1)
    behind = from_behind(field[..., field.shape[-1] - cells_y :], "dx", 1)
    return ahead, behind


def along_x(field, cells_y, faces=None):
    ahead, behind = faces_x(field, cells_y) if faces is None else faces
    plus = jnp.concatenate([field[..., cells_y:], ahead], axis=-1)
    minus = jnp.concatenate([behind, field[..., :-cells_y]], axis=-1)
    return plus, minus


def lane_selectors(cells_x, cells_y):
    lane = lax.broadcasted_iota(jnp.int32, (cells_x * cells_y, cells_x), 0)
    row = lax.broadcasted_iota(jnp.int32, (cells_x * cells_y, cells_x), 1)
    first = (lane == row * cells_y).astype(jnp.float32)
    last = (lane == row * cells_y + cells_y - 1).astype(jnp.float32)
    spreader = (lane // cells_y == row).astype(jnp.float32).T
    return first, last, spreader


def faces_y(field, selectors):
    first, last, _ = selectors
    flat = field.reshape(-1, field.shape[-1])
    exact = lax.Precision.HIGHEST
    ahead = from_behind(jnp.dot(flat, first, precision=exact), "dy", -1)
    behind = from_behind(jnp.dot(flat, last, precision=exact), "dy", 1)
    return ahead, behind


def along_y(field, selectors, cells_y, faces=None):
    spreader = selectors[2]
    shape = field.shape
    exact = lax.Precision.HIGHEST
    ahead, behind = faces_y(field, selectors) if faces is None else faces
    spread_ahead = jnp.dot(ahead, spreader, precision=exact).reshape(shape)
    spread_behind = jnp.dot(behind, spreader, precision=exact).reshape(shape)
    lane_y = lax.broadcasted_iota(jnp.int32, shape, len(shape) - 1) % cells_y
    plus = jnp.where(lane_y == cells_y - 1, spread_ahead, jnp.roll(field, -1, axis=-1))
    minus = jnp.where(lane_y == 0, spread_behind, jnp.roll(field, 1, axis=-1))
    return plus, minus


def fluid_step(velocity, pressure, deposits, faces, selectors, cells_y):
    solids = deposits[0]
    voidage = 1.0 / (1.0 + solids)
    growth = (1.0 + solids) * (1.0 + solids)
    drag_rate = deposits[1] * growth
    drag_pull = deposits[2:5] * growth
    stacked = jnp.concatenate([velocity, pressure[None]], axis=0)
    z_plus, z_minus = along_z(stacked)
    x_plus, x_minus = along_x(stacked, cells_y, faces[0])
    y_plus, y_minus = along_y(stacked, selectors, cells_y, faces[1])
    beside_all = (z_plus + z_minus) + x_plus + x_minus + y_plus + y_minus
    predicted = (
        velocity + time_step * (viscosity * (beside_all[:3] - 6.0 * velocity) + drag_pull)
    ) / (1.0 + time_step * drag_rate)
    flux = voidage[None] * predicted
    fx_plus, fx_minus = along_x(flux[0], cells_y)
    fy_plus, fy_minus = along_y(flux[1], selectors, cells_y)
    fz_plus, fz_minus = along_z(flux[2])
    divergence = 0.5 * (fx_plus - fx_minus) + 0.5 * (fy_plus - fy_minus) + 0.5 * (fz_plus - fz_minus)
    pressure_new = (beside_all[3] - divergence / time_step) / 6.0
    px_plus, px_minus = along_x(pressure_new, cells_y)
    py_plus, py_minus = along_y(pressure_new, selectors, cells_y)
    pz_plus, pz_minus = along_z(pressure_new)
    gradient = jnp.stack(
        [0.5 * (px_plus - px_minus), 0.5 * (py_plus - py_minus), 0.5 * (pz_plus - pz_minus)], axis=0
    )
    return (predicted - time_step * gradient, pressure_new)


def shards(particles, leave_lists, leave_counts, slot_cells, velocity, pressure):
    blocks_x = lax.axis_size("dx")
    blocks_y = lax.axis_size("dy")
    records = particles[0, 0]
    leaver_lists = leave_lists[0, 0]
    leaver_counts = leave_counts[0, 0]
    cell_index = slot_cells[0, 0]
    capacity = leaver_lists.shape[1]
    holders = records.shape[1]
    cells_x = velocity.shape[2] // blocks_x
    cells_y = velocity.shape[3] // blocks_y
    lanes = cells_x * cells_y
    depth = velocity.shape[1] * blocks_x * blocks_y

    fields = slabs_to_blocks(
        jnp.concatenate([velocity, pressure[None]], axis=0), blocks_x, blocks_y
    )
    flow = fields[:3]
    pressure_block = fields[3]

    positions = jnp.arange(capacity, dtype=jnp.int32)
    validity = (positions[None, :] < leaver_counts[:, None]).astype(jnp.float32)
    flat_list = leaver_lists.reshape(-1)
    named = (flat_list[None, :] == lax.broadcasted_iota(jnp.int32, (holders, flat_list.shape[0]), 0)) & (
        validity.reshape(1, -1) > 0
    )
    departed = jnp.any(named, axis=1).astype(jnp.float32)
    remaining = records * (1.0 - departed)[None, :]
    chosen = (
        lax.broadcasted_iota(jnp.int32, (holders, flat_list.shape[0]), 0) == flat_list[None, :]
    ).astype(jnp.bfloat16)
    high = lax.reduce_precision(records, exponent_bits=8, mantissa_bits=7)
    rest = records - high
    middle = lax.reduce_precision(rest, exponent_bits=8, mantissa_bits=7)
    low = rest - middle
    parts = jnp.concatenate([high, middle, low], axis=0).astype(jnp.bfloat16)
    picked_rows = jnp.dot(parts, chosen, preferred_element_type=jnp.float32)
    rows = records.shape[0]
    picked_rows = (picked_rows[:rows] + picked_rows[rows : 2 * rows]) + picked_rows[2 * rows :]
    outgoing = picked_rows.reshape(rows, 4, capacity) * validity[None]
    arrivals = migrate(outgoing)
    buffer = jnp.concatenate([remaining] + arrivals, axis=1)

    layer_of = cell_index // lanes
    lane_of = cell_index % lanes
    on_layer = (
        lax.broadcasted_iota(jnp.int32, (depth, cell_index.shape[0]), 0) == layer_of[None, :]
    ).astype(jnp.float32)
    on_lane = (
        lax.broadcasted_iota(jnp.int32, (cell_index.shape[0], lanes), 1) == lane_of[:, None]
    ).astype(jnp.bfloat16)

    selectors = lane_selectors(cells_x, cells_y)
    stacked = jnp.concatenate([flow, pressure_block[None]], axis=0)
    faces = (faces_x(stacked, cells_y), faces_y(stacked, selectors))
    for coupling in range(COUPLINGS):
        deposits = deposit_block(buffer, on_layer, on_lane)
        if coupling > 0:
            faces, deposits = lax.optimization_barrier((faces, deposits))
        flow, pressure_block = fluid_step(flow, pressure_block, deposits, faces, selectors, cells_y)
        if coupling < COUPLINGS - 1:
            stacked = jnp.concatenate([flow, pressure_block[None]], axis=0)
            faces = (faces_x(stacked, cells_y), faces_y(stacked, selectors))
        picked = gather_block(
            jnp.concatenate([flow, deposits[:1]], axis=0), on_layer, on_lane
        )
        if coupling == COUPLINGS - 1:
            fields = blocks_to_slabs(
                jnp.concatenate([flow, pressure_block[None]], axis=0), blocks_x, blocks_y, cells_x, cells_y
            )
            fields, picked = lax.optimization_barrier((fields, picked))
        buffer = advance_block(buffer, picked[:3], picked[3])

    return (buffer[None, None], fields[:3], fields[3])


def solution(mesh):
    placed = (
        P("dx", "dy", None, None),
        P("dx", "dy", None, None),
        P("dx", "dy", None),
        P("dx", "dy", None),
        P(None, ("dx", "dy"), None, None),
        P(("dx", "dy"), None, None),
    )
    return jax.shard_map(
        shards,
        mesh=mesh,
        in_specs=placed,
        out_specs=(
            P("dx", "dy", None, None),
            P(None, ("dx", "dy"), None, None),
            P(("dx", "dy"), None, None),
        ),
        check_vma=False,
    )
```

```python
import jax
import jax.numpy as jnp
from jax import lax
from jax.sharding import PartitionSpec as P

COUPLINGS = 2


time_step = 0.1
viscosity = 0.5
gravity = -1.0


def from_behind(value, axis, steps):
    count = lax.axis_size(axis)
    pairs = [(source, (source + steps) % count) for source in range(count)]
    return lax.ppermute(value, axis, pairs)


def migrate(outgoing):
    arrivals = []
    for offset in (1, -1):
        arrivals.append(from_behind(outgoing[:, (1 - offset) // 2], "dx", offset))
    for offset in (1, -1):
        arrivals.append(from_behind(outgoing[:, 2 + (1 - offset) // 2], "dy", offset))
    return arrivals


def split_bf16(values):
    high = lax.reduce_precision(values, exponent_bits=8, mantissa_bits=7)
    low = values - high
    return high.astype(jnp.bfloat16), low.astype(jnp.bfloat16)


def deposit_block(buffer, on_layer, on_lane):
    sources = jnp.concatenate([buffer[6:8], buffer[7][None] * buffer[0:3]], axis=0)
    layered = sources[:, None, :] * on_layer[None]
    high, low = split_bf16(layered)
    channels, layers, slots = layered.shape
    stacked = jnp.concatenate([high, low], axis=0).reshape(2 * channels * layers, slots)
    summed = jnp.dot(stacked, on_lane, preferred_element_type=jnp.float32)
    summed = summed.reshape(2, channels, layers, on_lane.shape[1])
    return summed[0] + summed[1]


def gather_block(fields, on_layer, on_lane):
    channels, layers, lanes = fields.shape
    high, low = split_bf16(fields)
    stacked = jnp.concatenate([high, low], axis=0).reshape(2 * channels * layers, lanes)
    picked = lax.dot_general(
        stacked, on_lane, (((1,), (1,)), ((), ())), preferred_element_type=jnp.float32
    )
    picked = picked.reshape(2, channels, layers, on_lane.shape[0])
    return jnp.sum((picked[0] + picked[1]) * on_layer[None], axis=1)


def advance_block(buffer, cell_flow, cell_solids):
    speeds = buffer[0:3]
    friction = buffer[7]
    mobility = buffer[8]
    cell_void = 1.0 / (1.0 + cell_solids)
    relaxation = time_step * friction * mobility / (cell_void * cell_void)
    live_mask = (buffer[6] > 0).astype(jnp.float32)
    gravity_push = jnp.zeros_like(speeds).at[2].set(time_step * gravity * live_mask)
    new_speeds = (speeds + relaxation * cell_flow + gravity_push) / (1.0 + relaxation)
    spins = buffer[3:6] / (1.0 + relaxation)
    places = buffer[9:12] + time_step * new_speeds
    return jnp.concatenate([new_speeds, spins, buffer[6:9], places, buffer[12:14]], axis=0)


def slabs_to_blocks(field, blocks_x, blocks_y):
    channels, layers_z, cells_nx, cells_ny = field.shape
    cells_x, cells_y = cells_nx // blocks_x, cells_ny // blocks_y
    arranged = field.reshape(channels, layers_z, blocks_x, cells_x, blocks_y, cells_y).transpose(
        0, 2, 4, 1, 3, 5
    )
    arranged = arranged.reshape(channels, blocks_x * blocks_y * layers_z, cells_x * cells_y)
    return lax.all_to_all(arranged, ("dx", "dy"), split_axis=1, concat_axis=1, tiled=True)


def blocks_to_slabs(field, blocks_x, blocks_y, cells_x, cells_y):
    channels, depth, lanes = field.shape
    layers_z = depth // (blocks_x * blocks_y)
    moved = lax.all_to_all(field, ("dx", "dy"), split_axis=1, concat_axis=1, tiled=True)
    arranged = moved.reshape(channels, blocks_x, blocks_y, layers_z, cells_x, cells_y).transpose(
        0, 3, 1, 4, 2, 5
    )
    return arranged.reshape(channels, layers_z, blocks_x * cells_x, blocks_y * cells_y)


def along_z(field):
    zero = jnp.zeros_like(field[..., :1, :])
    above = jnp.concatenate([field[..., 1:, :], zero], axis=-2)
    below = jnp.concatenate([zero, field[..., :-1, :]], axis=-2)
    return above, below


def faces_x(field, cells_y):
    ahead = from_behind(field[..., :cells_y], "dx", -1)
    behind = from_behind(field[..., field.shape[-1] - cells_y :], "dx", 1)
    return ahead, behind


def along_x(field, cells_y, faces=None):
    ahead, behind = faces_x(field, cells_y) if faces is None else faces
    plus = jnp.concatenate([field[..., cells_y:], ahead], axis=-1)
    minus = jnp.concatenate([behind, field[..., :-cells_y]], axis=-1)
    return plus, minus


def lane_selectors(cells_x, cells_y):
    lane = lax.broadcasted_iota(jnp.int32, (cells_x * cells_y, cells_x), 0)
    row = lax.broadcasted_iota(jnp.int32, (cells_x * cells_y, cells_x), 1)
    first = (lane == row * cells_y).astype(jnp.float32)
    last = (lane == row * cells_y + cells_y - 1).astype(jnp.float32)
    spreader = (lane // cells_y == row).astype(jnp.float32).T
    return first, last, spreader


def faces_y(field, selectors):
    first, last, _ = selectors
    flat = field.reshape(-1, field.shape[-1])
    exact = lax.Precision.HIGHEST
    ahead = from_behind(jnp.dot(flat, first, precision=exact), "dy", -1)
    behind = from_behind(jnp.dot(flat, last, precision=exact), "dy", 1)
    return ahead, behind


def along_y(field, selectors, cells_y, faces=None):
    spreader = selectors[2]
    shape = field.shape
    exact = lax.Precision.HIGHEST
    ahead, behind = faces_y(field, selectors) if faces is None else faces
    spread_ahead = jnp.dot(ahead, spreader, precision=exact).reshape(shape)
    spread_behind = jnp.dot(behind, spreader, precision=exact).reshape(shape)
    lane_y = lax.broadcasted_iota(jnp.int32, shape, len(shape) - 1) % cells_y
    plus = jnp.where(lane_y == cells_y - 1, spread_ahead, jnp.roll(field, -1, axis=-1))
    minus = jnp.where(lane_y == 0, spread_behind, jnp.roll(field, 1, axis=-1))
    return plus, minus


def fluid_step(velocity, pressure, deposits, faces, selectors, cells_y):
    solids = deposits[0]
    voidage = 1.0 / (1.0 + solids)
    growth = (1.0 + solids) * (1.0 + solids)
    drag_rate = deposits[1] * growth
    drag_pull = deposits[2:5] * growth
    stacked = jnp.concatenate([velocity, pressure[None]], axis=0)
    z_plus, z_minus = along_z(stacked)
    x_plus, x_minus = along_x(stacked, cells_y, faces[0])
    y_plus, y_minus = along_y(stacked, selectors, cells_y, faces[1])
    beside_all = (z_plus + z_minus) + x_plus + x_minus + y_plus + y_minus
    predicted = (
        velocity + time_step * (viscosity * (beside_all[:3] - 6.0 * velocity) + drag_pull)
    ) / (1.0 + time_step * drag_rate)
    flux = voidage[None] * predicted
    fx_plus, fx_minus = along_x(flux[0], cells_y)
    fy_plus, fy_minus = along_y(flux[1], selectors, cells_y)
    fz_plus, fz_minus = along_z(flux[2])
    divergence = 0.5 * (fx_plus - fx_minus) + 0.5 * (fy_plus - fy_minus) + 0.5 * (fz_plus - fz_minus)
    pressure_new = (beside_all[3] - divergence / time_step) / 6.0
    px_plus, px_minus = along_x(pressure_new, cells_y)
    py_plus, py_minus = along_y(pressure_new, selectors, cells_y)
    pz_plus, pz_minus = along_z(pressure_new)
    gradient = jnp.stack(
        [0.5 * (px_plus - px_minus), 0.5 * (py_plus - py_minus), 0.5 * (pz_plus - pz_minus)], axis=0
    )
    return (predicted - time_step * gradient, pressure_new)


def shards(particles, leave_lists, leave_counts, slot_cells, velocity, pressure):
    blocks_x = lax.axis_size("dx")
    blocks_y = lax.axis_size("dy")
    records = particles[0, 0]
    leaver_lists = leave_lists[0, 0]
    leaver_counts = leave_counts[0, 0]
    cell_index = slot_cells[0, 0]
    capacity = leaver_lists.shape[1]
    holders = records.shape[1]
    cells_x = velocity.shape[2] // blocks_x
    cells_y = velocity.shape[3] // blocks_y
    lanes = cells_x * cells_y
    depth = velocity.shape[1] * blocks_x * blocks_y

    fields = slabs_to_blocks(
        jnp.concatenate([velocity, pressure[None]], axis=0), blocks_x, blocks_y
    )
    positions = jnp.arange(capacity, dtype=jnp.int32)
    validity = (positions[None, :] < leaver_counts[:, None]).astype(jnp.float32)
    flat_list = leaver_lists.reshape(-1)
    named = (flat_list[None, :] == lax.broadcasted_iota(jnp.int32, (holders, flat_list.shape[0]), 0)) & (
        validity.reshape(1, -1) > 0
    )
    departed = jnp.any(named, axis=1).astype(jnp.float32)
    remaining = records * (1.0 - departed)[None, :]
    chosen = (
        lax.broadcasted_iota(jnp.int32, (holders, flat_list.shape[0]), 0) == flat_list[None, :]
    ).astype(jnp.bfloat16)
    high = lax.reduce_precision(records, exponent_bits=8, mantissa_bits=7)
    rest = records - high
    middle = lax.reduce_precision(rest, exponent_bits=8, mantissa_bits=7)
    low = rest - middle
    parts = jnp.concatenate([high, middle, low], axis=0).astype(jnp.bfloat16)
    picked_rows = jnp.dot(parts, chosen, preferred_element_type=jnp.float32)
    rows = records.shape[0]
    picked_rows = (picked_rows[:rows] + picked_rows[rows : 2 * rows]) + picked_rows[2 * rows :]
    outgoing = picked_rows.reshape(rows, 4, capacity) * validity[None]
    arrivals = migrate(outgoing)
    buffer = jnp.concatenate([remaining] + arrivals, axis=1)

    layer_of = cell_index // lanes
    lane_of = cell_index % lanes
    on_layer = (
        lax.broadcasted_iota(jnp.int32, (depth, cell_index.shape[0]), 0) == layer_of[None, :]
    ).astype(jnp.float32)
    on_lane = (
        lax.broadcasted_iota(jnp.int32, (cell_index.shape[0], lanes), 1) == lane_of[:, None]
    ).astype(jnp.bfloat16)

    selectors = lane_selectors(cells_x, cells_y)
    fields, buffer = lax.optimization_barrier((fields, buffer))
    flow = fields[:3]
    pressure_block = fields[3]
    stacked = jnp.concatenate([flow, pressure_block[None]], axis=0)
    faces = (faces_x(stacked, cells_y), faces_y(stacked, selectors))
    for coupling in range(COUPLINGS):
        deposits = deposit_block(buffer, on_layer, on_lane)
        faces, deposits = lax.optimization_barrier((faces, deposits))
        flow, pressure_block = fluid_step(flow, pressure_block, deposits, faces, selectors, cells_y)
        if coupling < COUPLINGS - 1:
            stacked = jnp.concatenate([flow, pressure_block[None]], axis=0)
            faces = (faces_x(stacked, cells_y), faces_y(stacked, selectors))
        picked = gather_block(
            jnp.concatenate([flow, deposits[:1]], axis=0), on_layer, on_lane
        )
        if coupling == COUPLINGS - 1:
            fields = blocks_to_slabs(
                jnp.concatenate([flow, pressure_block[None]], axis=0), blocks_x, blocks_y, cells_x, cells_y
            )
            fields, picked = lax.optimization_barrier((fields, picked))
        buffer = advance_block(buffer, picked[:3], picked[3])

    return (buffer[None, None], fields[:3], fields[3])


def solution(mesh):
    placed = (
        P("dx", "dy", None, None),
        P("dx", "dy", None, None),
        P("dx", "dy", None),
        P("dx", "dy", None),
        P(None, ("dx", "dy"), None, None),
        P(("dx", "dy"), None, None),
    )
    return jax.shard_map(
        shards,
        mesh=mesh,
        in_specs=placed,
        out_specs=(
            P("dx", "dy", None, None),
            P(None, ("dx", "dy"), None, None),
            P(("dx", "dy"), None, None),
        ),
        check_vma=False,
    )
```

```python
import jax
import jax.numpy as jnp
from jax import lax
from jax.sharding import PartitionSpec as P

COUPLINGS = 2


time_step = 0.1
viscosity = 0.5
gravity = -1.0


def from_behind(value, axis, steps):
    count = lax.axis_size(axis)
    pairs = [(source, (source + steps) % count) for source in range(count)]
    return lax.ppermute(value, axis, pairs)


def migrate(outgoing):
    arrivals = []
    for offset in (1, -1):
        arrivals.append(from_behind(outgoing[:, (1 - offset) // 2], "dx", offset))
    for offset in (1, -1):
        arrivals.append(from_behind(outgoing[:, 2 + (1 - offset) // 2], "dy", offset))
    return arrivals


def split_bf16(values):
    high = lax.reduce_precision(values, exponent_bits=8, mantissa_bits=7)
    low = values - high
    return high.astype(jnp.bfloat16), low.astype(jnp.bfloat16)


def deposit_block(buffer, on_layer, on_lane):
    sources = jnp.concatenate([buffer[6:8], buffer[7][None] * buffer[0:3]], axis=0)
    layered = sources[:, None, :] * on_layer[None]
    high, low = split_bf16(layered)
    channels, layers, slots = layered.shape
    stacked = jnp.concatenate([high, low], axis=0).reshape(2 * channels * layers, slots)
    summed = jnp.dot(stacked, on_lane, preferred_element_type=jnp.float32)
    summed = summed.reshape(2, channels, layers, on_lane.shape[1])
    return summed[0] + summed[1]


def gather_block(fields, on_layer, on_lane):
    channels, layers, lanes = fields.shape
    high, low = split_bf16(fields)
    stacked = jnp.concatenate([high, low], axis=0).reshape(2 * channels * layers, lanes)
    picked = lax.dot_general(
        stacked, on_lane, (((1,), (1,)), ((), ())), preferred_element_type=jnp.float32
    )
    picked = picked.reshape(2, channels, layers, on_lane.shape[0])
    return jnp.sum((picked[0] + picked[1]) * on_layer[None], axis=1)


def advance_block(buffer, cell_flow, cell_solids):
    speeds = buffer[0:3]
    friction = buffer[7]
    mobility = buffer[8]
    cell_void = 1.0 / (1.0 + cell_solids)
    relaxation = time_step * friction * mobility / (cell_void * cell_void)
    live_mask = (buffer[6] > 0).astype(jnp.float32)
    gravity_push = jnp.zeros_like(speeds).at[2].set(time_step * gravity * live_mask)
    new_speeds = (speeds + relaxation * cell_flow + gravity_push) / (1.0 + relaxation)
    spins = buffer[3:6] / (1.0 + relaxation)
    places = buffer[9:12] + time_step * new_speeds
    return jnp.concatenate([new_speeds, spins, buffer[6:9], places, buffer[12:14]], axis=0)


def slabs_to_blocks(field, blocks_x, blocks_y):
    channels, layers_z, cells_nx, cells_ny = field.shape
    cells_x, cells_y = cells_nx // blocks_x, cells_ny // blocks_y
    arranged = field.reshape(channels, layers_z, blocks_x, cells_x, blocks_y, cells_y).transpose(
        0, 2, 4, 1, 3, 5
    )
    arranged = arranged.reshape(channels, blocks_x * blocks_y * layers_z, cells_x * cells_y)
    return lax.all_to_all(arranged, ("dx", "dy"), split_axis=1, concat_axis=1, tiled=True)


def blocks_to_slabs(field, blocks_x, blocks_y, cells_x, cells_y):
    channels, depth, lanes = field.shape
    layers_z = depth // (blocks_x * blocks_y)
    moved = lax.all_to_all(field, ("dx", "dy"), split_axis=1, concat_axis=1, tiled=True)
    arranged = moved.reshape(channels, blocks_x, blocks_y, layers_z, cells_x, cells_y).transpose(
        0, 3, 1, 4, 2, 5
    )
    return arranged.reshape(channels, layers_z, blocks_x * cells_x, blocks_y * cells_y)


def along_z(field):
    zero = jnp.zeros_like(field[..., :1, :])
    above = jnp.concatenate([field[..., 1:, :], zero], axis=-2)
    below = jnp.concatenate([zero, field[..., :-1, :]], axis=-2)
    return above, below


def faces_x(field, cells_y):
    ahead = from_behind(field[..., :cells_y], "dx", -1)
    behind = from_behind(field[..., field.shape[-1] - cells_y :], "dx", 1)
    return ahead, behind


def along_x(field, cells_y, faces=None):
    ahead, behind = faces_x(field, cells_y) if faces is None else faces
    plus = jnp.concatenate([field[..., cells_y:], ahead], axis=-1)
    minus = jnp.concatenate([behind, field[..., :-cells_y]], axis=-1)
    return plus, minus


def lane_selectors(cells_x, cells_y):
    lanes = cells_x * cells_y
    lane = lax.broadcasted_iota(jnp.int32, (lanes, 2 * cells_x), 0)
    column = lax.broadcasted_iota(jnp.int32, (lanes, 2 * cells_x), 1)
    picks = jnp.where(column < cells_x, column * cells_y, (column - cells_x) * cells_y + cells_y - 1)
    select = lane == picks
    spread_pick = jnp.where(column < cells_x, column * cells_y + cells_y - 1, (column - cells_x) * cells_y)
    spread = (lane == spread_pick).T
    return select.astype(jnp.bfloat16), spread.astype(jnp.bfloat16)


def exact_pick(values, one_hot):
    high = lax.reduce_precision(values, exponent_bits=8, mantissa_bits=7)
    rest = values - high
    middle = lax.reduce_precision(rest, exponent_bits=8, mantissa_bits=7)
    low = rest - middle
    rows = values.shape[0]
    parts = jnp.concatenate([high, middle, low], axis=0).astype(jnp.bfloat16)
    picked = jnp.dot(parts, one_hot, preferred_element_type=jnp.float32)
    return (picked[:rows] + picked[rows : 2 * rows]) + picked[2 * rows :]


def faces_y(field, selectors):
    cells_x = selectors[0].shape[1] // 2
    both = exact_pick(field.reshape(-1, field.shape[-1]), selectors[0])
    ahead = from_behind(both[:, :cells_x], "dy", -1)
    behind = from_behind(both[:, cells_x:], "dy", 1)
    return ahead, behind


def along_y(field, selectors, cells_y, faces=None):
    shape = field.shape
    ahead, behind = faces_y(field, selectors) if faces is None else faces
    halo = exact_pick(jnp.concatenate([ahead, behind], axis=1), selectors[1]).reshape(shape)
    lane_y = lax.broadcasted_iota(jnp.int32, shape, len(shape) - 1) % cells_y
    plus = jnp.where(lane_y == cells_y - 1, halo, jnp.roll(field, -1, axis=-1))
    minus = jnp.where(lane_y == 0, halo, jnp.roll(field, 1, axis=-1))
    return plus, minus


def fluid_step(velocity, pressure, deposits, faces, selectors, cells_y):
    solids = deposits[0]
    voidage = 1.0 / (1.0 + solids)
    growth = (1.0 + solids) * (1.0 + solids)
    drag_rate = deposits[1] * growth
    drag_pull = deposits[2:5] * growth
    stacked = jnp.concatenate([velocity, pressure[None]], axis=0)
    z_plus, z_minus = along_z(stacked)
    x_plus, x_minus = along_x(stacked, cells_y, faces[0])
    y_plus, y_minus = along_y(stacked, selectors, cells_y, faces[1])
    beside_all = (z_plus + z_minus) + x_plus + x_minus + y_plus + y_minus
    predicted = (
        velocity + time_step * (viscosity * (beside_all[:3] - 6.0 * velocity) + drag_pull)
    ) / (1.0 + time_step * drag_rate)
    flux = voidage[None] * predicted
    fx_plus, fx_minus = along_x(flux[0], cells_y)
    fy_plus, fy_minus = along_y(flux[1], selectors, cells_y)
    fz_plus, fz_minus = along_z(flux[2])
    divergence = 0.5 * (fx_plus - fx_minus) + 0.5 * (fy_plus - fy_minus) + 0.5 * (fz_plus - fz_minus)
    pressure_new = (beside_all[3] - divergence / time_step) / 6.0
    px_plus, px_minus = along_x(pressure_new, cells_y)
    py_plus, py_minus = along_y(pressure_new, selectors, cells_y)
    pz_plus, pz_minus = along_z(pressure_new)
    gradient = jnp.stack(
        [0.5 * (px_plus - px_minus), 0.5 * (py_plus - py_minus), 0.5 * (pz_plus - pz_minus)], axis=0
    )
    return (predicted - time_step * gradient, pressure_new)


def shards(particles, leave_lists, leave_counts, slot_cells, velocity, pressure):
    blocks_x = lax.axis_size("dx")
    blocks_y = lax.axis_size("dy")
    records = particles[0, 0]
    leaver_lists = leave_lists[0, 0]
    leaver_counts = leave_counts[0, 0]
    cell_index = slot_cells[0, 0]
    capacity = leaver_lists.shape[1]
    holders = records.shape[1]
    cells_x = velocity.shape[2] // blocks_x
    cells_y = velocity.shape[3] // blocks_y
    lanes = cells_x * cells_y
    depth = velocity.shape[1] * blocks_x * blocks_y

    fields = slabs_to_blocks(
        jnp.concatenate([velocity, pressure[None]], axis=0), blocks_x, blocks_y
    )
    positions = jnp.arange(capacity, dtype=jnp.int32)
    validity = (positions[None, :] < leaver_counts[:, None]).astype(jnp.float32)
    flat_list = leaver_lists.reshape(-1)
    named = (flat_list[None, :] == lax.broadcasted_iota(jnp.int32, (holders, flat_list.shape[0]), 0)) & (
        validity.reshape(1, -1) > 0
    )
    departed = jnp.any(named, axis=1).astype(jnp.float32)
    remaining = records * (1.0 - departed)[None, :]
    chosen = (
        lax.broadcasted_iota(jnp.int32, (holders, flat_list.shape[0]), 0) == flat_list[None, :]
    ).astype(jnp.bfloat16)
    high = lax.reduce_precision(records, exponent_bits=8, mantissa_bits=7)
    rest = records - high
    middle = lax.reduce_precision(rest, exponent_bits=8, mantissa_bits=7)
    low = rest - middle
    parts = jnp.concatenate([high, middle, low], axis=0).astype(jnp.bfloat16)
    picked_rows = jnp.dot(parts, chosen, preferred_element_type=jnp.float32)
    rows = records.shape[0]
    picked_rows = (picked_rows[:rows] + picked_rows[rows : 2 * rows]) + picked_rows[2 * rows :]
    outgoing = picked_rows.reshape(rows, 4, capacity) * validity[None]
    arrivals = migrate(outgoing)
    buffer = jnp.concatenate([remaining] + arrivals, axis=1)

    layer_of = cell_index // lanes
    lane_of = cell_index % lanes
    on_layer = (
        lax.broadcasted_iota(jnp.int32, (depth, cell_index.shape[0]), 0) == layer_of[None, :]
    ).astype(jnp.float32)
    on_lane = (
        lax.broadcasted_iota(jnp.int32, (cell_index.shape[0], lanes), 1) == lane_of[:, None]
    ).astype(jnp.bfloat16)

    selectors = lane_selectors(cells_x, cells_y)
    fields, buffer = lax.optimization_barrier((fields, buffer))
    flow = fields[:3]
    pressure_block = fields[3]
    stacked = jnp.concatenate([flow, pressure_block[None]], axis=0)
    faces = (faces_x(stacked, cells_y), faces_y(stacked, selectors))
    for coupling in range(COUPLINGS):
        deposits = deposit_block(buffer, on_layer, on_lane)
        faces, deposits = lax.optimization_barrier((faces, deposits))
        flow, pressure_block = fluid_step(flow, pressure_block, deposits, faces, selectors, cells_y)
        if coupling < COUPLINGS - 1:
            stacked = jnp.concatenate([flow, pressure_block[None]], axis=0)
            faces = (faces_x(stacked, cells_y), faces_y(stacked, selectors))
        picked = gather_block(
            jnp.concatenate([flow, deposits[:1]], axis=0), on_layer, on_lane
        )
        if coupling == COUPLINGS - 1:
            fields = blocks_to_slabs(
                jnp.concatenate([flow, pressure_block[None]], axis=0), blocks_x, blocks_y, cells_x, cells_y
            )
            fields, picked = lax.optimization_barrier((fields, picked))
        buffer = advance_block(buffer, picked[:3], picked[3])

    return (buffer[None, None], fields[:3], fields[3])


def solution(mesh):
    placed = (
        P("dx", "dy", None, None),
        P("dx", "dy", None, None),
        P("dx", "dy", None),
        P("dx", "dy", None),
        P(None, ("dx", "dy"), None, None),
        P(("dx", "dy"), None, None),
    )
    return jax.shard_map(
        shards,
        mesh=mesh,
        in_specs=placed,
        out_specs=(
            P("dx", "dy", None, None),
            P(None, ("dx", "dy"), None, None),
            P(("dx", "dy"), None, None),
        ),
        check_vma=False,
    )
```

```python
import math

import jax
import jax.numpy as jnp
from jax import lax
from jax.sharding import PartitionSpec as P

COUPLINGS = 2


time_step = 0.1
viscosity = 0.5
gravity = -1.0


def from_behind(value, axis, steps):
    count = lax.axis_size(axis)
    pairs = [(source, (source + steps) % count) for source in range(count)]
    return lax.ppermute(value, axis, pairs)


def migrate(outgoing):
    arrivals = []
    for offset in (1, -1):
        arrivals.append(from_behind(outgoing[:, (1 - offset) // 2], "dx", offset))
    for offset in (1, -1):
        arrivals.append(from_behind(outgoing[:, 2 + (1 - offset) // 2], "dy", offset))
    return arrivals


def split_bf16(values):
    high = lax.reduce_precision(values, exponent_bits=8, mantissa_bits=7)
    low = values - high
    return high.astype(jnp.bfloat16), low.astype(jnp.bfloat16)


def deposit_block(buffer, on_layer, on_lane):
    sources = jnp.concatenate([buffer[6:8], buffer[7][None] * buffer[0:3]], axis=0)
    layered = sources[:, None, :] * on_layer[None]
    high, low = split_bf16(layered)
    channels, layers, slots = layered.shape
    stacked = jnp.concatenate([high, low], axis=0).reshape(2 * channels * layers, slots)
    summed = jnp.dot(stacked, on_lane, preferred_element_type=jnp.float32)
    summed = summed.reshape(2, channels, layers, on_lane.shape[1])
    return summed[0] + summed[1]


def gather_block(fields, on_layer, on_lane):
    channels, layers, lanes = fields.shape
    high, low = split_bf16(fields)
    stacked = jnp.concatenate([high, low], axis=0).reshape(2 * channels * layers, lanes)
    picked = lax.dot_general(
        stacked, on_lane, (((1,), (1,)), ((), ())), preferred_element_type=jnp.float32
    )
    picked = picked.reshape(2, channels, layers, on_lane.shape[0])
    return jnp.sum((picked[0] + picked[1]) * on_layer[None], axis=1)


def advance_block(buffer, cell_flow, cell_solids):
    speeds = buffer[0:3]
    friction = buffer[7]
    mobility = buffer[8]
    cell_void = 1.0 / (1.0 + cell_solids)
    relaxation = time_step * friction * mobility / (cell_void * cell_void)
    live_mask = (buffer[6] > 0).astype(jnp.float32)
    gravity_push = jnp.zeros_like(speeds).at[2].set(time_step * gravity * live_mask)
    new_speeds = (speeds + relaxation * cell_flow + gravity_push) / (1.0 + relaxation)
    spins = buffer[3:6] / (1.0 + relaxation)
    places = buffer[9:12] + time_step * new_speeds
    return jnp.concatenate([new_speeds, spins, buffer[6:9], places, buffer[12:14]], axis=0)


def slabs_to_blocks(field, blocks_x, blocks_y):
    channels, layers_z, cells_nx, cells_ny = field.shape
    cells_x, cells_y = cells_nx // blocks_x, cells_ny // blocks_y
    arranged = field.reshape(channels, layers_z, blocks_x, cells_x, blocks_y, cells_y).transpose(
        0, 2, 4, 1, 3, 5
    )
    arranged = arranged.reshape(channels, blocks_x * blocks_y * layers_z, cells_x * cells_y)
    return lax.all_to_all(arranged, ("dx", "dy"), split_axis=1, concat_axis=1, tiled=True)


def blocks_to_slabs(field, blocks_x, blocks_y, cells_x, cells_y):
    channels, depth, lanes = field.shape
    layers_z = depth // (blocks_x * blocks_y)
    moved = lax.all_to_all(field, ("dx", "dy"), split_axis=1, concat_axis=1, tiled=True)
    arranged = moved.reshape(channels, blocks_x, blocks_y, layers_z, cells_x, cells_y).transpose(
        0, 3, 1, 4, 2, 5
    )
    return arranged.reshape(channels, layers_z, blocks_x * cells_x, blocks_y * cells_y)


def along_z(field):
    zero = jnp.zeros_like(field[..., :1, :])
    above = jnp.concatenate([field[..., 1:, :], zero], axis=-2)
    below = jnp.concatenate([zero, field[..., :-1, :]], axis=-2)
    return above, below


def faces_x(field, cells_y):
    ahead = from_behind(field[..., :cells_y], "dx", -1)
    behind = from_behind(field[..., field.shape[-1] - cells_y :], "dx", 1)
    return ahead, behind


def along_x(field, cells_y, faces=None):
    ahead, behind = faces_x(field, cells_y) if faces is None else faces
    plus = jnp.concatenate([field[..., cells_y:], ahead], axis=-1)
    minus = jnp.concatenate([behind, field[..., :-cells_y]], axis=-1)
    return plus, minus


def lane_selectors(cells_x, cells_y):
    lanes = cells_x * cells_y
    lane = lax.broadcasted_iota(jnp.int32, (lanes, 2 * cells_x), 0)
    column = lax.broadcasted_iota(jnp.int32, (lanes, 2 * cells_x), 1)
    picks = jnp.where(column < cells_x, column * cells_y, (column - cells_x) * cells_y + cells_y - 1)
    select = lane == picks
    spread_pick = jnp.where(column < cells_x, column * cells_y + cells_y - 1, (column - cells_x) * cells_y)
    spread = (lane == spread_pick).T
    return select.astype(jnp.bfloat16), spread.astype(jnp.bfloat16)


def exact_pick(values, one_hot):
    high = lax.reduce_precision(values, exponent_bits=8, mantissa_bits=7)
    rest = values - high
    middle = lax.reduce_precision(rest, exponent_bits=8, mantissa_bits=7)
    low = rest - middle
    rows = values.shape[0]
    parts = jnp.concatenate([high, middle, low], axis=0).astype(jnp.bfloat16)
    picked = jnp.dot(parts, one_hot, preferred_element_type=jnp.float32)
    return (picked[:rows] + picked[rows : 2 * rows]) + picked[2 * rows :]


def faces_y(field, selectors):
    cells_x = selectors[0].shape[1] // 2
    both = exact_pick(field.reshape(-1, field.shape[-1]), selectors[0])
    ahead = from_behind(both[:, :cells_x], "dy", -1)
    behind = from_behind(both[:, cells_x:], "dy", 1)
    return ahead, behind


def along_y(field, selectors, cells_y, faces=None):
    shape = field.shape
    ahead, behind = faces_y(field, selectors) if faces is None else faces
    halo = exact_pick(jnp.concatenate([ahead, behind], axis=1), selectors[1]).reshape(shape)
    lane_y = lax.broadcasted_iota(jnp.int32, shape, len(shape) - 1) % cells_y
    plus = jnp.where(lane_y == cells_y - 1, halo, jnp.roll(field, -1, axis=-1))
    minus = jnp.where(lane_y == 0, halo, jnp.roll(field, 1, axis=-1))
    return plus, minus


def fluid_step(velocity, pressure, deposits, faces, selectors, cells_y):
    solids = deposits[0]
    voidage = 1.0 / (1.0 + solids)
    growth = (1.0 + solids) * (1.0 + solids)
    drag_rate = deposits[1] * growth
    drag_pull = deposits[2:5] * growth
    stacked = jnp.concatenate([velocity, pressure[None]], axis=0)
    z_plus, z_minus = along_z(stacked)
    x_plus, x_minus = along_x(stacked, cells_y, faces[0])
    y_plus, y_minus = along_y(stacked, selectors, cells_y, faces[1])
    beside_all = (z_plus + z_minus) + x_plus + x_minus + y_plus + y_minus
    predicted = (
        velocity + time_step * (viscosity * (beside_all[:3] - 6.0 * velocity) + drag_pull)
    ) / (1.0 + time_step * drag_rate)
    flux = voidage[None] * predicted
    fx_plus, fx_minus = along_x(flux[0], cells_y)
    fy_plus, fy_minus = along_y(flux[1], selectors, cells_y)
    fz_plus, fz_minus = along_z(flux[2])
    divergence = 0.5 * (fx_plus - fx_minus) + 0.5 * (fy_plus - fy_minus) + 0.5 * (fz_plus - fz_minus)
    pressure_new = (beside_all[3] - divergence / time_step) / 6.0
    px_plus, px_minus = along_x(pressure_new, cells_y)
    py_plus, py_minus = along_y(pressure_new, selectors, cells_y)
    pz_plus, pz_minus = along_z(pressure_new)
    gradient = jnp.stack(
        [0.5 * (px_plus - px_minus), 0.5 * (py_plus - py_minus), 0.5 * (pz_plus - pz_minus)], axis=0
    )
    return (predicted - time_step * gradient, pressure_new)


def shards(particles, leave_lists, leave_counts, slot_cells, velocity, pressure):
    blocks_x = lax.axis_size("dx")
    blocks_y = lax.axis_size("dy")
    records = particles[0, 0]
    leaver_lists = leave_lists[0, 0]
    leaver_counts = leave_counts[0, 0]
    cell_index = slot_cells[0, 0]
    capacity = leaver_lists.shape[1]
    holders = records.shape[1]
    cells_x = velocity.shape[2] // blocks_x
    cells_y = velocity.shape[3] // blocks_y
    lanes = cells_x * cells_y
    depth = velocity.shape[1] * blocks_x * blocks_y

    fields = slabs_to_blocks(
        jnp.concatenate([velocity, pressure[None]], axis=0), blocks_x, blocks_y
    )
    positions = jnp.arange(capacity, dtype=jnp.int32)
    validity = (positions[None, :] < leaver_counts[:, None]).astype(jnp.float32)
    flat_list = leaver_lists.reshape(-1)
    low_size = math.gcd(holders, 512)
    upper_size = holders // low_size
    listed = flat_list.shape[0]
    upper_of = flat_list // low_size
    lower_of = flat_list % low_size
    on_upper = lax.broadcasted_iota(jnp.int32, (upper_size, listed), 0) == upper_of[None, :]
    on_lower = lax.broadcasted_iota(jnp.int32, (low_size, listed), 0) == lower_of[None, :]
    valid_flat = validity.reshape(1, -1)
    departed = lax.dot_general(
        (on_upper.astype(jnp.float32) * valid_flat).astype(jnp.bfloat16),
        on_lower.astype(jnp.bfloat16),
        (((1,), (1,)), ((), ())),
        preferred_element_type=jnp.float32,
    ).reshape(holders)
    remaining = records * (1.0 - departed)[None, :]
    high = lax.reduce_precision(records, exponent_bits=8, mantissa_bits=7)
    rest = records - high
    middle = lax.reduce_precision(rest, exponent_bits=8, mantissa_bits=7)
    low = rest - middle
    rows = records.shape[0]
    parts = jnp.concatenate([high, middle, low], axis=0).astype(jnp.bfloat16)
    parts = parts.reshape(3 * rows * upper_size, low_size)
    by_lower = jnp.dot(parts, on_lower.astype(jnp.bfloat16), preferred_element_type=jnp.float32)
    by_lower = by_lower.reshape(3, rows, upper_size, listed)
    picked_parts = jnp.sum(by_lower * on_upper.astype(jnp.float32)[None, None], axis=2)
    picked_rows = (picked_parts[0] + picked_parts[1]) + picked_parts[2]
    outgoing = picked_rows.reshape(rows, 4, capacity) * validity[None]
    arrivals = migrate(outgoing)
    buffer = jnp.concatenate([remaining] + arrivals, axis=1)

    layer_of = cell_index // lanes
    lane_of = cell_index % lanes
    on_layer = (
        lax.broadcasted_iota(jnp.int32, (depth, cell_index.shape[0]), 0) == layer_of[None, :]
    ).astype(jnp.float32)
    on_lane = (
        lax.broadcasted_iota(jnp.int32, (cell_index.shape[0], lanes), 1) == lane_of[:, None]
    ).astype(jnp.bfloat16)

    selectors = lane_selectors(cells_x, cells_y)
    fields, buffer = lax.optimization_barrier((fields, buffer))
    flow = fields[:3]
    pressure_block = fields[3]
    stacked = jnp.concatenate([flow, pressure_block[None]], axis=0)
    faces = (faces_x(stacked, cells_y), faces_y(stacked, selectors))
    for coupling in range(COUPLINGS):
        deposits = deposit_block(buffer, on_layer, on_lane)
        faces, deposits = lax.optimization_barrier((faces, deposits))
        flow, pressure_block = fluid_step(flow, pressure_block, deposits, faces, selectors, cells_y)
        if coupling < COUPLINGS - 1:
            stacked = jnp.concatenate([flow, pressure_block[None]], axis=0)
            faces = (faces_x(stacked, cells_y), faces_y(stacked, selectors))
        picked = gather_block(
            jnp.concatenate([flow, deposits[:1]], axis=0), on_layer, on_lane
        )
        if coupling == COUPLINGS - 1:
            fields = blocks_to_slabs(
                jnp.concatenate([flow, pressure_block[None]], axis=0), blocks_x, blocks_y, cells_x, cells_y
            )
            fields, picked = lax.optimization_barrier((fields, picked))
        buffer = advance_block(buffer, picked[:3], picked[3])

    return (buffer[None, None], fields[:3], fields[3])


def solution(mesh):
    placed = (
        P("dx", "dy", None, None),
        P("dx", "dy", None, None),
        P("dx", "dy", None),
        P("dx", "dy", None),
        P(None, ("dx", "dy"), None, None),
        P(("dx", "dy"), None, None),
    )
    return jax.shard_map(
        shards,
        mesh=mesh,
        in_specs=placed,
        out_specs=(
            P("dx", "dy", None, None),
            P(None, ("dx", "dy"), None, None),
            P(("dx", "dy"), None, None),
        ),
        check_vma=False,
    )
```

```python
import math

import jax
import jax.numpy as jnp
from jax import lax
from jax.sharding import PartitionSpec as P

COUPLINGS = 2


time_step = 0.1
viscosity = 0.5
gravity = -1.0


def from_behind(value, axis, steps):
    count = lax.axis_size(axis)
    pairs = [(source, (source + steps) % count) for source in range(count)]
    return lax.ppermute(value, axis, pairs)


def migrate(outgoing):
    arrivals = []
    for offset in (1, -1):
        arrivals.append(from_behind(outgoing[:, (1 - offset) // 2], "dx", offset))
    for offset in (1, -1):
        arrivals.append(from_behind(outgoing[:, 2 + (1 - offset) // 2], "dy", offset))
    return arrivals


def split_bf16(values):
    high = lax.reduce_precision(values, exponent_bits=8, mantissa_bits=7)
    low = values - high
    return high.astype(jnp.bfloat16), low.astype(jnp.bfloat16)


def deposit_block(buffer, on_layer, on_lane):
    sources = jnp.concatenate([buffer[6:8], buffer[7][None] * buffer[0:3]], axis=0)
    layered = sources[:, None, :] * on_layer[None]
    high, low = split_bf16(layered)
    channels, layers, slots = layered.shape
    stacked = jnp.concatenate([high, low], axis=0).reshape(2 * channels * layers, slots)
    summed = jnp.dot(stacked, on_lane, preferred_element_type=jnp.float32)
    summed = summed.reshape(2, channels, layers, on_lane.shape[1])
    return summed[0] + summed[1]


def gather_block(fields, on_layer, on_lane):
    channels, layers, lanes = fields.shape
    high, low = split_bf16(fields)
    stacked = jnp.concatenate([high, low], axis=0).reshape(2 * channels * layers, lanes)
    picked = lax.dot_general(
        stacked, on_lane, (((1,), (1,)), ((), ())), preferred_element_type=jnp.float32
    )
    picked = picked.reshape(2, channels, layers, on_lane.shape[0])
    return jnp.sum((picked[0] + picked[1]) * on_layer[None], axis=1)


def advance_block(buffer, cell_flow, cell_solids):
    speeds = buffer[0:3]
    friction = buffer[7]
    mobility = buffer[8]
    cell_void = 1.0 / (1.0 + cell_solids)
    relaxation = time_step * friction * mobility / (cell_void * cell_void)
    live_mask = (buffer[6] > 0).astype(jnp.float32)
    gravity_push = jnp.zeros_like(speeds).at[2].set(time_step * gravity * live_mask)
    new_speeds = (speeds + relaxation * cell_flow + gravity_push) / (1.0 + relaxation)
    spins = buffer[3:6] / (1.0 + relaxation)
    places = buffer[9:12] + time_step * new_speeds
    return jnp.concatenate([new_speeds, spins, buffer[6:9], places, buffer[12:14]], axis=0)


def slabs_to_blocks(field, blocks_x, blocks_y):
    channels, layers_z, cells_nx, cells_ny = field.shape
    cells_x, cells_y = cells_nx // blocks_x, cells_ny // blocks_y
    arranged = field.reshape(channels, layers_z, blocks_x, cells_x, blocks_y, cells_y).transpose(
        0, 2, 4, 1, 3, 5
    )
    arranged = arranged.reshape(channels, blocks_x * blocks_y * layers_z, cells_x * cells_y)
    return lax.all_to_all(arranged, ("dx", "dy"), split_axis=1, concat_axis=1, tiled=True)


def blocks_to_slabs(field, blocks_x, blocks_y, cells_x, cells_y):
    channels, depth, lanes = field.shape
    layers_z = depth // (blocks_x * blocks_y)
    moved = lax.all_to_all(field, ("dx", "dy"), split_axis=1, concat_axis=1, tiled=True)
    arranged = moved.reshape(channels, blocks_x, blocks_y, layers_z, cells_x, cells_y).transpose(
        0, 3, 1, 4, 2, 5
    )
    return arranged.reshape(channels, layers_z, blocks_x * cells_x, blocks_y * cells_y)


def along_z(field):
    zero = jnp.zeros_like(field[..., :1, :])
    above = jnp.concatenate([field[..., 1:, :], zero], axis=-2)
    below = jnp.concatenate([zero, field[..., :-1, :]], axis=-2)
    return above, below


def faces_x(field, cells_y):
    ahead = from_behind(field[..., :cells_y], "dx", -1)
    behind = from_behind(field[..., field.shape[-1] - cells_y :], "dx", 1)
    return ahead, behind


def along_x(field, cells_y, faces=None):
    ahead, behind = faces_x(field, cells_y) if faces is None else faces
    plus = jnp.concatenate([field[..., cells_y:], ahead], axis=-1)
    minus = jnp.concatenate([behind, field[..., :-cells_y]], axis=-1)
    return plus, minus


def lane_selectors(cells_x, cells_y):
    lanes = cells_x * cells_y
    lane = lax.broadcasted_iota(jnp.int32, (lanes, 2 * cells_x), 0)
    column = lax.broadcasted_iota(jnp.int32, (lanes, 2 * cells_x), 1)
    picks = jnp.where(column < cells_x, column * cells_y, (column - cells_x) * cells_y + cells_y - 1)
    select = lane == picks
    spread_pick = jnp.where(column < cells_x, column * cells_y + cells_y - 1, (column - cells_x) * cells_y)
    spread = (lane == spread_pick).T
    return select.astype(jnp.bfloat16), spread.astype(jnp.bfloat16)


def exact_pick(values, one_hot):
    high = lax.reduce_precision(values, exponent_bits=8, mantissa_bits=7)
    rest = values - high
    middle = lax.reduce_precision(rest, exponent_bits=8, mantissa_bits=7)
    low = rest - middle
    rows = values.shape[0]
    parts = jnp.concatenate([high, middle, low], axis=0).astype(jnp.bfloat16)
    picked = jnp.dot(parts, one_hot, preferred_element_type=jnp.float32)
    return (picked[:rows] + picked[rows : 2 * rows]) + picked[2 * rows :]


def faces_y(field, selectors):
    cells_x = selectors[0].shape[1] // 2
    both = exact_pick(field.reshape(-1, field.shape[-1]), selectors[0])
    ahead = from_behind(both[:, :cells_x], "dy", -1)
    behind = from_behind(both[:, cells_x:], "dy", 1)
    return ahead, behind


def along_y(field, selectors, cells_y, faces=None):
    shape = field.shape
    ahead, behind = faces_y(field, selectors) if faces is None else faces
    halo = exact_pick(jnp.concatenate([ahead, behind], axis=1), selectors[1]).reshape(shape)
    lane_y = lax.broadcasted_iota(jnp.int32, shape, len(shape) - 1) % cells_y
    plus = jnp.where(lane_y == cells_y - 1, halo, jnp.roll(field, -1, axis=-1))
    minus = jnp.where(lane_y == 0, halo, jnp.roll(field, 1, axis=-1))
    return plus, minus


def fluid_step(velocity, pressure, deposits, faces, selectors, cells_y):
    solids = deposits[0]
    voidage = 1.0 / (1.0 + solids)
    growth = (1.0 + solids) * (1.0 + solids)
    drag_rate = deposits[1] * growth
    drag_pull = deposits[2:5] * growth
    stacked = jnp.concatenate([velocity, pressure[None]], axis=0)
    z_plus, z_minus = along_z(stacked)
    x_plus, x_minus = along_x(stacked, cells_y, faces[0])
    y_plus, y_minus = along_y(stacked, selectors, cells_y, faces[1])
    beside_all = (z_plus + z_minus) + x_plus + x_minus + y_plus + y_minus
    predicted = (
        velocity + time_step * (viscosity * (beside_all[:3] - 6.0 * velocity) + drag_pull)
    ) / (1.0 + time_step * drag_rate)
    flux = voidage[None] * predicted
    fx_plus, fx_minus = along_x(flux[0], cells_y)
    fy_plus, fy_minus = along_y(flux[1], selectors, cells_y)
    fz_plus, fz_minus = along_z(flux[2])
    divergence = 0.5 * (fx_plus - fx_minus) + 0.5 * (fy_plus - fy_minus) + 0.5 * (fz_plus - fz_minus)
    pressure_new = (beside_all[3] - divergence / time_step) / 6.0
    px_plus, px_minus = along_x(pressure_new, cells_y)
    py_plus, py_minus = along_y(pressure_new, selectors, cells_y)
    pz_plus, pz_minus = along_z(pressure_new)
    gradient = jnp.stack(
        [0.5 * (px_plus - px_minus), 0.5 * (py_plus - py_minus), 0.5 * (pz_plus - pz_minus)], axis=0
    )
    return (predicted - time_step * gradient, pressure_new)


def shards(particles, leave_lists, leave_counts, slot_cells, velocity, pressure):
    blocks_x = lax.axis_size("dx")
    blocks_y = lax.axis_size("dy")
    records = particles[0, 0]
    leaver_lists = leave_lists[0, 0]
    leaver_counts = leave_counts[0, 0]
    cell_index = slot_cells[0, 0]
    capacity = leaver_lists.shape[1]
    holders = records.shape[1]
    cells_x = velocity.shape[2] // blocks_x
    cells_y = velocity.shape[3] // blocks_y
    lanes = cells_x * cells_y
    depth = velocity.shape[1] * blocks_x * blocks_y

    fields = slabs_to_blocks(
        jnp.concatenate([velocity, pressure[None]], axis=0), blocks_x, blocks_y
    )
    positions = jnp.arange(capacity, dtype=jnp.int32)
    validity = (positions[None, :] < leaver_counts[:, None]).astype(jnp.float32)
    flat_list = leaver_lists.reshape(-1)
    low_size = math.gcd(holders, 512)
    upper_size = holders // low_size
    listed = flat_list.shape[0]
    upper_of = flat_list // low_size
    lower_of = flat_list % low_size
    on_upper = lax.broadcasted_iota(jnp.int32, (upper_size, listed), 0) == upper_of[None, :]
    on_lower = lax.broadcasted_iota(jnp.int32, (low_size, listed), 0) == lower_of[None, :]
    valid_flat = validity.reshape(1, -1)
    departed = lax.dot_general(
        (on_upper.astype(jnp.float32) * valid_flat).astype(jnp.bfloat16),
        on_lower.astype(jnp.bfloat16),
        (((1,), (1,)), ((), ())),
        preferred_element_type=jnp.float32,
    ).reshape(holders)
    remaining = records * (1.0 - departed)[None, :]
    high = lax.reduce_precision(records, exponent_bits=8, mantissa_bits=7)
    rest = records - high
    middle = lax.reduce_precision(rest, exponent_bits=8, mantissa_bits=7)
    low = rest - middle
    rows = records.shape[0]
    parts = jnp.concatenate([high, middle, low], axis=0).astype(jnp.bfloat16)
    parts = parts.reshape(3 * rows * upper_size, low_size)
    by_lower = jnp.dot(parts, on_lower.astype(jnp.bfloat16), preferred_element_type=jnp.float32)
    by_lower = by_lower.reshape(3, rows, upper_size, listed)
    picked_parts = jnp.sum(by_lower * on_upper.astype(jnp.float32)[None, None], axis=2)
    picked_rows = (picked_parts[0] + picked_parts[1]) + picked_parts[2]
    outgoing = picked_rows.reshape(rows, 4, capacity) * validity[None]
    arrivals = migrate(outgoing)
    buffer = jnp.concatenate([remaining] + arrivals, axis=1)

    layer_of = cell_index // lanes
    lane_of = cell_index % lanes
    on_layer = (
        lax.broadcasted_iota(jnp.int32, (depth, cell_index.shape[0]), 0) == layer_of[None, :]
    ).astype(jnp.float32)
    on_lane = (
        lax.broadcasted_iota(jnp.int32, (cell_index.shape[0], lanes), 1) == lane_of[:, None]
    ).astype(jnp.bfloat16)

    selectors = lane_selectors(cells_x, cells_y)
    fields, buffer = lax.optimization_barrier((fields, buffer))
    flow = fields[:3]
    pressure_block = fields[3]
    stacked = jnp.concatenate([flow, pressure_block[None]], axis=0)
    faces = (faces_x(stacked, cells_y), faces_y(stacked, selectors))
    for coupling in range(COUPLINGS):
        deposits = deposit_block(buffer, on_layer, on_lane)
        faces, deposits = lax.optimization_barrier((faces, deposits))
        flow, pressure_block = fluid_step(flow, pressure_block, deposits, faces, selectors, cells_y)
        if coupling < COUPLINGS - 1:
            stacked = jnp.concatenate([flow, pressure_block[None]], axis=0)
            faces = (faces_x(stacked, cells_y), faces_y(stacked, selectors))
        if coupling == COUPLINGS - 1:
            pressure_out = blocks_to_slabs(pressure_block[None], blocks_x, blocks_y, cells_x, cells_y)
            pressure_out, flow = lax.optimization_barrier((pressure_out, flow))
        picked = gather_block(
            jnp.concatenate([flow, deposits[:1]], axis=0), on_layer, on_lane
        )
        if coupling == COUPLINGS - 1:
            velocity_out = blocks_to_slabs(flow, blocks_x, blocks_y, cells_x, cells_y)
            velocity_out, picked = lax.optimization_barrier((velocity_out, picked))
        buffer = advance_block(buffer, picked[:3], picked[3])

    return (buffer[None, None], velocity_out, pressure_out[0])


def solution(mesh):
    placed = (
        P("dx", "dy", None, None),
        P("dx", "dy", None, None),
        P("dx", "dy", None),
        P("dx", "dy", None),
        P(None, ("dx", "dy"), None, None),
        P(("dx", "dy"), None, None),
    )
    return jax.shard_map(
        shards,
        mesh=mesh,
        in_specs=placed,
        out_specs=(
            P("dx", "dy", None, None),
            P(None, ("dx", "dy"), None, None),
            P(("dx", "dy"), None, None),
        ),
        check_vma=False,
    )
```

```python
import math

import jax
import jax.numpy as jnp
from jax import lax
from jax.sharding import PartitionSpec as P

COUPLINGS = 2


time_step = 0.1
viscosity = 0.5
gravity = -1.0


def from_behind(value, axis, steps):
    count = lax.axis_size(axis)
    pairs = [(source, (source + steps) % count) for source in range(count)]
    return lax.ppermute(value, axis, pairs)


def migrate(outgoing):
    arrivals = []
    for offset in (1, -1):
        arrivals.append(from_behind(outgoing[:, (1 - offset) // 2], "dx", offset))
    for offset in (1, -1):
        arrivals.append(from_behind(outgoing[:, 2 + (1 - offset) // 2], "dy", offset))
    return arrivals


def split_bf16(values):
    high = lax.reduce_precision(values, exponent_bits=8, mantissa_bits=7)
    low = values - high
    return high.astype(jnp.bfloat16), low.astype(jnp.bfloat16)


def deposit_block(buffer, on_layer, on_lane):
    sources = jnp.concatenate([buffer[6:8], buffer[7][None] * buffer[0:3]], axis=0)
    layered = sources[:, None, :] * on_layer[None]
    high, low = split_bf16(layered)
    channels, layers, slots = layered.shape
    stacked = jnp.concatenate([high, low], axis=0).reshape(2 * channels * layers, slots)
    summed = jnp.dot(stacked, on_lane, preferred_element_type=jnp.float32)
    summed = summed.reshape(2, channels, layers, on_lane.shape[1])
    return summed[0] + summed[1]


def gather_block(fields, on_layer, on_lane):
    channels, layers, lanes = fields.shape
    high, low = split_bf16(fields)
    stacked = jnp.concatenate([high, low], axis=0).reshape(2 * channels * layers, lanes)
    picked = lax.dot_general(
        stacked, on_lane, (((1,), (1,)), ((), ())), preferred_element_type=jnp.float32
    )
    picked = picked.reshape(2, channels, layers, on_lane.shape[0])
    return jnp.sum((picked[0] + picked[1]) * on_layer[None], axis=1)


def advance_block(buffer, cell_flow, cell_solids):
    speeds = buffer[0:3]
    friction = buffer[7]
    mobility = buffer[8]
    cell_void = 1.0 / (1.0 + cell_solids)
    relaxation = time_step * friction * mobility / (cell_void * cell_void)
    live_mask = (buffer[6] > 0).astype(jnp.float32)
    gravity_push = jnp.zeros_like(speeds).at[2].set(time_step * gravity * live_mask)
    new_speeds = (speeds + relaxation * cell_flow + gravity_push) / (1.0 + relaxation)
    spins = buffer[3:6] / (1.0 + relaxation)
    places = buffer[9:12] + time_step * new_speeds
    return jnp.concatenate([new_speeds, spins, buffer[6:9], places, buffer[12:14]], axis=0)


def slabs_to_blocks(field, blocks_x, blocks_y):
    channels, layers_z, cells_nx, cells_ny = field.shape
    cells_x, cells_y = cells_nx // blocks_x, cells_ny // blocks_y
    arranged = field.reshape(channels, layers_z, blocks_x, cells_x, blocks_y, cells_y).transpose(
        0, 2, 4, 1, 3, 5
    )
    arranged = arranged.reshape(channels, blocks_x * blocks_y * layers_z, cells_x * cells_y)
    return lax.all_to_all(arranged, ("dx", "dy"), split_axis=1, concat_axis=1, tiled=True)


def blocks_to_slabs(field, blocks_x, blocks_y, cells_x, cells_y):
    channels, depth, lanes = field.shape
    layers_z = depth // (blocks_x * blocks_y)
    moved = lax.all_to_all(field, ("dx", "dy"), split_axis=1, concat_axis=1, tiled=True)
    arranged = moved.reshape(channels, blocks_x, blocks_y, layers_z, cells_x, cells_y).transpose(
        0, 3, 1, 4, 2, 5
    )
    return arranged.reshape(channels, layers_z, blocks_x * cells_x, blocks_y * cells_y)


def along_z(field):
    zero = jnp.zeros_like(field[..., :1, :])
    above = jnp.concatenate([field[..., 1:, :], zero], axis=-2)
    below = jnp.concatenate([zero, field[..., :-1, :]], axis=-2)
    return above, below


def neighbour_faces(low_face, high_face, axis):
    count = lax.axis_size(axis)
    gathered = lax.all_gather(jnp.stack([low_face, high_face]), axis)
    here = lax.axis_index(axis)
    ahead = lax.dynamic_index_in_dim(gathered, (here + 1) % count, 0, keepdims=False)[0]
    behind = lax.dynamic_index_in_dim(gathered, (here + count - 1) % count, 0, keepdims=False)[1]
    return ahead, behind


def faces_x(field, cells_y):
    return neighbour_faces(field[..., :cells_y], field[..., field.shape[-1] - cells_y :], "dx")


def along_x(field, cells_y, faces=None):
    ahead, behind = faces_x(field, cells_y) if faces is None else faces
    plus = jnp.concatenate([field[..., cells_y:], ahead], axis=-1)
    minus = jnp.concatenate([behind, field[..., :-cells_y]], axis=-1)
    return plus, minus


def lane_selectors(cells_x, cells_y):
    lanes = cells_x * cells_y
    lane = lax.broadcasted_iota(jnp.int32, (lanes, 2 * cells_x), 0)
    column = lax.broadcasted_iota(jnp.int32, (lanes, 2 * cells_x), 1)
    picks = jnp.where(column < cells_x, column * cells_y, (column - cells_x) * cells_y + cells_y - 1)
    select = lane == picks
    spread_pick = jnp.where(column < cells_x, column * cells_y + cells_y - 1, (column - cells_x) * cells_y)
    spread = (lane == spread_pick).T
    return select.astype(jnp.bfloat16), spread.astype(jnp.bfloat16)


def exact_pick(values, one_hot):
    high = lax.reduce_precision(values, exponent_bits=8, mantissa_bits=7)
    rest = values - high
    middle = lax.reduce_precision(rest, exponent_bits=8, mantissa_bits=7)
    low = rest - middle
    rows = values.shape[0]
    parts = jnp.concatenate([high, middle, low], axis=0).astype(jnp.bfloat16)
    picked = jnp.dot(parts, one_hot, preferred_element_type=jnp.float32)
    return (picked[:rows] + picked[rows : 2 * rows]) + picked[2 * rows :]


def faces_y(field, selectors):
    cells_x = selectors[0].shape[1] // 2
    both = exact_pick(field.reshape(-1, field.shape[-1]), selectors[0])
    return neighbour_faces(both[:, :cells_x], both[:, cells_x:], "dy")


def along_y(field, selectors, cells_y, faces=None):
    shape = field.shape
    ahead, behind = faces_y(field, selectors) if faces is None else faces
    halo = exact_pick(jnp.concatenate([ahead, behind], axis=1), selectors[1]).reshape(shape)
    lane_y = lax.broadcasted_iota(jnp.int32, shape, len(shape) - 1) % cells_y
    plus = jnp.where(lane_y == cells_y - 1, halo, jnp.roll(field, -1, axis=-1))
    minus = jnp.where(lane_y == 0, halo, jnp.roll(field, 1, axis=-1))
    return plus, minus


def fluid_step(velocity, pressure, deposits, faces, selectors, cells_y):
    solids = deposits[0]
    voidage = 1.0 / (1.0 + solids)
    growth = (1.0 + solids) * (1.0 + solids)
    drag_rate = deposits[1] * growth
    drag_pull = deposits[2:5] * growth
    stacked = jnp.concatenate([velocity, pressure[None]], axis=0)
    z_plus, z_minus = along_z(stacked)
    x_plus, x_minus = along_x(stacked, cells_y, faces[0])
    y_plus, y_minus = along_y(stacked, selectors, cells_y, faces[1])
    beside_all = (z_plus + z_minus) + x_plus + x_minus + y_plus + y_minus
    predicted = (
        velocity + time_step * (viscosity * (beside_all[:3] - 6.0 * velocity) + drag_pull)
    ) / (1.0 + time_step * drag_rate)
    flux = voidage[None] * predicted
    fx_plus, fx_minus = along_x(flux[0], cells_y)
    fy_plus, fy_minus = along_y(flux[1], selectors, cells_y)
    fz_plus, fz_minus = along_z(flux[2])
    divergence = 0.5 * (fx_plus - fx_minus) + 0.5 * (fy_plus - fy_minus) + 0.5 * (fz_plus - fz_minus)
    pressure_new = (beside_all[3] - divergence / time_step) / 6.0
    px_plus, px_minus = along_x(pressure_new, cells_y)
    py_plus, py_minus = along_y(pressure_new, selectors, cells_y)
    pz_plus, pz_minus = along_z(pressure_new)
    gradient = jnp.stack(
        [0.5 * (px_plus - px_minus), 0.5 * (py_plus - py_minus), 0.5 * (pz_plus - pz_minus)], axis=0
    )
    return (predicted - time_step * gradient, pressure_new)


def shards(particles, leave_lists, leave_counts, slot_cells, velocity, pressure):
    blocks_x = lax.axis_size("dx")
    blocks_y = lax.axis_size("dy")
    records = particles[0, 0]
    leaver_lists = leave_lists[0, 0]
    leaver_counts = leave_counts[0, 0]
    cell_index = slot_cells[0, 0]
    capacity = leaver_lists.shape[1]
    holders = records.shape[1]
    cells_x = velocity.shape[2] // blocks_x
    cells_y = velocity.shape[3] // blocks_y
    lanes = cells_x * cells_y
    depth = velocity.shape[1] * blocks_x * blocks_y

    fields = slabs_to_blocks(
        jnp.concatenate([velocity, pressure[None]], axis=0), blocks_x, blocks_y
    )
    positions = jnp.arange(capacity, dtype=jnp.int32)
    validity = (positions[None, :] < leaver_counts[:, None]).astype(jnp.float32)
    flat_list = leaver_lists.reshape(-1)
    low_size = math.gcd(holders, 512)
    upper_size = holders // low_size
    listed = flat_list.shape[0]
    upper_of = flat_list // low_size
    lower_of = flat_list % low_size
    on_upper = lax.broadcasted_iota(jnp.int32, (upper_size, listed), 0) == upper_of[None, :]
    on_lower = lax.broadcasted_iota(jnp.int32, (low_size, listed), 0) == lower_of[None, :]
    valid_flat = validity.reshape(1, -1)
    departed = lax.dot_general(
        (on_upper.astype(jnp.float32) * valid_flat).astype(jnp.bfloat16),
        on_lower.astype(jnp.bfloat16),
        (((1,), (1,)), ((), ())),
        preferred_element_type=jnp.float32,
    ).reshape(holders)
    remaining = records * (1.0 - departed)[None, :]
    high = lax.reduce_precision(records, exponent_bits=8, mantissa_bits=7)
    rest = records - high
    middle = lax.reduce_precision(rest, exponent_bits=8, mantissa_bits=7)
    low = rest - middle
    rows = records.shape[0]
    parts = jnp.concatenate([high, middle, low], axis=0).astype(jnp.bfloat16)
    parts = parts.reshape(3 * rows * upper_size, low_size)
    by_lower = jnp.dot(parts, on_lower.astype(jnp.bfloat16), preferred_element_type=jnp.float32)
    by_lower = by_lower.reshape(3, rows, upper_size, listed)
    picked_parts = jnp.sum(by_lower * on_upper.astype(jnp.float32)[None, None], axis=2)
    picked_rows = (picked_parts[0] + picked_parts[1]) + picked_parts[2]
    outgoing = picked_rows.reshape(rows, 4, capacity) * validity[None]
    arrivals = migrate(outgoing)
    buffer = jnp.concatenate([remaining] + arrivals, axis=1)

    layer_of = cell_index // lanes
    lane_of = cell_index % lanes
    on_layer = (
        lax.broadcasted_iota(jnp.int32, (depth, cell_index.shape[0]), 0) == layer_of[None, :]
    ).astype(jnp.float32)
    on_lane = (
        lax.broadcasted_iota(jnp.int32, (cell_index.shape[0], lanes), 1) == lane_of[:, None]
    ).astype(jnp.bfloat16)

    selectors = lane_selectors(cells_x, cells_y)
    fields, buffer = lax.optimization_barrier((fields, buffer))
    flow = fields[:3]
    pressure_block = fields[3]
    stacked = jnp.concatenate([flow, pressure_block[None]], axis=0)
    faces = (faces_x(stacked, cells_y), faces_y(stacked, selectors))
    for coupling in range(COUPLINGS):
        deposits = deposit_block(buffer, on_layer, on_lane)
        faces, deposits = lax.optimization_barrier((faces, deposits))
        flow, pressure_block = fluid_step(flow, pressure_block, deposits, faces, selectors, cells_y)
        if coupling < COUPLINGS - 1:
            stacked = jnp.concatenate([flow, pressure_block[None]], axis=0)
            faces = (faces_x(stacked, cells_y), faces_y(stacked, selectors))
        picked = gather_block(
            jnp.concatenate([flow, deposits[:1]], axis=0), on_layer, on_lane
        )
        if coupling == COUPLINGS - 1:
            fields = blocks_to_slabs(
                jnp.concatenate([flow, pressure_block[None]], axis=0), blocks_x, blocks_y, cells_x, cells_y
            )
            fields, picked = lax.optimization_barrier((fields, picked))
        buffer = advance_block(buffer, picked[:3], picked[3])

    return (buffer[None, None], fields[:3], fields[3])


def solution(mesh):
    placed = (
        P("dx", "dy", None, None),
        P("dx", "dy", None, None),
        P("dx", "dy", None),
        P("dx", "dy", None),
        P(None, ("dx", "dy"), None, None),
        P(("dx", "dy"), None, None),
    )
    return jax.shard_map(
        shards,
        mesh=mesh,
        in_specs=placed,
        out_specs=(
            P("dx", "dy", None, None),
            P(None, ("dx", "dy"), None, None),
            P(("dx", "dy"), None, None),
        ),
        check_vma=False,
    )
```

```python
import math

import jax
import jax.numpy as jnp
from jax import lax
from jax.sharding import PartitionSpec as P

COUPLINGS = 2


time_step = 0.1
viscosity = 0.5
gravity = -1.0


def from_behind(value, axis, steps):
    count = lax.axis_size(axis)
    pairs = [(source, (source + steps) % count) for source in range(count)]
    return lax.ppermute(value, axis, pairs)


def migrate(outgoing):
    arrivals = []
    for offset in (1, -1):
        arrivals.append(from_behind(outgoing[:, (1 - offset) // 2], "dx", offset))
    for offset in (1, -1):
        arrivals.append(from_behind(outgoing[:, 2 + (1 - offset) // 2], "dy", offset))
    return arrivals


def split_bf16(values):
    high = lax.reduce_precision(values, exponent_bits=8, mantissa_bits=7)
    low = values - high
    return high.astype(jnp.bfloat16), low.astype(jnp.bfloat16)


def deposit_block(buffer, on_layer, on_lane):
    sources = jnp.concatenate([buffer[6:8], buffer[7][None] * buffer[0:3]], axis=0)
    layered = sources[:, None, :] * on_layer[None]
    high, low = split_bf16(layered)
    channels, layers, slots = layered.shape
    stacked = jnp.concatenate([high, low], axis=0).reshape(2 * channels * layers, slots)
    summed = jnp.dot(stacked, on_lane, preferred_element_type=jnp.float32)
    summed = summed.reshape(2, channels, layers, on_lane.shape[1])
    return summed[0] + summed[1]


def gather_block(fields, on_layer, on_lane):
    channels, layers, lanes = fields.shape
    high, low = split_bf16(fields)
    stacked = jnp.concatenate([high, low], axis=0).reshape(2 * channels * layers, lanes)
    picked = jnp.dot(stacked, on_lane, preferred_element_type=jnp.float32)
    picked = picked.reshape(2, channels, layers, on_lane.shape[1])
    return jnp.sum((picked[0] + picked[1]) * on_layer[None], axis=1)


def advance_block(buffer, cell_flow, cell_solids):
    speeds = buffer[0:3]
    friction = buffer[7]
    mobility = buffer[8]
    cell_void = 1.0 / (1.0 + cell_solids)
    relaxation = time_step * friction * mobility / (cell_void * cell_void)
    live_mask = (buffer[6] > 0).astype(jnp.float32)
    gravity_push = jnp.zeros_like(speeds).at[2].set(time_step * gravity * live_mask)
    new_speeds = (speeds + relaxation * cell_flow + gravity_push) / (1.0 + relaxation)
    spins = buffer[3:6] / (1.0 + relaxation)
    places = buffer[9:12] + time_step * new_speeds
    return jnp.concatenate([new_speeds, spins, buffer[6:9], places, buffer[12:14]], axis=0)


def slabs_to_blocks(field, blocks_x, blocks_y):
    channels, layers_z, cells_nx, cells_ny = field.shape
    cells_x, cells_y = cells_nx // blocks_x, cells_ny // blocks_y
    arranged = field.reshape(channels, layers_z, blocks_x, cells_x, blocks_y, cells_y).transpose(
        0, 2, 4, 1, 3, 5
    )
    arranged = arranged.reshape(channels, blocks_x * blocks_y * layers_z, cells_x * cells_y)
    return lax.all_to_all(arranged, ("dx", "dy"), split_axis=1, concat_axis=1, tiled=True)


def blocks_to_slabs(field, blocks_x, blocks_y, cells_x, cells_y):
    channels, depth, lanes = field.shape
    layers_z = depth // (blocks_x * blocks_y)
    return lax.all_to_all(field, ("dx", "dy"), split_axis=1, concat_axis=1, tiled=True)


def arrange_slabs(moved, blocks_x, blocks_y, cells_x, cells_y):
    channels, depth, lanes = moved.shape
    layers_z = depth // (blocks_x * blocks_y)
    arranged = moved.reshape(channels, blocks_x, blocks_y, layers_z, cells_x, cells_y).transpose(
        0, 3, 1, 4, 2, 5
    )
    return arranged.reshape(channels, layers_z, blocks_x * cells_x, blocks_y * cells_y)


def along_z(field):
    zero = jnp.zeros_like(field[..., :1, :])
    above = jnp.concatenate([field[..., 1:, :], zero], axis=-2)
    below = jnp.concatenate([zero, field[..., :-1, :]], axis=-2)
    return above, below


def faces_x(field, cells_y):
    ahead = from_behind(field[..., :cells_y], "dx", -1)
    behind = from_behind(field[..., field.shape[-1] - cells_y :], "dx", 1)
    return ahead, behind


def along_x(field, cells_y, faces=None):
    ahead, behind = faces_x(field, cells_y) if faces is None else faces
    plus = jnp.concatenate([field[..., cells_y:], ahead], axis=-1)
    minus = jnp.concatenate([behind, field[..., :-cells_y]], axis=-1)
    return plus, minus


def lane_selectors(cells_x, cells_y):
    lanes = cells_x * cells_y
    lane = lax.broadcasted_iota(jnp.int32, (lanes, 2 * cells_x), 0)
    column = lax.broadcasted_iota(jnp.int32, (lanes, 2 * cells_x), 1)
    picks = jnp.where(column < cells_x, column * cells_y, (column - cells_x) * cells_y + cells_y - 1)
    select = lane == picks
    spread_pick = jnp.where(column < cells_x, column * cells_y + cells_y - 1, (column - cells_x) * cells_y)
    spread = (lane == spread_pick).T
    return select.astype(jnp.bfloat16), spread.astype(jnp.bfloat16)


def exact_pick(values, one_hot):
    high = lax.reduce_precision(values, exponent_bits=8, mantissa_bits=7)
    rest = values - high
    middle = lax.reduce_precision(rest, exponent_bits=8, mantissa_bits=7)
    low = rest - middle
    rows = values.shape[0]
    parts = jnp.concatenate([high, middle, low], axis=0).astype(jnp.bfloat16)
    picked = jnp.dot(parts, one_hot, preferred_element_type=jnp.float32)
    return (picked[:rows] + picked[rows : 2 * rows]) + picked[2 * rows :]


def faces_y(field, selectors):
    cells_x = selectors[0].shape[1] // 2
    both = exact_pick(field.reshape(-1, field.shape[-1]), selectors[0])
    ahead = from_behind(both[:, :cells_x], "dy", -1)
    behind = from_behind(both[:, cells_x:], "dy", 1)
    return ahead, behind


def along_y(field, selectors, cells_y, faces=None):
    shape = field.shape
    ahead, behind = faces_y(field, selectors) if faces is None else faces
    halo = exact_pick(jnp.concatenate([ahead, behind], axis=1), selectors[1]).reshape(shape)
    lane_y = lax.broadcasted_iota(jnp.int32, shape, len(shape) - 1) % cells_y
    plus = jnp.where(lane_y == cells_y - 1, halo, jnp.roll(field, -1, axis=-1))
    minus = jnp.where(lane_y == 0, halo, jnp.roll(field, 1, axis=-1))
    return plus, minus


def fluid_step(velocity, pressure, deposits, faces, selectors, cells_y):
    solids = deposits[0]
    voidage = 1.0 / (1.0 + solids)
    growth = (1.0 + solids) * (1.0 + solids)
    drag_rate = deposits[1] * growth
    drag_pull = deposits[2:5] * growth
    stacked = jnp.concatenate([velocity, pressure[None]], axis=0)
    z_plus, z_minus = along_z(stacked)
    x_plus, x_minus = along_x(stacked, cells_y, faces[0])
    y_plus, y_minus = along_y(stacked, selectors, cells_y, faces[1])
    beside_all = (z_plus + z_minus) + x_plus + x_minus + y_plus + y_minus
    predicted = (
        velocity + time_step * (viscosity * (beside_all[:3] - 6.0 * velocity) + drag_pull)
    ) / (1.0 + time_step * drag_rate)
    flux = voidage[None] * predicted
    fx_plus, fx_minus = along_x(flux[0], cells_y)
    fy_plus, fy_minus = along_y(flux[1], selectors, cells_y)
    fz_plus, fz_minus = along_z(flux[2])
    divergence = 0.5 * (fx_plus - fx_minus) + 0.5 * (fy_plus - fy_minus) + 0.5 * (fz_plus - fz_minus)
    pressure_new = (beside_all[3] - divergence / time_step) / 6.0
    px_plus, px_minus = along_x(pressure_new, cells_y)
    py_plus, py_minus = along_y(pressure_new, selectors, cells_y)
    pz_plus, pz_minus = along_z(pressure_new)
    gradient = jnp.stack(
        [0.5 * (px_plus - px_minus), 0.5 * (py_plus - py_minus), 0.5 * (pz_plus - pz_minus)], axis=0
    )
    return (predicted - time_step * gradient, pressure_new)


def shards(particles, leave_lists, leave_counts, slot_cells, velocity, pressure):
    blocks_x = lax.axis_size("dx")
    blocks_y = lax.axis_size("dy")
    records = particles[0, 0]
    leaver_lists = leave_lists[0, 0]
    leaver_counts = leave_counts[0, 0]
    cell_index = slot_cells[0, 0]
    capacity = leaver_lists.shape[1]
    holders = records.shape[1]
    cells_x = velocity.shape[2] // blocks_x
    cells_y = velocity.shape[3] // blocks_y
    lanes = cells_x * cells_y
    depth = velocity.shape[1] * blocks_x * blocks_y

    fields = slabs_to_blocks(
        jnp.concatenate([velocity, pressure[None]], axis=0), blocks_x, blocks_y
    )
    positions = jnp.arange(capacity, dtype=jnp.int32)
    validity = (positions[None, :] < leaver_counts[:, None]).astype(jnp.float32)
    flat_list = leaver_lists.reshape(-1)
    low_size = math.gcd(holders, 512)
    upper_size = holders // low_size
    listed = flat_list.shape[0]
    upper_of = flat_list // low_size
    lower_of = flat_list % low_size
    on_upper = lax.broadcasted_iota(jnp.int32, (upper_size, listed), 0) == upper_of[None, :]
    on_lower = lax.broadcasted_iota(jnp.int32, (low_size, listed), 0) == lower_of[None, :]
    valid_flat = validity.reshape(1, -1)
    departed = lax.dot_general(
        (on_upper.astype(jnp.float32) * valid_flat).astype(jnp.bfloat16),
        on_lower.astype(jnp.bfloat16),
        (((1,), (1,)), ((), ())),
        preferred_element_type=jnp.float32,
    ).reshape(holders)
    remaining = records * (1.0 - departed)[None, :]
    high = lax.reduce_precision(records, exponent_bits=8, mantissa_bits=7)
    rest = records - high
    middle = lax.reduce_precision(rest, exponent_bits=8, mantissa_bits=7)
    low = rest - middle
    rows = records.shape[0]
    parts = jnp.concatenate([high, middle, low], axis=0).astype(jnp.bfloat16)
    parts = parts.reshape(3 * rows * upper_size, low_size)
    by_lower = jnp.dot(parts, on_lower.astype(jnp.bfloat16), preferred_element_type=jnp.float32)
    by_lower = by_lower.reshape(3, rows, upper_size, listed)
    picked_parts = jnp.sum(by_lower * on_upper.astype(jnp.float32)[None, None], axis=2)
    picked_rows = (picked_parts[0] + picked_parts[1]) + picked_parts[2]
    outgoing = picked_rows.reshape(rows, 4, capacity) * validity[None]
    arrivals = migrate(outgoing)
    buffer = jnp.concatenate([remaining] + arrivals, axis=1)

    layer_of = cell_index // lanes
    lane_of = cell_index % lanes
    on_layer = (
        lax.broadcasted_iota(jnp.int32, (depth, cell_index.shape[0]), 0) == layer_of[None, :]
    ).astype(jnp.float32)
    on_lane = (
        lax.broadcasted_iota(jnp.int32, (cell_index.shape[0], lanes), 1) == lane_of[:, None]
    ).astype(jnp.bfloat16)
    lane_on = (
        lax.broadcasted_iota(jnp.int32, (lanes, cell_index.shape[0]), 0) == lane_of[None, :]
    ).astype(jnp.bfloat16)

    selectors = lane_selectors(cells_x, cells_y)
    fields, buffer = lax.optimization_barrier((fields, buffer))
    flow = fields[:3]
    pressure_block = fields[3]
    stacked = jnp.concatenate([flow, pressure_block[None]], axis=0)
    faces = (faces_x(stacked, cells_y), faces_y(stacked, selectors))
    for coupling in range(COUPLINGS):
        deposits = deposit_block(buffer, on_layer, on_lane)
        faces, deposits = lax.optimization_barrier((faces, deposits))
        flow, pressure_block = fluid_step(flow, pressure_block, deposits, faces, selectors, cells_y)
        picked = gather_block(
            jnp.concatenate([flow, deposits[:1]], axis=0), on_layer, lane_on
        )
        stacked = jnp.concatenate([flow, pressure_block[None]], axis=0)
        if coupling < COUPLINGS - 1:
            stacked, picked = lax.optimization_barrier((stacked, picked))
            faces = (faces_x(stacked, cells_y), faces_y(stacked, selectors))
        else:
            moved = blocks_to_slabs(stacked, blocks_x, blocks_y, cells_x, cells_y)
        buffer = advance_block(buffer, picked[:3], picked[3])

    moved, particles_out = lax.optimization_barrier((moved, buffer[None, None]))
    velocity_out = arrange_slabs(moved[:3], blocks_x, blocks_y, cells_x, cells_y)
    pressure_out = arrange_slabs(moved[3:], blocks_x, blocks_y, cells_x, cells_y)
    return (particles_out, velocity_out, pressure_out[0])


def solution(mesh):
    placed = (
        P("dx", "dy", None, None),
        P("dx", "dy", None, None),
        P("dx", "dy", None),
        P("dx", "dy", None),
        P(None, ("dx", "dy"), None, None),
        P(("dx", "dy"), None, None),
    )
    return jax.shard_map(
        shards,
        mesh=mesh,
        in_specs=placed,
        out_specs=(
            P("dx", "dy", None, None),
            P(None, ("dx", "dy"), None, None),
            P(("dx", "dy"), None, None),
        ),
        check_vma=False,
    )
```

```python
import math

import jax
import jax.numpy as jnp
from jax import lax
from jax.sharding import PartitionSpec as P

COUPLINGS = 2


time_step = 0.1
viscosity = 0.5
gravity = -1.0


def from_behind(value, axis, steps):
    count = lax.axis_size(axis)
    pairs = [(source, (source + steps) % count) for source in range(count)]
    return lax.ppermute(value, axis, pairs)


def migrate(outgoing):
    arrivals = []
    for offset in (1, -1):
        arrivals.append(from_behind(outgoing[:, (1 - offset) // 2], "dx", offset))
    for offset in (1, -1):
        arrivals.append(from_behind(outgoing[:, 2 + (1 - offset) // 2], "dy", offset))
    return arrivals


def split_bf16(values):
    high = lax.reduce_precision(values, exponent_bits=8, mantissa_bits=7)
    low = values - high
    return high.astype(jnp.bfloat16), low.astype(jnp.bfloat16)


def deposit_block(buffer, on_layer, on_lane):
    sources = jnp.concatenate([buffer[6:8], buffer[7][None] * buffer[0:3]], axis=0)
    layered = sources[:, None, :] * on_layer[None]
    high, low = split_bf16(layered)
    channels, layers, slots = layered.shape
    stacked = jnp.concatenate([high, low], axis=0).reshape(2 * channels * layers, slots)
    summed = jnp.dot(stacked, on_lane, preferred_element_type=jnp.float32)
    summed = summed.reshape(2, channels, layers, on_lane.shape[1])
    return summed[0] + summed[1]


def gather_block(fields, on_layer, on_lane):
    channels, layers, lanes = fields.shape
    high, low = split_bf16(fields)
    stacked = jnp.concatenate([high, low], axis=0).reshape(2 * channels * layers, lanes)
    picked = jnp.dot(stacked, on_lane, preferred_element_type=jnp.float32)
    picked = picked.reshape(2, channels, layers, on_lane.shape[1])
    return jnp.sum((picked[0] + picked[1]) * on_layer[None], axis=1)


def advance_block(buffer, cell_flow, cell_solids):
    speeds = buffer[0:3]
    friction = buffer[7]
    mobility = buffer[8]
    cell_void = 1.0 / (1.0 + cell_solids)
    relaxation = time_step * friction * mobility / (cell_void * cell_void)
    live_mask = (buffer[6] > 0).astype(jnp.float32)
    gravity_push = jnp.zeros_like(speeds).at[2].set(time_step * gravity * live_mask)
    new_speeds = (speeds + relaxation * cell_flow + gravity_push) / (1.0 + relaxation)
    spins = buffer[3:6] / (1.0 + relaxation)
    places = buffer[9:12] + time_step * new_speeds
    return jnp.concatenate([new_speeds, spins, buffer[6:9], places, buffer[12:14]], axis=0)


def slabs_to_blocks(field, blocks_x, blocks_y):
    channels, layers_z, cells_nx, cells_ny = field.shape
    cells_x, cells_y = cells_nx // blocks_x, cells_ny // blocks_y
    arranged = field.reshape(channels, layers_z, blocks_x, cells_x, blocks_y, cells_y).transpose(
        0, 2, 4, 1, 3, 5
    )
    arranged = arranged.reshape(channels, blocks_x * blocks_y * layers_z, cells_x * cells_y)
    return lax.all_to_all(arranged, ("dx", "dy"), split_axis=1, concat_axis=1, tiled=True)


def blocks_to_slabs(field, blocks_x, blocks_y, cells_x, cells_y):
    channels, depth, lanes = field.shape
    layers_z = depth // (blocks_x * blocks_y)
    return lax.all_to_all(field, ("dx", "dy"), split_axis=1, concat_axis=1, tiled=True)


def arrange_slabs(moved, blocks_x, blocks_y, cells_x, cells_y):
    channels, depth, lanes = moved.shape
    layers_z = depth // (blocks_x * blocks_y)
    arranged = moved.reshape(channels, blocks_x, blocks_y, layers_z, cells_x, cells_y).transpose(
        0, 3, 1, 4, 2, 5
    )
    return arranged.reshape(channels, layers_z, blocks_x * cells_x, blocks_y * cells_y)


def along_z(field):
    zero = jnp.zeros_like(field[..., :1, :])
    above = jnp.concatenate([field[..., 1:, :], zero], axis=-2)
    below = jnp.concatenate([zero, field[..., :-1, :]], axis=-2)
    return above, below


def faces_x(field, cells_y):
    ahead = from_behind(field[..., :cells_y], "dx", -1)
    behind = from_behind(field[..., field.shape[-1] - cells_y :], "dx", 1)
    return ahead, behind


def along_x(field, cells_y, faces=None):
    ahead, behind = faces_x(field, cells_y) if faces is None else faces
    plus = jnp.concatenate([field[..., cells_y:], ahead], axis=-1)
    minus = jnp.concatenate([behind, field[..., :-cells_y]], axis=-1)
    return plus, minus


def lane_selectors(cells_x, cells_y):
    lanes = cells_x * cells_y
    lane = lax.broadcasted_iota(jnp.int32, (lanes, 2 * cells_x), 0)
    column = lax.broadcasted_iota(jnp.int32, (lanes, 2 * cells_x), 1)
    picks = jnp.where(column < cells_x, column * cells_y, (column - cells_x) * cells_y + cells_y - 1)
    select = lane == picks
    spread_pick = jnp.where(column < cells_x, column * cells_y + cells_y - 1, (column - cells_x) * cells_y)
    spread = (lane == spread_pick).T
    return select.astype(jnp.bfloat16), spread.astype(jnp.bfloat16)


def exact_pick(values, one_hot):
    high = lax.reduce_precision(values, exponent_bits=8, mantissa_bits=7)
    rest = values - high
    middle = lax.reduce_precision(rest, exponent_bits=8, mantissa_bits=7)
    low = rest - middle
    rows = values.shape[0]
    parts = jnp.concatenate([high, middle, low], axis=0).astype(jnp.bfloat16)
    picked = jnp.dot(parts, one_hot, preferred_element_type=jnp.float32)
    return (picked[:rows] + picked[rows : 2 * rows]) + picked[2 * rows :]


def faces_y(field, selectors):
    cells_x = selectors[0].shape[1] // 2
    both = exact_pick(field.reshape(-1, field.shape[-1]), selectors[0])
    ahead = from_behind(both[:, :cells_x], "dy", -1)
    behind = from_behind(both[:, cells_x:], "dy", 1)
    return ahead, behind


def along_y(field, selectors, cells_y, faces=None):
    shape = field.shape
    ahead, behind = faces_y(field, selectors) if faces is None else faces
    halo = exact_pick(jnp.concatenate([ahead, behind], axis=1), selectors[1]).reshape(shape)
    lane_y = lax.broadcasted_iota(jnp.int32, shape, len(shape) - 1) % cells_y
    plus = jnp.where(lane_y == cells_y - 1, halo, jnp.roll(field, -1, axis=-1))
    minus = jnp.where(lane_y == 0, halo, jnp.roll(field, 1, axis=-1))
    return plus, minus


def fluid_predict(velocity, pressure, deposits, faces, selectors, cells_y):
    solids = deposits[0]
    voidage = 1.0 / (1.0 + solids)
    growth = (1.0 + solids) * (1.0 + solids)
    drag_rate = deposits[1] * growth
    drag_pull = deposits[2:5] * growth
    stacked = jnp.concatenate([velocity, pressure[None]], axis=0)
    z_plus, z_minus = along_z(stacked)
    x_plus, x_minus = along_x(stacked, cells_y, faces[0])
    y_plus, y_minus = along_y(stacked, selectors, cells_y, faces[1])
    beside_all = (z_plus + z_minus) + x_plus + x_minus + y_plus + y_minus
    predicted = (
        velocity + time_step * (viscosity * (beside_all[:3] - 6.0 * velocity) + drag_pull)
    ) / (1.0 + time_step * drag_rate)
    flux = voidage[None] * predicted
    fx_plus, fx_minus = along_x(flux[0], cells_y)
    fy_plus, fy_minus = along_y(flux[1], selectors, cells_y)
    fz_plus, fz_minus = along_z(flux[2])
    divergence = 0.5 * (fx_plus - fx_minus) + 0.5 * (fy_plus - fy_minus) + 0.5 * (fz_plus - fz_minus)
    pressure_new = (beside_all[3] - divergence / time_step) / 6.0
    pz_plus, pz_minus = along_z(pressure_new)
    flow_z = predicted[2] - time_step * (0.5 * (pz_plus - pz_minus))
    return predicted, pressure_new, flow_z


def fluid_correct(predicted, pressure_new, flow_z, selectors, cells_y):
    px_plus, px_minus = along_x(pressure_new, cells_y)
    py_plus, py_minus = along_y(pressure_new, selectors, cells_y)
    flow_x = predicted[0] - time_step * (0.5 * (px_plus - px_minus))
    flow_y = predicted[1] - time_step * (0.5 * (py_plus - py_minus))
    return jnp.stack([flow_x, flow_y, flow_z], axis=0)


def planar_correct(slabs):
    pressure = slabs[3]
    grad_x = 0.5 * (jnp.roll(pressure, -1, axis=1) - jnp.roll(pressure, 1, axis=1))
    grad_y = 0.5 * (jnp.roll(pressure, -1, axis=2) - jnp.roll(pressure, 1, axis=2))
    flow_x = slabs[0] - time_step * grad_x
    flow_y = slabs[1] - time_step * grad_y
    return jnp.stack([flow_x, flow_y, slabs[2]], axis=0), pressure


def shards(particles, leave_lists, leave_counts, slot_cells, velocity, pressure):
    blocks_x = lax.axis_size("dx")
    blocks_y = lax.axis_size("dy")
    records = particles[0, 0]
    leaver_lists = leave_lists[0, 0]
    leaver_counts = leave_counts[0, 0]
    cell_index = slot_cells[0, 0]
    capacity = leaver_lists.shape[1]
    holders = records.shape[1]
    cells_x = velocity.shape[2] // blocks_x
    cells_y = velocity.shape[3] // blocks_y
    lanes = cells_x * cells_y
    depth = velocity.shape[1] * blocks_x * blocks_y

    fields = slabs_to_blocks(
        jnp.concatenate([velocity, pressure[None]], axis=0), blocks_x, blocks_y
    )
    positions = jnp.arange(capacity, dtype=jnp.int32)
    validity = (positions[None, :] < leaver_counts[:, None]).astype(jnp.float32)
    flat_list = leaver_lists.reshape(-1)
    low_size = math.gcd(holders, 512)
    upper_size = holders // low_size
    listed = flat_list.shape[0]
    upper_of = flat_list // low_size
    lower_of = flat_list % low_size
    on_upper = lax.broadcasted_iota(jnp.int32, (upper_size, listed), 0) == upper_of[None, :]
    on_lower = lax.broadcasted_iota(jnp.int32, (low_size, listed), 0) == lower_of[None, :]
    valid_flat = validity.reshape(1, -1)
    departed = lax.dot_general(
        (on_upper.astype(jnp.float32) * valid_flat).astype(jnp.bfloat16),
        on_lower.astype(jnp.bfloat16),
        (((1,), (1,)), ((), ())),
        preferred_element_type=jnp.float32,
    ).reshape(holders)
    remaining = records * (1.0 - departed)[None, :]
    high = lax.reduce_precision(records, exponent_bits=8, mantissa_bits=7)
    rest = records - high
    middle = lax.reduce_precision(rest, exponent_bits=8, mantissa_bits=7)
    low = rest - middle
    rows = records.shape[0]
    parts = jnp.concatenate([high, middle, low], axis=0).astype(jnp.bfloat16)
    parts = parts.reshape(3 * rows * upper_size, low_size)
    by_lower = jnp.dot(parts, on_lower.astype(jnp.bfloat16), preferred_element_type=jnp.float32)
    by_lower = by_lower.reshape(3, rows, upper_size, listed)
    picked_parts = jnp.sum(by_lower * on_upper.astype(jnp.float32)[None, None], axis=2)
    picked_rows = (picked_parts[0] + picked_parts[1]) + picked_parts[2]
    outgoing = picked_rows.reshape(rows, 4, capacity) * validity[None]
    arrivals = migrate(outgoing)
    buffer = jnp.concatenate([remaining] + arrivals, axis=1)

    layer_of = cell_index // lanes
    lane_of = cell_index % lanes
    on_layer = (
        lax.broadcasted_iota(jnp.int32, (depth, cell_index.shape[0]), 0) == layer_of[None, :]
    ).astype(jnp.float32)
    on_lane = (
        lax.broadcasted_iota(jnp.int32, (cell_index.shape[0], lanes), 1) == lane_of[:, None]
    ).astype(jnp.bfloat16)
    lane_on = (
        lax.broadcasted_iota(jnp.int32, (lanes, cell_index.shape[0]), 0) == lane_of[None, :]
    ).astype(jnp.bfloat16)

    selectors = lane_selectors(cells_x, cells_y)
    fields, buffer = lax.optimization_barrier((fields, buffer))
    flow = fields[:3]
    pressure_block = fields[3]
    stacked = jnp.concatenate([flow, pressure_block[None]], axis=0)
    faces = (faces_x(stacked, cells_y), faces_y(stacked, selectors))
    for coupling in range(COUPLINGS):
        deposits = deposit_block(buffer, on_layer, on_lane)
        faces, deposits = lax.optimization_barrier((faces, deposits))
        predicted, pressure_block, flow_z = fluid_predict(
            flow, pressure_block, deposits, faces, selectors, cells_y
        )
        if coupling == COUPLINGS - 1:
            outgoing_fields = jnp.concatenate([predicted[:2], flow_z[None], pressure_block[None]], axis=0)
            outgoing_fields, pressure_block = lax.optimization_barrier((outgoing_fields, pressure_block))
            moved = blocks_to_slabs(outgoing_fields, blocks_x, blocks_y, cells_x, cells_y)
        flow = fluid_correct(predicted, pressure_block, flow_z, selectors, cells_y)
        picked = gather_block(
            jnp.concatenate([flow, deposits[:1]], axis=0), on_layer, lane_on
        )
        if coupling < COUPLINGS - 1:
            stacked = jnp.concatenate([flow, pressure_block[None]], axis=0)
            stacked, picked = lax.optimization_barrier((stacked, picked))
            faces = (faces_x(stacked, cells_y), faces_y(stacked, selectors))
        buffer = advance_block(buffer, picked[:3], picked[3])

    moved, particles_out = lax.optimization_barrier((moved, buffer[None, None]))
    slabs = arrange_slabs(moved, blocks_x, blocks_y, cells_x, cells_y)
    velocity_out, pressure_out = planar_correct(slabs)
    return (particles_out, velocity_out, pressure_out)


def solution(mesh):
    placed = (
        P("dx", "dy", None, None),
        P("dx", "dy", None, None),
        P("dx", "dy", None),
        P("dx", "dy", None),
        P(None, ("dx", "dy"), None, None),
        P(("dx", "dy"), None, None),
    )
    return jax.shard_map(
        shards,
        mesh=mesh,
        in_specs=placed,
        out_specs=(
            P("dx", "dy", None, None),
            P(None, ("dx", "dy"), None, None),
            P(("dx", "dy"), None, None),
        ),
        check_vma=False,
    )
```

```python
import math

import jax
import jax.numpy as jnp
from jax import lax
from jax.sharding import PartitionSpec as P

COUPLINGS = 2


time_step = 0.1
viscosity = 0.5
gravity = -1.0


def from_behind(value, axis, steps):
    count = lax.axis_size(axis)
    pairs = [(source, (source + steps) % count) for source in range(count)]
    return lax.ppermute(value, axis, pairs)


def migrate(outgoing):
    arrivals = []
    for offset in (1, -1):
        arrivals.append(from_behind(outgoing[:, (1 - offset) // 2], "dx", offset))
    for offset in (1, -1):
        arrivals.append(from_behind(outgoing[:, 2 + (1 - offset) // 2], "dy", offset))
    return arrivals


def split_bf16(values):
    high = lax.reduce_precision(values, exponent_bits=8, mantissa_bits=7)
    low = values - high
    return high.astype(jnp.bfloat16), low.astype(jnp.bfloat16)


def deposit_block(buffer, on_layer, on_lane):
    sources = jnp.concatenate([buffer[6:8], buffer[7][None] * buffer[0:3]], axis=0)
    layered = sources[:, None, :] * on_layer[None]
    high, low = split_bf16(layered)
    channels, layers, slots = layered.shape
    stacked = jnp.concatenate([high, low], axis=0).reshape(2 * channels * layers, slots)
    summed = jnp.dot(stacked, on_lane, preferred_element_type=jnp.float32)
    summed = summed.reshape(2, channels, layers, on_lane.shape[1])
    return summed[0] + summed[1]


def gather_block(fields, on_layer, on_lane):
    channels, layers, lanes = fields.shape
    high, low = split_bf16(fields)
    stacked = jnp.concatenate([high, low], axis=0).reshape(2 * channels * layers, lanes)
    picked = jnp.dot(stacked, on_lane, preferred_element_type=jnp.float32)
    picked = picked.reshape(2, channels, layers, on_lane.shape[1])
    return jnp.sum((picked[0] + picked[1]) * on_layer[None], axis=1)


def advance_block(buffer, cell_flow, cell_solids):
    speeds = buffer[0:3]
    friction = buffer[7]
    mobility = buffer[8]
    cell_void = 1.0 / (1.0 + cell_solids)
    relaxation = time_step * friction * mobility / (cell_void * cell_void)
    live_mask = (buffer[6] > 0).astype(jnp.float32)
    still = jnp.zeros_like(live_mask)
    gravity_push = jnp.stack([still, still, time_step * gravity * live_mask], axis=0)
    new_speeds = (speeds + relaxation * cell_flow + gravity_push) / (1.0 + relaxation)
    spins = buffer[3:6] / (1.0 + relaxation)
    places = buffer[9:12] + time_step * new_speeds
    return jnp.concatenate([new_speeds, spins, buffer[6:9], places, buffer[12:14]], axis=0)


def slabs_to_blocks(field, blocks_x, blocks_y):
    channels, layers_z, cells_nx, cells_ny = field.shape
    cells_x, cells_y = cells_nx // blocks_x, cells_ny // blocks_y
    arranged = field.reshape(channels, layers_z, blocks_x, cells_x, blocks_y, cells_y).transpose(
        0, 2, 4, 1, 3, 5
    )
    arranged = arranged.reshape(channels, blocks_x * blocks_y * layers_z, cells_x * cells_y)
    return lax.all_to_all(arranged, ("dx", "dy"), split_axis=1, concat_axis=1, tiled=True)


def blocks_to_slabs(field, blocks_x, blocks_y, cells_x, cells_y):
    channels, depth, lanes = field.shape
    layers_z = depth // (blocks_x * blocks_y)
    return lax.all_to_all(field, ("dx", "dy"), split_axis=1, concat_axis=1, tiled=True)


def arrange_slabs(moved, blocks_x, blocks_y, cells_x, cells_y):
    channels, depth, lanes = moved.shape
    layers_z = depth // (blocks_x * blocks_y)
    arranged = moved.reshape(channels, blocks_x, blocks_y, layers_z, cells_x, cells_y).transpose(
        0, 3, 1, 4, 2, 5
    )
    return arranged.reshape(channels, layers_z, blocks_x * cells_x, blocks_y * cells_y)


def along_z(field):
    zero = jnp.zeros_like(field[..., :1, :])
    above = jnp.concatenate([field[..., 1:, :], zero], axis=-2)
    below = jnp.concatenate([zero, field[..., :-1, :]], axis=-2)
    return above, below


def faces_x(field, cells_y):
    ahead = from_behind(field[..., :cells_y], "dx", -1)
    behind = from_behind(field[..., field.shape[-1] - cells_y :], "dx", 1)
    return ahead, behind


def along_x(field, cells_y, faces=None):
    ahead, behind = faces_x(field, cells_y) if faces is None else faces
    plus = jnp.concatenate([field[..., cells_y:], ahead], axis=-1)
    minus = jnp.concatenate([behind, field[..., :-cells_y]], axis=-1)
    return plus, minus


def lane_selectors(cells_x, cells_y):
    lanes = cells_x * cells_y
    lane = lax.broadcasted_iota(jnp.int32, (lanes, 2 * cells_x), 0)
    column = lax.broadcasted_iota(jnp.int32, (lanes, 2 * cells_x), 1)
    picks = jnp.where(column < cells_x, column * cells_y, (column - cells_x) * cells_y + cells_y - 1)
    select = lane == picks
    spread_pick = jnp.where(column < cells_x, column * cells_y + cells_y - 1, (column - cells_x) * cells_y)
    spread = (lane == spread_pick).T
    return select.astype(jnp.bfloat16), spread.astype(jnp.bfloat16)


def exact_pick(values, one_hot):
    high = lax.reduce_precision(values, exponent_bits=8, mantissa_bits=7)
    rest = values - high
    middle = lax.reduce_precision(rest, exponent_bits=8, mantissa_bits=7)
    low = rest - middle
    rows = values.shape[0]
    parts = jnp.concatenate([high, middle, low], axis=0).astype(jnp.bfloat16)
    picked = jnp.dot(parts, one_hot, preferred_element_type=jnp.float32)
    return (picked[:rows] + picked[rows : 2 * rows]) + picked[2 * rows :]


def faces_y(field, selectors):
    cells_x = selectors[0].shape[1] // 2
    both = exact_pick(field.reshape(-1, field.shape[-1]), selectors[0])
    ahead = from_behind(both[:, :cells_x], "dy", -1)
    behind = from_behind(both[:, cells_x:], "dy", 1)
    return ahead, behind


def along_y(field, selectors, cells_y, faces=None):
    shape = field.shape
    ahead, behind = faces_y(field, selectors) if faces is None else faces
    halo = exact_pick(jnp.concatenate([ahead, behind], axis=1), selectors[1]).reshape(shape)
    lane_y = lax.broadcasted_iota(jnp.int32, shape, len(shape) - 1) % cells_y
    plus = jnp.where(lane_y == cells_y - 1, halo, jnp.roll(field, -1, axis=-1))
    minus = jnp.where(lane_y == 0, halo, jnp.roll(field, 1, axis=-1))
    return plus, minus


def fluid_step(velocity, pressure, deposits, faces, selectors, cells_y):
    solids = deposits[0]
    voidage = 1.0 / (1.0 + solids)
    growth = (1.0 + solids) * (1.0 + solids)
    drag_rate = deposits[1] * growth
    drag_pull = deposits[2:5] * growth
    stacked = jnp.concatenate([velocity, pressure[None]], axis=0)
    z_plus, z_minus = along_z(stacked)
    x_plus, x_minus = along_x(stacked, cells_y, faces[0])
    y_plus, y_minus = along_y(stacked, selectors, cells_y, faces[1])
    beside_all = (z_plus + z_minus) + x_plus + x_minus + y_plus + y_minus
    predicted = (
        velocity + time_step * (viscosity * (beside_all[:3] - 6.0 * velocity) + drag_pull)
    ) / (1.0 + time_step * drag_rate)
    flux = voidage[None] * predicted
    fx_plus, fx_minus = along_x(flux[0], cells_y)
    fy_plus, fy_minus = along_y(flux[1], selectors, cells_y)
    fz_plus, fz_minus = along_z(flux[2])
    divergence = 0.5 * (fx_plus - fx_minus) + 0.5 * (fy_plus - fy_minus) + 0.5 * (fz_plus - fz_minus)
    pressure_new = (beside_all[3] - divergence / time_step) / 6.0
    px_plus, px_minus = along_x(pressure_new, cells_y)
    py_plus, py_minus = along_y(pressure_new, selectors, cells_y)
    pz_plus, pz_minus = along_z(pressure_new)
    gradient = jnp.stack(
        [0.5 * (px_plus - px_minus), 0.5 * (py_plus - py_minus), 0.5 * (pz_plus - pz_minus)], axis=0
    )
    return (predicted - time_step * gradient, pressure_new)


def shards(particles, leave_lists, leave_counts, slot_cells, velocity, pressure):
    blocks_x = lax.axis_size("dx")
    blocks_y = lax.axis_size("dy")
    records = particles[0, 0]
    leaver_lists = leave_lists[0, 0]
    leaver_counts = leave_counts[0, 0]
    cell_index = slot_cells[0, 0]
    capacity = leaver_lists.shape[1]
    holders = records.shape[1]
    cells_x = velocity.shape[2] // blocks_x
    cells_y = velocity.shape[3] // blocks_y
    lanes = cells_x * cells_y
    depth = velocity.shape[1] * blocks_x * blocks_y

    fields = slabs_to_blocks(
        jnp.concatenate([velocity, pressure[None]], axis=0), blocks_x, blocks_y
    )
    positions = jnp.arange(capacity, dtype=jnp.int32)
    validity = (positions[None, :] < leaver_counts[:, None]).astype(jnp.float32)
    flat_list = leaver_lists.reshape(-1)
    low_size = math.gcd(holders, 512)
    upper_size = holders // low_size
    listed = flat_list.shape[0]
    upper_of = flat_list // low_size
    lower_of = flat_list % low_size
    on_upper = lax.broadcasted_iota(jnp.int32, (upper_size, listed), 0) == upper_of[None, :]
    on_lower = lax.broadcasted_iota(jnp.int32, (low_size, listed), 0) == lower_of[None, :]
    valid_flat = validity.reshape(1, -1)
    departed = lax.dot_general(
        (on_upper.astype(jnp.float32) * valid_flat).astype(jnp.bfloat16),
        on_lower.astype(jnp.bfloat16),
        (((1,), (1,)), ((), ())),
        preferred_element_type=jnp.float32,
    ).reshape(holders)
    remaining = records * (1.0 - departed)[None, :]
    high = lax.reduce_precision(records, exponent_bits=8, mantissa_bits=7)
    rest = records - high
    middle = lax.reduce_precision(rest, exponent_bits=8, mantissa_bits=7)
    low = rest - middle
    rows = records.shape[0]
    parts = jnp.concatenate([high, middle, low], axis=0).astype(jnp.bfloat16)
    parts = parts.reshape(3 * rows * upper_size, low_size)
    by_lower = jnp.dot(parts, on_lower.astype(jnp.bfloat16), preferred_element_type=jnp.float32)
    by_lower = by_lower.reshape(3, rows, upper_size, listed)
    picked_parts = jnp.sum(by_lower * on_upper.astype(jnp.float32)[None, None], axis=2)
    picked_rows = (picked_parts[0] + picked_parts[1]) + picked_parts[2]
    outgoing = picked_rows.reshape(rows, 4, capacity) * validity[None]
    arrivals = migrate(outgoing)
    buffer = jnp.concatenate([remaining] + arrivals, axis=1)

    layer_of = cell_index // lanes
    lane_of = cell_index % lanes
    on_layer = (
        lax.broadcasted_iota(jnp.int32, (depth, cell_index.shape[0]), 0) == layer_of[None, :]
    ).astype(jnp.float32)
    on_lane = (
        lax.broadcasted_iota(jnp.int32, (cell_index.shape[0], lanes), 1) == lane_of[:, None]
    ).astype(jnp.bfloat16)
    lane_on = (
        lax.broadcasted_iota(jnp.int32, (lanes, cell_index.shape[0]), 0) == lane_of[None, :]
    ).astype(jnp.bfloat16)

    selectors = lane_selectors(cells_x, cells_y)
    resident_deposits = deposit_block(remaining, on_layer[:, :holders], on_lane[:holders])
    fields, buffer, resident_deposits = lax.optimization_barrier((fields, buffer, resident_deposits))
    flow = fields[:3]
    pressure_block = fields[3]
    stacked = jnp.concatenate([flow, pressure_block[None]], axis=0)
    faces = (faces_x(stacked, cells_y), faces_y(stacked, selectors))
    for coupling in range(COUPLINGS):
        if coupling == 0:
            deposits = resident_deposits + deposit_block(
                buffer[:, holders:], on_layer[:, holders:], on_lane[holders:]
            )
        else:
            deposits = deposit_block(buffer, on_layer, on_lane)
        faces, deposits = lax.optimization_barrier((faces, deposits))
        flow, pressure_block = fluid_step(flow, pressure_block, deposits, faces, selectors, cells_y)
        picked = gather_block(
            jnp.concatenate([flow, deposits[:1]], axis=0), on_layer, lane_on
        )
        stacked = jnp.concatenate([flow, pressure_block[None]], axis=0)
        if coupling < COUPLINGS - 1:
            stacked, picked = lax.optimization_barrier((stacked, picked))
            faces = (faces_x(stacked, cells_y), faces_y(stacked, selectors))
        else:
            moved = blocks_to_slabs(stacked, blocks_x, blocks_y, cells_x, cells_y)
        buffer = advance_block(buffer, picked[:3], picked[3])

    moved, particles_out = lax.optimization_barrier((moved, buffer[None, None]))
    velocity_out = arrange_slabs(moved[:3], blocks_x, blocks_y, cells_x, cells_y)
    pressure_out = arrange_slabs(moved[3:], blocks_x, blocks_y, cells_x, cells_y)
    return (particles_out, velocity_out, pressure_out[0])


def solution(mesh):
    placed = (
        P("dx", "dy", None, None),
        P("dx", "dy", None, None),
        P("dx", "dy", None),
        P("dx", "dy", None),
        P(None, ("dx", "dy"), None, None),
        P(("dx", "dy"), None, None),
    )
    return jax.shard_map(
        shards,
        mesh=mesh,
        in_specs=placed,
        out_specs=(
            P("dx", "dy", None, None),
            P(None, ("dx", "dy"), None, None),
            P(("dx", "dy"), None, None),
        ),
        check_vma=False,
    )
```

```python
import math

import jax
import jax.numpy as jnp
from jax import lax
from jax.sharding import PartitionSpec as P

COUPLINGS = 2


time_step = 0.1
viscosity = 0.5
gravity = -1.0


def from_behind(value, axis, steps):
    count = lax.axis_size(axis)
    pairs = [(source, (source + steps) % count) for source in range(count)]
    return lax.ppermute(value, axis, pairs)


def migrate(outgoing):
    arrivals = []
    for offset in (1, -1):
        arrivals.append(from_behind(outgoing[:, (1 - offset) // 2], "dx", offset))
    for offset in (1, -1):
        arrivals.append(from_behind(outgoing[:, 2 + (1 - offset) // 2], "dy", offset))
    return arrivals


def split_bf16(values):
    high = lax.reduce_precision(values, exponent_bits=8, mantissa_bits=7)
    low = values - high
    return high.astype(jnp.bfloat16), low.astype(jnp.bfloat16)


def deposit_block(buffer, on_layer, on_lane):
    sources = jnp.concatenate([buffer[6:8], buffer[7][None] * buffer[0:3]], axis=0)
    layered = sources[:, None, :] * on_layer[None]
    high, low = split_bf16(layered)
    channels, layers, slots = layered.shape
    stacked = jnp.concatenate([high, low], axis=0).reshape(2 * channels * layers, slots)
    summed = jnp.dot(stacked, on_lane, preferred_element_type=jnp.float32)
    summed = summed.reshape(2, channels, layers, on_lane.shape[1])
    return summed[0] + summed[1]


def gather_block(fields, on_layer, on_lane):
    channels, layers, lanes = fields.shape
    high, low = split_bf16(fields)
    stacked = jnp.concatenate([high, low], axis=0).reshape(2 * channels * layers, lanes)
    picked = jnp.dot(stacked, on_lane, preferred_element_type=jnp.float32)
    picked = picked.reshape(2, channels, layers, on_lane.shape[1])
    return jnp.sum((picked[0] + picked[1]) * on_layer[None], axis=1)


def advance_block(buffer, cell_flow, cell_solids):
    speeds = buffer[0:3]
    friction = buffer[7]
    mobility = buffer[8]
    cell_void = 1.0 / (1.0 + cell_solids)
    relaxation = time_step * friction * mobility / (cell_void * cell_void)
    live_mask = (buffer[6] > 0).astype(jnp.float32)
    still = jnp.zeros_like(live_mask)
    gravity_push = jnp.stack([still, still, time_step * gravity * live_mask], axis=0)
    new_speeds = (speeds + relaxation * cell_flow + gravity_push) / (1.0 + relaxation)
    spins = buffer[3:6] / (1.0 + relaxation)
    places = buffer[9:12] + time_step * new_speeds
    return jnp.concatenate([new_speeds, spins, buffer[6:9], places, buffer[12:14]], axis=0)


def slabs_to_blocks(field, blocks_x, blocks_y):
    channels, layers_z, cells_nx, cells_ny = field.shape
    cells_x, cells_y = cells_nx // blocks_x, cells_ny // blocks_y
    arranged = field.reshape(channels, layers_z, blocks_x, cells_x, blocks_y, cells_y).transpose(
        0, 2, 4, 1, 3, 5
    )
    arranged = arranged.reshape(channels, blocks_x * blocks_y * layers_z, cells_x * cells_y)
    return lax.all_to_all(arranged, ("dx", "dy"), split_axis=1, concat_axis=1, tiled=True)


def blocks_to_slabs(field, blocks_x, blocks_y, cells_x, cells_y):
    channels, depth, lanes = field.shape
    layers_z = depth // (blocks_x * blocks_y)
    return lax.all_to_all(field, ("dx", "dy"), split_axis=1, concat_axis=1, tiled=True)


def arrange_slabs(moved, blocks_x, blocks_y, cells_x, cells_y):
    channels, depth, lanes = moved.shape
    layers_z = depth // (blocks_x * blocks_y)
    arranged = moved.reshape(channels, blocks_x, blocks_y, layers_z, cells_x, cells_y).transpose(
        0, 3, 1, 4, 2, 5
    )
    return arranged.reshape(channels, layers_z, blocks_x * cells_x, blocks_y * cells_y)


def along_z(field):
    zero = jnp.zeros_like(field[..., :1, :])
    above = jnp.concatenate([field[..., 1:, :], zero], axis=-2)
    below = jnp.concatenate([zero, field[..., :-1, :]], axis=-2)
    return above, below


def faces_x(field, cells_y):
    ahead = from_behind(field[..., :cells_y], "dx", -1)
    behind = from_behind(field[..., field.shape[-1] - cells_y :], "dx", 1)
    return ahead, behind


def along_x(field, cells_y, faces=None):
    ahead, behind = faces_x(field, cells_y) if faces is None else faces
    plus = jnp.concatenate([field[..., cells_y:], ahead], axis=-1)
    minus = jnp.concatenate([behind, field[..., :-cells_y]], axis=-1)
    return plus, minus


def lane_selectors(cells_x, cells_y):
    lanes = cells_x * cells_y
    lane = lax.broadcasted_iota(jnp.int32, (lanes, 2 * cells_x), 0)
    column = lax.broadcasted_iota(jnp.int32, (lanes, 2 * cells_x), 1)
    picks = jnp.where(column < cells_x, column * cells_y, (column - cells_x) * cells_y + cells_y - 1)
    select = lane == picks
    spread_pick = jnp.where(column < cells_x, column * cells_y + cells_y - 1, (column - cells_x) * cells_y)
    spread = (lane == spread_pick).T
    return select.astype(jnp.bfloat16), spread.astype(jnp.bfloat16)


def exact_pick(values, one_hot):
    high = lax.reduce_precision(values, exponent_bits=8, mantissa_bits=7)
    rest = values - high
    middle = lax.reduce_precision(rest, exponent_bits=8, mantissa_bits=7)
    low = rest - middle
    rows = values.shape[0]
    parts = jnp.concatenate([high, middle, low], axis=0).astype(jnp.bfloat16)
    picked = jnp.dot(parts, one_hot, preferred_element_type=jnp.float32)
    return (picked[:rows] + picked[rows : 2 * rows]) + picked[2 * rows :]


def faces_y(field, selectors):
    cells_x = selectors[0].shape[1] // 2
    both = exact_pick(field.reshape(-1, field.shape[-1]), selectors[0])
    ahead = from_behind(both[:, :cells_x], "dy", -1)
    behind = from_behind(both[:, cells_x:], "dy", 1)
    return ahead, behind


def along_y(field, selectors, cells_y, faces=None):
    shape = field.shape
    ahead, behind = faces_y(field, selectors) if faces is None else faces
    halo = exact_pick(jnp.concatenate([ahead, behind], axis=1), selectors[1]).reshape(shape)
    lane_y = lax.broadcasted_iota(jnp.int32, shape, len(shape) - 1) % cells_y
    plus = jnp.where(lane_y == cells_y - 1, halo, jnp.roll(field, -1, axis=-1))
    minus = jnp.where(lane_y == 0, halo, jnp.roll(field, 1, axis=-1))
    return plus, minus


def fluid_step(velocity, pressure, deposits, faces, selectors, cells_y):
    solids = deposits[0]
    voidage = 1.0 / (1.0 + solids)
    growth = (1.0 + solids) * (1.0 + solids)
    drag_rate = deposits[1] * growth
    drag_pull = deposits[2:5] * growth
    stacked = jnp.concatenate([velocity, pressure[None]], axis=0)
    z_plus, z_minus = along_z(stacked)
    x_plus, x_minus = along_x(stacked, cells_y, faces[0])
    y_plus, y_minus = along_y(stacked, selectors, cells_y, faces[1])
    beside_all = (z_plus + z_minus) + x_plus + x_minus + y_plus + y_minus
    predicted = (
        velocity + time_step * (viscosity * (beside_all[:3] - 6.0 * velocity) + drag_pull)
    ) / (1.0 + time_step * drag_rate)
    flux = voidage[None] * predicted
    fx_plus, fx_minus = along_x(flux[0], cells_y)
    fy_plus, fy_minus = along_y(flux[1], selectors, cells_y)
    fz_plus, fz_minus = along_z(flux[2])
    divergence = 0.5 * (fx_plus - fx_minus) + 0.5 * (fy_plus - fy_minus) + 0.5 * (fz_plus - fz_minus)
    pressure_new = (beside_all[3] - divergence / time_step) / 6.0
    px_plus, px_minus = along_x(pressure_new, cells_y)
    py_plus, py_minus = along_y(pressure_new, selectors, cells_y)
    pz_plus, pz_minus = along_z(pressure_new)
    gradient = jnp.stack(
        [0.5 * (px_plus - px_minus), 0.5 * (py_plus - py_minus), 0.5 * (pz_plus - pz_minus)], axis=0
    )
    return (predicted - time_step * gradient, pressure_new)


def shards(particles, leave_lists, leave_counts, slot_cells, velocity, pressure):
    blocks_x = lax.axis_size("dx")
    blocks_y = lax.axis_size("dy")
    records = particles[0, 0]
    leaver_lists = leave_lists[0, 0]
    leaver_counts = leave_counts[0, 0]
    cell_index = slot_cells[0, 0]
    capacity = leaver_lists.shape[1]
    holders = records.shape[1]
    cells_x = velocity.shape[2] // blocks_x
    cells_y = velocity.shape[3] // blocks_y
    lanes = cells_x * cells_y
    depth = velocity.shape[1] * blocks_x * blocks_y

    fields = slabs_to_blocks(
        jnp.concatenate([velocity, pressure[None]], axis=0), blocks_x, blocks_y
    )
    positions = jnp.arange(capacity, dtype=jnp.int32)
    validity = (positions[None, :] < leaver_counts[:, None]).astype(jnp.float32)
    flat_list = leaver_lists.reshape(-1)
    low_size = math.gcd(holders, 512)
    upper_size = holders // low_size
    listed = flat_list.shape[0]
    upper_of = flat_list // low_size
    lower_of = flat_list % low_size
    on_upper = lax.broadcasted_iota(jnp.int32, (upper_size, listed), 0) == upper_of[None, :]
    on_lower = lax.broadcasted_iota(jnp.int32, (low_size, listed), 0) == lower_of[None, :]
    valid_flat = validity.reshape(1, -1)
    departed = lax.dot_general(
        (on_upper.astype(jnp.float32) * valid_flat).astype(jnp.bfloat16),
        on_lower.astype(jnp.bfloat16),
        (((1,), (1,)), ((), ())),
        preferred_element_type=jnp.float32,
    ).reshape(holders)
    remaining = records * (1.0 - departed)[None, :]
    high = lax.reduce_precision(records, exponent_bits=8, mantissa_bits=7)
    rest = records - high
    middle = lax.reduce_precision(rest, exponent_bits=8, mantissa_bits=7)
    low = rest - middle
    rows = records.shape[0]
    parts = jnp.concatenate([high, middle, low], axis=0).astype(jnp.bfloat16)
    parts = parts.reshape(3 * rows * upper_size, low_size)
    by_lower = jnp.dot(parts, on_lower.astype(jnp.bfloat16), preferred_element_type=jnp.float32)
    by_lower = by_lower.reshape(3, rows, upper_size, listed)
    picked_parts = jnp.sum(by_lower * on_upper.astype(jnp.float32)[None, None], axis=2)
    picked_rows = (picked_parts[0] + picked_parts[1]) + picked_parts[2]
    outgoing = picked_rows.reshape(rows, 4, capacity) * validity[None]
    arrivals = migrate(outgoing)
    buffer = jnp.concatenate([remaining] + arrivals, axis=1)

    layer_of = cell_index // lanes
    lane_of = cell_index % lanes
    on_layer = (
        lax.broadcasted_iota(jnp.int32, (depth, cell_index.shape[0]), 0) == layer_of[None, :]
    ).astype(jnp.float32)

    def lane_one_hot(lane_index):
        return (
            lax.broadcasted_iota(jnp.int32, (lane_index.shape[0], lanes), 1) == lane_index[:, None]
        ).astype(jnp.bfloat16)

    lane_on = (
        lax.broadcasted_iota(jnp.int32, (lanes, cell_index.shape[0]), 0) == lane_of[None, :]
    ).astype(jnp.bfloat16)

    selectors = lane_selectors(cells_x, cells_y)
    resident_deposits = deposit_block(remaining, on_layer[:, :holders], lane_one_hot(lane_of[:holders]))
    fields, buffer, resident_deposits = lax.optimization_barrier((fields, buffer, resident_deposits))
    flow = fields[:3]
    pressure_block = fields[3]
    stacked = jnp.concatenate([flow, pressure_block[None]], axis=0)
    faces = (faces_x(stacked, cells_y), faces_y(stacked, selectors))
    for coupling in range(COUPLINGS):
        if coupling == 0:
            deposits = resident_deposits + deposit_block(
                buffer[:, holders:], on_layer[:, holders:], lane_one_hot(lane_of[holders:])
            )
        else:
            deposits = deposit_block(buffer, on_layer, lane_one_hot(lane_of))
        faces, deposits = lax.optimization_barrier((faces, deposits))
        flow, pressure_block = fluid_step(flow, pressure_block, deposits, faces, selectors, cells_y)
        picked = gather_block(
            jnp.concatenate([flow, deposits[:1]], axis=0), on_layer, lane_on
        )
        stacked = jnp.concatenate([flow, pressure_block[None]], axis=0)
        if coupling < COUPLINGS - 1:
            stacked, picked = lax.optimization_barrier((stacked, picked))
            faces = (faces_x(stacked, cells_y), faces_y(stacked, selectors))
        else:
            moved = blocks_to_slabs(stacked, blocks_x, blocks_y, cells_x, cells_y)
        buffer = advance_block(buffer, picked[:3], picked[3])

    moved, particles_out = lax.optimization_barrier((moved, buffer[None, None]))
    velocity_out = arrange_slabs(moved[:3], blocks_x, blocks_y, cells_x, cells_y)
    pressure_out = arrange_slabs(moved[3:], blocks_x, blocks_y, cells_x, cells_y)
    return (particles_out, velocity_out, pressure_out[0])


def solution(mesh):
    placed = (
        P("dx", "dy", None, None),
        P("dx", "dy", None, None),
        P("dx", "dy", None),
        P("dx", "dy", None),
        P(None, ("dx", "dy"), None, None),
        P(("dx", "dy"), None, None),
    )
    return jax.shard_map(
        shards,
        mesh=mesh,
        in_specs=placed,
        out_specs=(
            P("dx", "dy", None, None),
            P(None, ("dx", "dy"), None, None),
            P(("dx", "dy"), None, None),
        ),
        check_vma=False,
    )
```

```python
import math

import jax
import jax.numpy as jnp
from jax import lax
from jax.experimental.layout import Layout, with_layout_constraint
from jax.sharding import PartitionSpec as P

COUPLINGS = 2


time_step = 0.1
viscosity = 0.5
gravity = -1.0


def from_behind(value, axis, steps):
    count = lax.axis_size(axis)
    pairs = [(source, (source + steps) % count) for source in range(count)]
    return lax.ppermute(value, axis, pairs)


def migrate(outgoing):
    arrivals = []
    for offset in (1, -1):
        arrivals.append(from_behind(outgoing[:, (1 - offset) // 2], "dx", offset))
    for offset in (1, -1):
        arrivals.append(from_behind(outgoing[:, 2 + (1 - offset) // 2], "dy", offset))
    return arrivals


def split_bf16(values):
    high = lax.reduce_precision(values, exponent_bits=8, mantissa_bits=7)
    low = values - high
    return high.astype(jnp.bfloat16), low.astype(jnp.bfloat16)


def deposit_block(buffer, on_layer, on_lane):
    sources = jnp.concatenate([buffer[6:8], buffer[7][None] * buffer[0:3]], axis=0)
    layered = sources[:, None, :] * on_layer[None]
    high, low = split_bf16(layered)
    channels, layers, slots = layered.shape
    stacked = jnp.concatenate([high, low], axis=0).reshape(2 * channels * layers, slots)
    summed = jnp.dot(stacked, on_lane, preferred_element_type=jnp.float32)
    summed = summed.reshape(2, channels, layers, on_lane.shape[1])
    return summed[0] + summed[1]


def gather_block(fields, on_layer, on_lane):
    channels, layers, lanes = fields.shape
    high, low = split_bf16(fields)
    stacked = jnp.concatenate([high, low], axis=0).reshape(2 * channels * layers, lanes)
    picked = jnp.dot(stacked, on_lane, preferred_element_type=jnp.float32)
    picked = picked.reshape(2, channels, layers, on_lane.shape[1])
    return jnp.sum((picked[0] + picked[1]) * on_layer[None], axis=1)


def advance_block(buffer, cell_flow, cell_solids):
    speeds = buffer[0:3]
    friction = buffer[7]
    mobility = buffer[8]
    cell_void = 1.0 / (1.0 + cell_solids)
    relaxation = time_step * friction * mobility / (cell_void * cell_void)
    live_mask = (buffer[6] > 0).astype(jnp.float32)
    still = jnp.zeros_like(live_mask)
    gravity_push = jnp.stack([still, still, time_step * gravity * live_mask], axis=0)
    new_speeds = (speeds + relaxation * cell_flow + gravity_push) / (1.0 + relaxation)
    spins = buffer[3:6] / (1.0 + relaxation)
    places = buffer[9:12] + time_step * new_speeds
    return jnp.concatenate([new_speeds, spins, buffer[6:9], places, buffer[12:14]], axis=0)


def slabs_to_blocks(field, blocks_x, blocks_y):
    channels, layers_z, cells_nx, cells_ny = field.shape
    cells_x, cells_y = cells_nx // blocks_x, cells_ny // blocks_y
    arranged = field.reshape(channels, layers_z, blocks_x, cells_x, blocks_y, cells_y).transpose(
        0, 2, 4, 1, 3, 5
    )
    arranged = arranged.reshape(channels, blocks_x * blocks_y * layers_z, cells_x * cells_y)
    return lax.all_to_all(arranged, ("dx", "dy"), split_axis=1, concat_axis=1, tiled=True)


def blocks_to_slabs(field, blocks_x, blocks_y, cells_x, cells_y):
    channels, depth, lanes = field.shape
    layers_z = depth // (blocks_x * blocks_y)
    return lax.all_to_all(field, ("dx", "dy"), split_axis=1, concat_axis=1, tiled=True)


def arrange_slabs(moved, blocks_x, blocks_y, cells_x, cells_y):
    channels, depth, lanes = moved.shape
    layers_z = depth // (blocks_x * blocks_y)
    arranged = moved.reshape(channels, blocks_x, blocks_y, layers_z, cells_x, cells_y).transpose(
        0, 3, 1, 4, 2, 5
    )
    return arranged.reshape(channels, layers_z, blocks_x * cells_x, blocks_y * cells_y)


def along_z(field):
    zero = jnp.zeros_like(field[..., :1, :])
    above = jnp.concatenate([field[..., 1:, :], zero], axis=-2)
    below = jnp.concatenate([zero, field[..., :-1, :]], axis=-2)
    return above, below


def faces_x(field, cells_y):
    ahead = from_behind(field[..., :cells_y], "dx", -1)
    behind = from_behind(field[..., field.shape[-1] - cells_y :], "dx", 1)
    return ahead, behind


def along_x(field, cells_y, faces=None):
    ahead, behind = faces_x(field, cells_y) if faces is None else faces
    plus = jnp.concatenate([field[..., cells_y:], ahead], axis=-1)
    minus = jnp.concatenate([behind, field[..., :-cells_y]], axis=-1)
    return plus, minus


def lane_selectors(cells_x, cells_y):
    lanes = cells_x * cells_y
    lane = lax.broadcasted_iota(jnp.int32, (lanes, 2 * cells_x), 0)
    column = lax.broadcasted_iota(jnp.int32, (lanes, 2 * cells_x), 1)
    picks = jnp.where(column < cells_x, column * cells_y, (column - cells_x) * cells_y + cells_y - 1)
    select = lane == picks
    spread_pick = jnp.where(column < cells_x, column * cells_y + cells_y - 1, (column - cells_x) * cells_y)
    spread = (lane == spread_pick).T
    return select.astype(jnp.bfloat16), spread.astype(jnp.bfloat16)


def exact_pick(values, one_hot):
    high = lax.reduce_precision(values, exponent_bits=8, mantissa_bits=7)
    rest = values - high
    middle = lax.reduce_precision(rest, exponent_bits=8, mantissa_bits=7)
    low = rest - middle
    rows = values.shape[0]
    parts = jnp.concatenate([high, middle, low], axis=0).astype(jnp.bfloat16)
    picked = jnp.dot(parts, one_hot, preferred_element_type=jnp.float32)
    return (picked[:rows] + picked[rows : 2 * rows]) + picked[2 * rows :]


def faces_y(field, selectors):
    cells_x = selectors[0].shape[1] // 2
    both = exact_pick(field.reshape(-1, field.shape[-1]), selectors[0])
    ahead = from_behind(both[:, :cells_x], "dy", -1)
    behind = from_behind(both[:, cells_x:], "dy", 1)
    return ahead, behind


def along_y(field, selectors, cells_y, faces=None):
    shape = field.shape
    ahead, behind = faces_y(field, selectors) if faces is None else faces
    halo = exact_pick(jnp.concatenate([ahead, behind], axis=1), selectors[1]).reshape(shape)
    lane_y = lax.broadcasted_iota(jnp.int32, shape, len(shape) - 1) % cells_y
    plus = jnp.where(lane_y == cells_y - 1, halo, jnp.roll(field, -1, axis=-1))
    minus = jnp.where(lane_y == 0, halo, jnp.roll(field, 1, axis=-1))
    return plus, minus


def fluid_step(velocity, pressure, deposits, faces, selectors, cells_y):
    solids = deposits[0]
    voidage = 1.0 / (1.0 + solids)
    growth = (1.0 + solids) * (1.0 + solids)
    drag_rate = deposits[1] * growth
    drag_pull = deposits[2:5] * growth
    stacked = jnp.concatenate([velocity, pressure[None]], axis=0)
    z_plus, z_minus = along_z(stacked)
    x_plus, x_minus = along_x(stacked, cells_y, faces[0])
    y_plus, y_minus = along_y(stacked, selectors, cells_y, faces[1])
    beside_all = (z_plus + z_minus) + x_plus + x_minus + y_plus + y_minus
    predicted = (
        velocity + time_step * (viscosity * (beside_all[:3] - 6.0 * velocity) + drag_pull)
    ) / (1.0 + time_step * drag_rate)
    flux = voidage[None] * predicted
    fx_plus, fx_minus = along_x(flux[0], cells_y)
    fy_plus, fy_minus = along_y(flux[1], selectors, cells_y)
    fz_plus, fz_minus = along_z(flux[2])
    divergence = 0.5 * (fx_plus - fx_minus) + 0.5 * (fy_plus - fy_minus) + 0.5 * (fz_plus - fz_minus)
    pressure_new = (beside_all[3] - divergence / time_step) / 6.0
    px_plus, px_minus = along_x(pressure_new, cells_y)
    py_plus, py_minus = along_y(pressure_new, selectors, cells_y)
    pz_plus, pz_minus = along_z(pressure_new)
    gradient = jnp.stack(
        [0.5 * (px_plus - px_minus), 0.5 * (py_plus - py_minus), 0.5 * (pz_plus - pz_minus)], axis=0
    )
    return jnp.concatenate([predicted - time_step * gradient, pressure_new[None]], axis=0)


def shards(particles, leave_lists, leave_counts, slot_cells, velocity, pressure):
    blocks_x = lax.axis_size("dx")
    blocks_y = lax.axis_size("dy")
    records = particles[0, 0]
    leaver_lists = leave_lists[0, 0]
    leaver_counts = leave_counts[0, 0]
    cell_index = slot_cells[0, 0]
    capacity = leaver_lists.shape[1]
    holders = records.shape[1]
    cells_x = velocity.shape[2] // blocks_x
    cells_y = velocity.shape[3] // blocks_y
    lanes = cells_x * cells_y
    depth = velocity.shape[1] * blocks_x * blocks_y

    fields = slabs_to_blocks(
        jnp.concatenate([velocity, pressure[None]], axis=0), blocks_x, blocks_y
    )
    positions = jnp.arange(capacity, dtype=jnp.int32)
    validity = (positions[None, :] < leaver_counts[:, None]).astype(jnp.float32)
    flat_list = leaver_lists.reshape(-1)
    low_size = math.gcd(holders, 512)
    upper_size = holders // low_size
    listed = flat_list.shape[0]
    upper_of = flat_list // low_size
    lower_of = flat_list % low_size
    on_upper = lax.broadcasted_iota(jnp.int32, (upper_size, listed), 0) == upper_of[None, :]
    on_lower = lax.broadcasted_iota(jnp.int32, (low_size, listed), 0) == lower_of[None, :]
    valid_flat = validity.reshape(1, -1)
    departed = lax.dot_general(
        (on_upper.astype(jnp.float32) * valid_flat).astype(jnp.bfloat16),
        on_lower.astype(jnp.bfloat16),
        (((1,), (1,)), ((), ())),
        preferred_element_type=jnp.float32,
    ).reshape(holders)
    remaining = records * (1.0 - departed)[None, :]
    high = lax.reduce_precision(records, exponent_bits=8, mantissa_bits=7)
    rest = records - high
    middle = lax.reduce_precision(rest, exponent_bits=8, mantissa_bits=7)
    low = rest - middle
    rows = records.shape[0]
    parts = jnp.concatenate([high, middle, low], axis=0).astype(jnp.bfloat16)
    parts = parts.reshape(3 * rows * upper_size, low_size)
    by_lower = jnp.dot(parts, on_lower.astype(jnp.bfloat16), preferred_element_type=jnp.float32)
    by_lower = by_lower.reshape(3, rows, upper_size, listed)
    picked_parts = jnp.sum(by_lower * on_upper.astype(jnp.float32)[None, None], axis=2)
    picked_rows = (picked_parts[0] + picked_parts[1]) + picked_parts[2]
    outgoing = picked_rows.reshape(rows, 4, capacity) * validity[None]
    arrivals = migrate(outgoing)
    buffer = jnp.concatenate([remaining] + arrivals, axis=1)

    layer_of = cell_index // lanes
    lane_of = cell_index % lanes
    on_layer = (
        lax.broadcasted_iota(jnp.int32, (depth, cell_index.shape[0]), 0) == layer_of[None, :]
    ).astype(jnp.float32)

    def lane_one_hot(lane_index):
        return (
            lax.broadcasted_iota(jnp.int32, (lane_index.shape[0], lanes), 1) == lane_index[:, None]
        ).astype(jnp.bfloat16)

    lane_on = (
        lax.broadcasted_iota(jnp.int32, (lanes, cell_index.shape[0]), 0) == lane_of[None, :]
    ).astype(jnp.bfloat16)

    selectors = lane_selectors(cells_x, cells_y)
    resident_deposits = deposit_block(remaining, on_layer[:, :holders], lane_one_hot(lane_of[:holders]))
    fields, buffer, resident_deposits = lax.optimization_barrier((fields, buffer, resident_deposits))
    flow = fields[:3]
    pressure_block = fields[3]
    stacked = jnp.concatenate([flow, pressure_block[None]], axis=0)
    faces = (faces_x(stacked, cells_y), faces_y(stacked, selectors))
    for coupling in range(COUPLINGS):
        if coupling == 0:
            deposits = resident_deposits + deposit_block(
                buffer[:, holders:], on_layer[:, holders:], lane_one_hot(lane_of[holders:])
            )
        else:
            deposits = deposit_block(buffer, on_layer, lane_one_hot(lane_of))
        faces, deposits = lax.optimization_barrier((faces, deposits))
        stacked = fluid_step(flow, pressure_block, deposits, faces, selectors, cells_y)
        if coupling == COUPLINGS - 1:
            stacked = with_layout_constraint(stacked, Layout((1, 0, 2)))
        flow, pressure_block = stacked[:3], stacked[3]
        picked = gather_block(
            jnp.concatenate([flow, deposits[:1]], axis=0), on_layer, lane_on
        )
        if coupling < COUPLINGS - 1:
            stacked, picked = lax.optimization_barrier((stacked, picked))
            faces = (faces_x(stacked, cells_y), faces_y(stacked, selectors))
        else:
            moved = blocks_to_slabs(stacked, blocks_x, blocks_y, cells_x, cells_y)
        buffer = advance_block(buffer, picked[:3], picked[3])

    moved, particles_out = lax.optimization_barrier((moved, buffer[None, None]))
    velocity_out = arrange_slabs(moved[:3], blocks_x, blocks_y, cells_x, cells_y)
    pressure_out = arrange_slabs(moved[3:], blocks_x, blocks_y, cells_x, cells_y)
    return (particles_out, velocity_out, pressure_out[0])


def solution(mesh):
    placed = (
        P("dx", "dy", None, None),
        P("dx", "dy", None, None),
        P("dx", "dy", None),
        P("dx", "dy", None),
        P(None, ("dx", "dy"), None, None),
        P(("dx", "dy"), None, None),
    )
    return jax.shard_map(
        shards,
        mesh=mesh,
        in_specs=placed,
        out_specs=(
            P("dx", "dy", None, None),
            P(None, ("dx", "dy"), None, None),
            P(("dx", "dy"), None, None),
        ),
        check_vma=False,
    )
```

```python
import math

import jax
import jax.numpy as jnp
from jax import lax
from jax.sharding import PartitionSpec as P

COUPLINGS = 2


time_step = 0.1
viscosity = 0.5
gravity = -1.0


def from_behind(value, axis, steps):
    count = lax.axis_size(axis)
    pairs = [(source, (source + steps) % count) for source in range(count)]
    return lax.ppermute(value, axis, pairs)


def migrate(outgoing):
    arrivals = []
    for offset in (1, -1):
        arrivals.append(from_behind(outgoing[:, (1 - offset) // 2], "dx", offset))
    for offset in (1, -1):
        arrivals.append(from_behind(outgoing[:, 2 + (1 - offset) // 2], "dy", offset))
    return arrivals


def split_bf16(values):
    high = lax.reduce_precision(values, exponent_bits=8, mantissa_bits=7)
    low = values - high
    return high.astype(jnp.bfloat16), low.astype(jnp.bfloat16)


def deposit_block(buffer, on_layer, on_lane):
    sources = jnp.concatenate([buffer[6:8], buffer[7][None] * buffer[0:3]], axis=0)
    high, low = split_bf16(sources)
    parts = jnp.concatenate([high, low], axis=0)
    mask = on_layer.astype(jnp.bfloat16)
    channels, slots = sources.shape
    layers = on_layer.shape[0]
    stacked = (parts[:, None, :] * mask[None]).reshape(2 * channels * layers, slots)
    summed = jnp.dot(stacked, on_lane, preferred_element_type=jnp.float32)
    summed = summed.reshape(2, channels, layers, on_lane.shape[1])
    return summed[0] + summed[1]


def gather_block(fields, on_layer, on_lane):
    channels, layers, lanes = fields.shape
    high, low = split_bf16(fields)
    stacked = jnp.concatenate([high, low], axis=0).reshape(2 * channels * layers, lanes)
    picked = jnp.dot(stacked, on_lane, preferred_element_type=jnp.float32)
    picked = picked.reshape(2, channels, layers, on_lane.shape[1])
    return jnp.sum((picked[0] + picked[1]) * on_layer[None], axis=1)


def advance_block(buffer, cell_flow, cell_solids):
    speeds = buffer[0:3]
    friction = buffer[7]
    mobility = buffer[8]
    cell_void = 1.0 / (1.0 + cell_solids)
    relaxation = time_step * friction * mobility / (cell_void * cell_void)
    live_mask = (buffer[6] > 0).astype(jnp.float32)
    still = jnp.zeros_like(live_mask)
    gravity_push = jnp.stack([still, still, time_step * gravity * live_mask], axis=0)
    new_speeds = (speeds + relaxation * cell_flow + gravity_push) / (1.0 + relaxation)
    spins = buffer[3:6] / (1.0 + relaxation)
    places = buffer[9:12] + time_step * new_speeds
    return jnp.concatenate([new_speeds, spins, buffer[6:9], places, buffer[12:14]], axis=0)


def slabs_to_blocks(field, blocks_x, blocks_y):
    channels, layers_z, cells_nx, cells_ny = field.shape
    cells_x, cells_y = cells_nx // blocks_x, cells_ny // blocks_y
    arranged = field.reshape(channels, layers_z, blocks_x, cells_x, blocks_y, cells_y).transpose(
        0, 2, 4, 1, 3, 5
    )
    arranged = arranged.reshape(channels, blocks_x * blocks_y * layers_z, cells_x * cells_y)
    return lax.all_to_all(arranged, ("dx", "dy"), split_axis=1, concat_axis=1, tiled=True)


def blocks_to_slabs(field, blocks_x, blocks_y, cells_x, cells_y):
    channels, depth, lanes = field.shape
    layers_z = depth // (blocks_x * blocks_y)
    return lax.all_to_all(field, ("dx", "dy"), split_axis=1, concat_axis=1, tiled=True)


def arrange_slabs(moved, blocks_x, blocks_y, cells_x, cells_y):
    channels, depth, lanes = moved.shape
    layers_z = depth // (blocks_x * blocks_y)
    arranged = moved.reshape(channels, blocks_x, blocks_y, layers_z, cells_x, cells_y).transpose(
        0, 3, 1, 4, 2, 5
    )
    return arranged.reshape(channels, layers_z, blocks_x * cells_x, blocks_y * cells_y)


def along_z(field):
    zero = jnp.zeros_like(field[..., :1, :])
    above = jnp.concatenate([field[..., 1:, :], zero], axis=-2)
    below = jnp.concatenate([zero, field[..., :-1, :]], axis=-2)
    return above, below


def faces_x(field, cells_y):
    ahead = from_behind(field[..., :cells_y], "dx", -1)
    behind = from_behind(field[..., field.shape[-1] - cells_y :], "dx", 1)
    return ahead, behind


def along_x(field, cells_y, faces=None):
    ahead, behind = faces_x(field, cells_y) if faces is None else faces
    plus = jnp.concatenate([field[..., cells_y:], ahead], axis=-1)
    minus = jnp.concatenate([behind, field[..., :-cells_y]], axis=-1)
    return plus, minus


def lane_selectors(cells_x, cells_y):
    lanes = cells_x * cells_y
    lane = lax.broadcasted_iota(jnp.int32, (lanes, 2 * cells_x), 0)
    column = lax.broadcasted_iota(jnp.int32, (lanes, 2 * cells_x), 1)
    picks = jnp.where(column < cells_x, column * cells_y, (column - cells_x) * cells_y + cells_y - 1)
    select = lane == picks
    spread_pick = jnp.where(column < cells_x, column * cells_y + cells_y - 1, (column - cells_x) * cells_y)
    spread = (lane == spread_pick).T
    return select.astype(jnp.bfloat16), spread.astype(jnp.bfloat16)


def exact_pick(values, one_hot):
    high = lax.reduce_precision(values, exponent_bits=8, mantissa_bits=7)
    rest = values - high
    middle = lax.reduce_precision(rest, exponent_bits=8, mantissa_bits=7)
    low = rest - middle
    rows = values.shape[0]
    parts = jnp.concatenate([high, middle, low], axis=0).astype(jnp.bfloat16)
    picked = jnp.dot(parts, one_hot, preferred_element_type=jnp.float32)
    return (picked[:rows] + picked[rows : 2 * rows]) + picked[2 * rows :]


def faces_y(field, selectors):
    cells_x = selectors[0].shape[1] // 2
    both = exact_pick(field.reshape(-1, field.shape[-1]), selectors[0])
    ahead = from_behind(both[:, :cells_x], "dy", -1)
    behind = from_behind(both[:, cells_x:], "dy", 1)
    return ahead, behind


def along_y(field, selectors, cells_y, faces=None):
    shape = field.shape
    ahead, behind = faces_y(field, selectors) if faces is None else faces
    halo = exact_pick(jnp.concatenate([ahead, behind], axis=1), selectors[1]).reshape(shape)
    lane_y = lax.broadcasted_iota(jnp.int32, shape, len(shape) - 1) % cells_y
    plus = jnp.where(lane_y == cells_y - 1, halo, jnp.roll(field, -1, axis=-1))
    minus = jnp.where(lane_y == 0, halo, jnp.roll(field, 1, axis=-1))
    return plus, minus


def fluid_step(velocity, pressure, deposits, faces, selectors, cells_y):
    solids = deposits[0]
    voidage = 1.0 / (1.0 + solids)
    growth = (1.0 + solids) * (1.0 + solids)
    drag_rate = deposits[1] * growth
    drag_pull = deposits[2:5] * growth
    stacked = jnp.concatenate([velocity, pressure[None]], axis=0)
    z_plus, z_minus = along_z(stacked)
    x_plus, x_minus = along_x(stacked, cells_y, faces[0])
    y_plus, y_minus = along_y(stacked, selectors, cells_y, faces[1])
    beside_all = (z_plus + z_minus) + x_plus + x_minus + y_plus + y_minus
    predicted = (
        velocity + time_step * (viscosity * (beside_all[:3] - 6.0 * velocity) + drag_pull)
    ) / (1.0 + time_step * drag_rate)
    flux = voidage[None] * predicted
    fx_plus, fx_minus = along_x(flux[0], cells_y)
    fy_plus, fy_minus = along_y(flux[1], selectors, cells_y)
    fz_plus, fz_minus = along_z(flux[2])
    divergence = 0.5 * (fx_plus - fx_minus) + 0.5 * (fy_plus - fy_minus) + 0.5 * (fz_plus - fz_minus)
    pressure_new = (beside_all[3] - divergence / time_step) / 6.0
    px_plus, px_minus = along_x(pressure_new, cells_y)
    py_plus, py_minus = along_y(pressure_new, selectors, cells_y)
    pz_plus, pz_minus = along_z(pressure_new)
    gradient = jnp.stack(
        [0.5 * (px_plus - px_minus), 0.5 * (py_plus - py_minus), 0.5 * (pz_plus - pz_minus)], axis=0
    )
    return (predicted - time_step * gradient, pressure_new)


def shards(particles, leave_lists, leave_counts, slot_cells, velocity, pressure):
    blocks_x = lax.axis_size("dx")
    blocks_y = lax.axis_size("dy")
    records = particles[0, 0]
    leaver_lists = leave_lists[0, 0]
    leaver_counts = leave_counts[0, 0]
    cell_index = slot_cells[0, 0]
    capacity = leaver_lists.shape[1]
    holders = records.shape[1]
    cells_x = velocity.shape[2] // blocks_x
    cells_y = velocity.shape[3] // blocks_y
    lanes = cells_x * cells_y
    depth = velocity.shape[1] * blocks_x * blocks_y

    fields = slabs_to_blocks(
        jnp.concatenate([velocity, pressure[None]], axis=0), blocks_x, blocks_y
    )
    positions = jnp.arange(capacity, dtype=jnp.int32)
    validity = (positions[None, :] < leaver_counts[:, None]).astype(jnp.float32)
    flat_list = leaver_lists.reshape(-1)
    low_size = math.gcd(holders, 512)
    upper_size = holders // low_size
    listed = flat_list.shape[0]
    upper_of = flat_list // low_size
    lower_of = flat_list % low_size
    on_upper = lax.broadcasted_iota(jnp.int32, (upper_size, listed), 0) == upper_of[None, :]
    on_lower = lax.broadcasted_iota(jnp.int32, (low_size, listed), 0) == lower_of[None, :]
    valid_flat = validity.reshape(1, -1)
    departed = lax.dot_general(
        (on_upper.astype(jnp.float32) * valid_flat).astype(jnp.bfloat16),
        on_lower.astype(jnp.bfloat16),
        (((1,), (1,)), ((), ())),
        preferred_element_type=jnp.float32,
    ).reshape(holders)
    remaining = records * (1.0 - departed)[None, :]
    high = lax.reduce_precision(records, exponent_bits=8, mantissa_bits=7)
    rest = records - high
    middle = lax.reduce_precision(rest, exponent_bits=8, mantissa_bits=7)
    low = rest - middle
    rows = records.shape[0]
    parts = jnp.concatenate([high, middle, low], axis=0).astype(jnp.bfloat16)
    parts = parts.reshape(3 * rows * upper_size, low_size)
    by_lower = jnp.dot(parts, on_lower.astype(jnp.bfloat16), preferred_element_type=jnp.float32)
    by_lower = by_lower.reshape(3, rows, upper_size, listed)
    picked_parts = jnp.sum(by_lower * on_upper.astype(jnp.float32)[None, None], axis=2)
    picked_rows = (picked_parts[0] + picked_parts[1]) + picked_parts[2]
    outgoing = picked_rows.reshape(rows, 4, capacity) * validity[None]
    arrivals = migrate(outgoing)
    buffer = jnp.concatenate([remaining] + arrivals, axis=1)

    layer_of = cell_index // lanes
    lane_of = cell_index % lanes
    on_layer = (
        lax.broadcasted_iota(jnp.int32, (depth, cell_index.shape[0]), 0) == layer_of[None, :]
    ).astype(jnp.float32)

    def lane_one_hot(lane_index):
        return (
            lax.broadcasted_iota(jnp.int32, (lane_index.shape[0], lanes), 1) == lane_index[:, None]
        ).astype(jnp.bfloat16)

    lane_on = (
        lax.broadcasted_iota(jnp.int32, (lanes, cell_index.shape[0]), 0) == lane_of[None, :]
    ).astype(jnp.bfloat16)

    selectors = lane_selectors(cells_x, cells_y)
    resident_deposits = deposit_block(remaining, on_layer[:, :holders], lane_one_hot(lane_of[:holders]))
    fields, buffer, resident_deposits = lax.optimization_barrier((fields, buffer, resident_deposits))
    flow = fields[:3]
    pressure_block = fields[3]
    stacked = jnp.concatenate([flow, pressure_block[None]], axis=0)
    faces = (faces_x(stacked, cells_y), faces_y(stacked, selectors))
    for coupling in range(COUPLINGS):
        if coupling == 0:
            deposits = resident_deposits + deposit_block(
                buffer[:, holders:], on_layer[:, holders:], lane_one_hot(lane_of[holders:])
            )
        else:
            deposits = deposit_block(buffer, on_layer, lane_one_hot(lane_of))
        faces, deposits = lax.optimization_barrier((faces, deposits))
        flow, pressure_block = fluid_step(flow, pressure_block, deposits, faces, selectors, cells_y)
        picked = gather_block(
            jnp.concatenate([flow, deposits[:1]], axis=0), on_layer, lane_on
        )
        stacked = jnp.concatenate([flow, pressure_block[None]], axis=0)
        if coupling < COUPLINGS - 1:
            stacked, picked = lax.optimization_barrier((stacked, picked))
            faces = (faces_x(stacked, cells_y), faces_y(stacked, selectors))
        else:
            moved = blocks_to_slabs(stacked, blocks_x, blocks_y, cells_x, cells_y)
        buffer = advance_block(buffer, picked[:3], picked[3])

    moved, particles_out = lax.optimization_barrier((moved, buffer[None, None]))
    velocity_out = arrange_slabs(moved[:3], blocks_x, blocks_y, cells_x, cells_y)
    pressure_out = arrange_slabs(moved[3:], blocks_x, blocks_y, cells_x, cells_y)
    return (particles_out, velocity_out, pressure_out[0])


def solution(mesh):
    placed = (
        P("dx", "dy", None, None),
        P("dx", "dy", None, None),
        P("dx", "dy", None),
        P("dx", "dy", None),
        P(None, ("dx", "dy"), None, None),
        P(("dx", "dy"), None, None),
    )
    return jax.shard_map(
        shards,
        mesh=mesh,
        in_specs=placed,
        out_specs=(
            P("dx", "dy", None, None),
            P(None, ("dx", "dy"), None, None),
            P(("dx", "dy"), None, None),
        ),
        check_vma=False,
    )
```

```python
import math

import jax
import jax.numpy as jnp
from jax import lax
from jax.sharding import PartitionSpec as P

COUPLINGS = 2


time_step = 0.1
viscosity = 0.5
gravity = -1.0


def from_behind(value, axis, steps):
    count = lax.axis_size(axis)
    pairs = [(source, (source + steps) % count) for source in range(count)]
    return lax.ppermute(value, axis, pairs)


def migrate(outgoing):
    arrivals = []
    for offset in (1, -1):
        arrivals.append(from_behind(outgoing[:, (1 - offset) // 2], "dx", offset))
    for offset in (1, -1):
        arrivals.append(from_behind(outgoing[:, 2 + (1 - offset) // 2], "dy", offset))
    return arrivals


def split_bf16(values):
    high = lax.reduce_precision(values, exponent_bits=8, mantissa_bits=7)
    low = values - high
    return high.astype(jnp.bfloat16), low.astype(jnp.bfloat16)


def deposit_block(buffer, on_layer, on_lane):
    sources = jnp.concatenate([buffer[6:8], buffer[7][None] * buffer[0:3]], axis=0)
    high, low = split_bf16(sources)
    parts = jnp.concatenate([high, low], axis=0)
    mask = on_layer.astype(jnp.bfloat16)
    channels, slots = sources.shape
    layers = on_layer.shape[0]
    stacked = (parts[:, None, :] * mask[None]).reshape(2 * channels * layers, slots)
    summed = jnp.dot(stacked, on_lane, preferred_element_type=jnp.float32)
    summed = summed.reshape(2, channels, layers, on_lane.shape[1])
    return summed[0] + summed[1]


def gather_block(field_list, on_layer, on_lane):
    pieces = [split_bf16(field) for field in field_list]
    high = jnp.concatenate([piece[0] for piece in pieces], axis=0)
    low = jnp.concatenate([piece[1] for piece in pieces], axis=0)
    channels, layers, lanes = high.shape
    stacked = jnp.concatenate([high, low], axis=0).reshape(2 * channels * layers, lanes)
    picked = jnp.dot(stacked, on_lane, preferred_element_type=jnp.float32)
    picked = picked.reshape(2, channels, layers, on_lane.shape[1])
    return jnp.sum((picked[0] + picked[1]) * on_layer[None], axis=1)


def advance_block(buffer, cell_flow, cell_solids):
    speeds = buffer[0:3]
    friction = buffer[7]
    mobility = buffer[8]
    cell_void = 1.0 / (1.0 + cell_solids)
    relaxation = time_step * friction * mobility / (cell_void * cell_void)
    live_mask = (buffer[6] > 0).astype(jnp.float32)
    still = jnp.zeros_like(live_mask)
    gravity_push = jnp.stack([still, still, time_step * gravity * live_mask], axis=0)
    new_speeds = (speeds + relaxation * cell_flow + gravity_push) / (1.0 + relaxation)
    spins = buffer[3:6] / (1.0 + relaxation)
    places = buffer[9:12] + time_step * new_speeds
    return jnp.concatenate([new_speeds, spins, buffer[6:9], places, buffer[12:14]], axis=0)


def slabs_to_blocks(field, blocks_x, blocks_y):
    channels, layers_z, cells_nx, cells_ny = field.shape
    cells_x, cells_y = cells_nx // blocks_x, cells_ny // blocks_y
    arranged = field.reshape(channels, layers_z, blocks_x, cells_x, blocks_y, cells_y).transpose(
        0, 2, 4, 1, 3, 5
    )
    arranged = arranged.reshape(channels, blocks_x * blocks_y * layers_z, cells_x * cells_y)
    return lax.all_to_all(arranged, ("dx", "dy"), split_axis=1, concat_axis=1, tiled=True)


def blocks_to_slabs(field, blocks_x, blocks_y, cells_x, cells_y):
    channels, depth, lanes = field.shape
    layers_z = depth // (blocks_x * blocks_y)
    return lax.all_to_all(field, ("dx", "dy"), split_axis=1, concat_axis=1, tiled=True)


def arrange_slabs(moved, blocks_x, blocks_y, cells_x, cells_y):
    channels, depth, lanes = moved.shape
    layers_z = depth // (blocks_x * blocks_y)
    arranged = moved.reshape(channels, blocks_x, blocks_y, layers_z, cells_x, cells_y).transpose(
        0, 3, 1, 4, 2, 5
    )
    return arranged.reshape(channels, layers_z, blocks_x * cells_x, blocks_y * cells_y)


def along_z(field):
    zero = jnp.zeros_like(field[..., :1, :])
    above = jnp.concatenate([field[..., 1:, :], zero], axis=-2)
    below = jnp.concatenate([zero, field[..., :-1, :]], axis=-2)
    return above, below


def faces_x(field, cells_y):
    ahead = from_behind(field[..., :cells_y], "dx", -1)
    behind = from_behind(field[..., field.shape[-1] - cells_y :], "dx", 1)
    return ahead, behind


def along_x(field, cells_y, faces=None):
    ahead, behind = faces_x(field, cells_y) if faces is None else faces
    plus = jnp.concatenate([field[..., cells_y:], ahead], axis=-1)
    minus = jnp.concatenate([behind, field[..., :-cells_y]], axis=-1)
    return plus, minus


def lane_selectors(cells_x, cells_y):
    lanes = cells_x * cells_y
    lane = lax.broadcasted_iota(jnp.int32, (lanes, 2 * cells_x), 0)
    column = lax.broadcasted_iota(jnp.int32, (lanes, 2 * cells_x), 1)
    picks = jnp.where(column < cells_x, column * cells_y, (column - cells_x) * cells_y + cells_y - 1)
    select = lane == picks
    spread_pick = jnp.where(column < cells_x, column * cells_y + cells_y - 1, (column - cells_x) * cells_y)
    spread = (lane == spread_pick).T
    return select.astype(jnp.bfloat16), spread.astype(jnp.bfloat16)


def exact_pick(values, one_hot):
    high = lax.reduce_precision(values, exponent_bits=8, mantissa_bits=7)
    rest = values - high
    middle = lax.reduce_precision(rest, exponent_bits=8, mantissa_bits=7)
    low = rest - middle
    rows = values.shape[0]
    parts = jnp.concatenate([high, middle, low], axis=0).astype(jnp.bfloat16)
    picked = jnp.dot(parts, one_hot, preferred_element_type=jnp.float32)
    return (picked[:rows] + picked[rows : 2 * rows]) + picked[2 * rows :]


def faces_y(field, selectors):
    cells_x = selectors[0].shape[1] // 2
    both = exact_pick(field.reshape(-1, field.shape[-1]), selectors[0])
    ahead = from_behind(both[:, :cells_x], "dy", -1)
    behind = from_behind(both[:, cells_x:], "dy", 1)
    return ahead, behind


def along_y(field, selectors, cells_y, faces=None):
    shape = field.shape
    ahead, behind = faces_y(field, selectors) if faces is None else faces
    halo = exact_pick(jnp.concatenate([ahead, behind], axis=1), selectors[1]).reshape(shape)
    lane_y = lax.broadcasted_iota(jnp.int32, shape, len(shape) - 1) % cells_y
    plus = jnp.where(lane_y == cells_y - 1, halo, jnp.roll(field, -1, axis=-1))
    minus = jnp.where(lane_y == 0, halo, jnp.roll(field, 1, axis=-1))
    return plus, minus


def fluid_step(velocity, pressure, deposits, faces, selectors, cells_y):
    solids = deposits[0]
    voidage = 1.0 / (1.0 + solids)
    growth = (1.0 + solids) * (1.0 + solids)
    drag_rate = deposits[1] * growth
    drag_pull = deposits[2:5] * growth
    stacked = jnp.concatenate([velocity, pressure[None]], axis=0)
    z_plus, z_minus = along_z(stacked)
    x_plus, x_minus = along_x(stacked, cells_y, faces[0])
    y_plus, y_minus = along_y(stacked, selectors, cells_y, faces[1])
    beside_all = (z_plus + z_minus) + x_plus + x_minus + y_plus + y_minus
    predicted = (
        velocity + time_step * (viscosity * (beside_all[:3] - 6.0 * velocity) + drag_pull)
    ) / (1.0 + time_step * drag_rate)
    flux = voidage[None] * predicted
    fx_plus, fx_minus = along_x(flux[0], cells_y)
    fy_plus, fy_minus = along_y(flux[1], selectors, cells_y)
    fz_plus, fz_minus = along_z(flux[2])
    divergence = 0.5 * (fx_plus - fx_minus) + 0.5 * (fy_plus - fy_minus) + 0.5 * (fz_plus - fz_minus)
    pressure_new = (beside_all[3] - divergence / time_step) / 6.0
    px_plus, px_minus = along_x(pressure_new, cells_y)
    py_plus, py_minus = along_y(pressure_new, selectors, cells_y)
    pz_plus, pz_minus = along_z(pressure_new)
    gradient = jnp.stack(
        [0.5 * (px_plus - px_minus), 0.5 * (py_plus - py_minus), 0.5 * (pz_plus - pz_minus)], axis=0
    )
    return (predicted - time_step * gradient, pressure_new)


def shards(particles, leave_lists, leave_counts, slot_cells, velocity, pressure):
    blocks_x = lax.axis_size("dx")
    blocks_y = lax.axis_size("dy")
    records = particles[0, 0]
    leaver_lists = leave_lists[0, 0]
    leaver_counts = leave_counts[0, 0]
    cell_index = slot_cells[0, 0]
    capacity = leaver_lists.shape[1]
    holders = records.shape[1]
    cells_x = velocity.shape[2] // blocks_x
    cells_y = velocity.shape[3] // blocks_y
    lanes = cells_x * cells_y
    depth = velocity.shape[1] * blocks_x * blocks_y

    fields = slabs_to_blocks(
        jnp.concatenate([velocity, pressure[None]], axis=0), blocks_x, blocks_y
    )
    positions = jnp.arange(capacity, dtype=jnp.int32)
    validity = (positions[None, :] < leaver_counts[:, None]).astype(jnp.float32)
    flat_list = leaver_lists.reshape(-1)
    low_size = math.gcd(holders, 512)
    upper_size = holders // low_size
    listed = flat_list.shape[0]
    upper_of = flat_list // low_size
    lower_of = flat_list % low_size
    on_upper = lax.broadcasted_iota(jnp.int32, (upper_size, listed), 0) == upper_of[None, :]
    on_lower = lax.broadcasted_iota(jnp.int32, (low_size, listed), 0) == lower_of[None, :]
    valid_flat = validity.reshape(1, -1)
    departed = lax.dot_general(
        (on_upper.astype(jnp.float32) * valid_flat).astype(jnp.bfloat16),
        on_lower.astype(jnp.bfloat16),
        (((1,), (1,)), ((), ())),
        preferred_element_type=jnp.float32,
    ).reshape(holders)
    remaining = records * (1.0 - departed)[None, :]
    high = lax.reduce_precision(records, exponent_bits=8, mantissa_bits=7)
    rest = records - high
    middle = lax.reduce_precision(rest, exponent_bits=8, mantissa_bits=7)
    low = rest - middle
    rows = records.shape[0]
    parts = jnp.concatenate([high, middle, low], axis=0).astype(jnp.bfloat16)
    parts = parts.reshape(3 * rows * upper_size, low_size)
    by_lower = jnp.dot(parts, on_lower.astype(jnp.bfloat16), preferred_element_type=jnp.float32)
    by_lower = by_lower.reshape(3, rows, upper_size, listed)
    picked_parts = jnp.sum(by_lower * on_upper.astype(jnp.float32)[None, None], axis=2)
    picked_rows = (picked_parts[0] + picked_parts[1]) + picked_parts[2]
    outgoing = picked_rows.reshape(rows, 4, capacity) * validity[None]
    arrivals = migrate(outgoing)
    buffer = jnp.concatenate([remaining] + arrivals, axis=1)

    layer_of = cell_index // lanes
    lane_of = cell_index % lanes
    on_layer = (
        lax.broadcasted_iota(jnp.int32, (depth, cell_index.shape[0]), 0) == layer_of[None, :]
    ).astype(jnp.float32)

    def lane_one_hot(lane_index):
        return (
            lax.broadcasted_iota(jnp.int32, (lane_index.shape[0], lanes), 1) == lane_index[:, None]
        ).astype(jnp.bfloat16)

    lane_on = (
        lax.broadcasted_iota(jnp.int32, (lanes, cell_index.shape[0]), 0) == lane_of[None, :]
    ).astype(jnp.bfloat16)

    selectors = lane_selectors(cells_x, cells_y)
    resident_deposits = deposit_block(remaining, on_layer[:, :holders], lane_one_hot(lane_of[:holders]))
    fields, buffer, resident_deposits = lax.optimization_barrier((fields, buffer, resident_deposits))
    flow = fields[:3]
    pressure_block = fields[3]
    stacked = jnp.concatenate([flow, pressure_block[None]], axis=0)
    faces = (faces_x(stacked, cells_y), faces_y(stacked, selectors))
    for coupling in range(COUPLINGS):
        if coupling == 0:
            deposits = resident_deposits + deposit_block(
                buffer[:, holders:], on_layer[:, holders:], lane_one_hot(lane_of[holders:])
            )
        else:
            deposits = deposit_block(buffer, on_layer, lane_one_hot(lane_of))
        faces, deposits = lax.optimization_barrier((faces, deposits))
        flow, pressure_block = fluid_step(flow, pressure_block, deposits, faces, selectors, cells_y)
        picked = gather_block(
            (flow, deposits[:1]), on_layer, lane_on
        )
        stacked = jnp.concatenate([flow, pressure_block[None]], axis=0)
        if coupling < COUPLINGS - 1:
            stacked, picked = lax.optimization_barrier((stacked, picked))
            faces = (faces_x(stacked, cells_y), faces_y(stacked, selectors))
        else:
            moved = blocks_to_slabs(stacked, blocks_x, blocks_y, cells_x, cells_y)
        buffer = advance_block(buffer, picked[:3], picked[3])

    moved, particles_out = lax.optimization_barrier((moved, buffer[None, None]))
    velocity_out = arrange_slabs(moved[:3], blocks_x, blocks_y, cells_x, cells_y)
    pressure_out = arrange_slabs(moved[3:], blocks_x, blocks_y, cells_x, cells_y)
    return (particles_out, velocity_out, pressure_out[0])


def solution(mesh):
    placed = (
        P("dx", "dy", None, None),
        P("dx", "dy", None, None),
        P("dx", "dy", None),
        P("dx", "dy", None),
        P(None, ("dx", "dy"), None, None),
        P(("dx", "dy"), None, None),
    )
    return jax.shard_map(
        shards,
        mesh=mesh,
        in_specs=placed,
        out_specs=(
            P("dx", "dy", None, None),
            P(None, ("dx", "dy"), None, None),
            P(("dx", "dy"), None, None),
        ),
        check_vma=False,
    )
```
